32 devices in a mesh: kv: 2 (over x), ep: 16 (over z, y, core).
Axes of the slice: x: 2, y: 2, z: 4, core: 2. Of those that a mesh axis runs over, the one named last changes fastest.
Arguments:
- resid: bfloat16 [16, 256, 2048], P('ep', 'kv'), may hold values from -6 to 6
- queries: bfloat16 [16, 256, 1024], P('ep', 'kv'), may hold values from -6 to 6
- new_keys: bfloat16 [16, 256, 1024], P('ep', 'kv'), may hold values from -6 to 6
- new_values: bfloat16 [16, 256, 1024], P('ep', 'kv'), may hold values from -6 to 6
- cache_keys: bfloat16 [16, 2048, 1024], P('ep', 'kv'), may hold values from -6 to 6
- cache_values: bfloat16 [16, 2048, 1024], P('ep', 'kv'), may hold values from -6 to 6
- cached_len: int32 [16], replicated, may hold values from 64 to 2048, as said below
- group_request: int32 [16], P('ep'), may hold values from 0 to 15, each once
- w_out: bfloat16 [1024, 2048], replicated, may hold values from -0.1875 to 0.1875
- norm_gain: bfloat16 [2048], replicated, may hold values from 0.099609375 to 1.8984375
- route_ids: int32 [16, 256, 8], P('ep', 'kv'), may hold values from 0 to 15, all different within a row; in each aligned block of 128 rows (0 to 127, 128 to 255, ..., all dimensions but the last counted through in order) at most 96 rows name the same one
- route_weights: float32 [16, 256, 8], P('ep', 'kv'), may hold values from 0.1 to 0.5
- gate_w: bfloat16 [16, 2048, 512], P('ep', None, 'kv'), may hold values from -0.125 to 0.125
- up_w: bfloat16 [16, 2048, 512], P('ep', None, 'kv'), may hold values from -0.125 to 0.125
- down_w: bfloat16 [16, 512, 2048], P('ep', 'kv'), may hold values from -0.25 to 0.25
Outputs:
- layer_out: bfloat16 [16, 256, 2048], P('ep', 'kv')
The draws below stay inside these ranges and needn't reach their ends.
Inputs may be any that keep to these rules, and one draw needn't show every extreme that they name: `route_ids`: among the 128 tokens of one device no expert is named more than 96 times, a bound that some block reaches. `cached_len`: some request has exactly 2048 cached positions. `group_request`: every request is held by exactly one group.
All inputs are finite; a program needn't handle non-finite values.
Results may differ from the reference program's by a relative error of at most 0.015.
Values may be sent and summed in bfloat16 or wider, within the bound.
No kernel may reach another device: no remote copies, remote signals or barrier semaphores. Data moves between devices by JAX's collectives and lax.ppermute only.
A program may use at most 128 MiB of HBM per device.

```python
import math
import jax
import jax.numpy as jnp
import numpy as np
from jax import lax

D = 2048
HEAD_DIM = 128
HEADS = 8
FF = 512
TOP = 8
TOK_DEV = 128
HD = 1024
EXPERTS = 16
NEW = 256
CACHE = 2048
REQS = 16
CAP = 96
N_KV = 2
N_EP = 16


def paired_rows(key):
    base = jax.random.fold_in(key, 4242)
    key_query, key_key = jax.random.split(base, 2)
    shape = (REQS, NEW, HEADS * HEAD_DIM)
    query_vals = jnp.clip(1.5 * jax.random.normal(key_query, shape, jnp.float32), -6.0, 6.0)
    key_vals = jnp.clip(1.5 * jax.random.normal(key_key, shape, jnp.float32), -6.0, 6.0)
    return (query_vals, key_vals)


def draw_queries(key, part):
    query_vals, key_vals = paired_rows(key)
    return query_vals.astype(jnp.bfloat16)


def draw_new_keys(key, part):
    query_vals, key_vals = paired_rows(key)
    return key_vals.astype(jnp.bfloat16)


def draw_cached_len(key, part):
    base = jax.random.fold_in(key, 977)
    key_long, key_short, key_full, key_index = jax.random.split(base, 4)
    is_long = jax.random.randint(key_long, (REQS,), 0, 4) == 0
    short_len = jax.random.randint(key_short, (REQS,), CACHE // 32, CACHE // 16 + 1)
    long_len = CACHE - jax.random.randint(key_full, (REQS,), 0, CACHE // 8 + 1)
    lengths = jnp.where(is_long, long_len, short_len)
    chosen = jax.random.randint(key_index, (), 0, REQS)
    lengths = lengths.at[chosen].set(CACHE)
    lengths = lengths.at[(chosen + 1) % REQS].set(CACHE // 32)
    return lengths.astype(jnp.int32)


def block_levels(stream_key, dims, cuts, low, high):
    level, own = 1.0, jax.random.fold_in(stream_key, 6)
    for axis_at, blocks in cuts:
        draws = jnp.exp(jax.random.uniform(jax.random.fold_in(own, axis_at), (blocks,), jnp.float32, low / len(cuts), high / len(cuts)))
        level = level * jnp.repeat(draws, dims[axis_at] // blocks).reshape([-1 if axis == axis_at else 1 for axis in range(len(dims))])
    return level


def assign_block(stream_key, own, number, rows, count, top, limit, skew):
    order = jax.random.permutation(stream_key, count)
    heavy_load, ordinary = portions_of(count, rows * top, limit, skew, True), portions_of(count, rows * top, limit, skew, False)
    places = jnp.arange(count)

    def named(tallies, rotation):
        used = int((tallies > 0).sum())
        fixed = max(1, used // 4)
        moved = fixed + (places - fixed + rotation * (used - fixed)) % max(1, count - fixed)
        return jnp.zeros((count,), jnp.int32).at[order[jnp.where(places < fixed, places, moved)]].set(jnp.asarray(tallies, jnp.int32))

    tallies = jnp.where(number % 4 == 0, named(heavy_load, number // 4), named(ordinary, number - number // 4 - 1))
    mixed = jax.random.permutation(jax.random.fold_in(own, 3), count)
    giver, taker = mixed[0:count // 2 * 2:2], mixed[1:count // 2 * 2:2]
    room = jnp.minimum(tallies[giver] - 1, limit - tallies[taker]) // 2
    room = jnp.where((giver == order[0]) | (taker == order[0]) | (tallies[taker] == 0), 0, jnp.maximum(room, 0))
    moved = jax.random.randint(jax.random.fold_in(own, 4), (count // 2,), 0, 1 << 20) % (room + 1)
    tallies = tallies.at[giver].add(-moved).at[taker].add(moved)
    items = jnp.searchsorted(jnp.cumsum(tallies), jnp.arange(rows * top), side="right").astype(jnp.int32)
    table = items.reshape(top, rows).T
    table = table[jax.random.permutation(jax.random.fold_in(own, 1), rows)]
    rotation = jax.random.randint(jax.random.fold_in(own, 2), (rows, 1), 0, top)
    return jnp.take_along_axis(table, (jnp.arange(top)[None, :] + rotation) % top, axis=1)


def portions_of(count, total, most, lean, full):
    weights = [(1 << 20) // math.isqrt(standing ** lean) + 1 for standing in range(1, count + 1)]
    largest = most if full else min(most, max(-(-total // count), total * weights[0] // sum(weights)))
    least = 1 if total - largest >= count - 1 else 0
    given, spare = [largest] + [least] * (count - 1), total - largest - least * (count - 1)
    while spare > 0:
        free = [i for i in range(1, count) if given[i] < largest] or [i for i in range(1, count) if given[i] < most]
        mass, budget = sum([weights[i] for i in free]), spare
        for i in free:
            addition = min(most - given[i], max(1, budget * weights[i] // mass), spare)
            given[i] = given[i] + addition
            spare = spare - addition
    return np.array(given)


def gaussian(rng, extent, spread, limit, pieces=(), kind=jnp.bfloat16):
    entries = spread * jax.random.normal(rng, extent, jnp.float32)
    if pieces:
        entries = entries * block_levels(rng, extent, pieces, -0.22, 0.18)
    return jnp.clip(entries, -limit, limit).astype(kind)


def setup_inputs(seed: int = 0) -> dict:
    streams_of = jax.random.split(jax.random.key(seed), 16)
    resid = gaussian(streams_of[0], (REQS, NEW, D), 1.0, 6.0, ((0, 16), (1, 2)))
    queries = draw_queries(jax.random.fold_in(streams_of[15], 71), 0)
    new_keys = draw_new_keys(jax.random.fold_in(streams_of[15], 71), 0)
    new_values = gaussian(streams_of[3], (REQS, NEW, HD), 1.0, 6.0, ((0, 16), (1, 2)))
    cache_keys = gaussian(streams_of[4], (REQS, CACHE, HD), 1.5, 6.0, ((0, 16), (1, 2)))
    cache_values = gaussian(streams_of[5], (REQS, CACHE, HD), 1.0, 6.0, ((0, 16), (1, 2)))
    cached_len = draw_cached_len(jax.random.fold_in(streams_of[15], 71), 0)
    group_request = jax.random.permutation(streams_of[7], REQS).astype(jnp.int32)
    w_out = gaussian(streams_of[8], (HD, D), HD ** -0.5, 0.1875)
    norm_gain = jnp.clip(1.0 + 0.18 * jax.random.normal(streams_of[9], (D,), jnp.float32), 0.099609375, 1.8984375).astype(jnp.bfloat16)
    route_ids_keys = jax.random.split(jax.random.fold_in(streams_of[10], 1), REQS * NEW // TOK_DEV)
    route_ids_turns = jax.random.permutation(jax.random.fold_in(streams_of[10], 3), REQS * NEW // TOK_DEV)
    route_ids = jax.vmap(lambda own, number: assign_block(jax.random.fold_in(streams_of[10], 2), own, number, TOK_DEV, EXPERTS, TOP, CAP, 1))(route_ids_keys, route_ids_turns).reshape((REQS, NEW, TOP))
    route_weights = jnp.clip(0.1 + 0.4 * jax.random.uniform(streams_of[11], (REQS, NEW, TOP), jnp.float32) ** block_levels(streams_of[11], (REQS, NEW, TOP), ((0, 16), (1, 2)), -0.2, 0.2), 0.1, 0.5)
    gate_w = gaussian(streams_of[12], (EXPERTS, D, FF), D ** -0.5, 0.125, ((0, 16), (2, 2)))
    up_w = gaussian(streams_of[13], (EXPERTS, D, FF), D ** -0.5, 0.125, ((0, 16), (2, 2)))
    down_w = gaussian(streams_of[14], (EXPERTS, FF, D), FF ** -0.5, 0.25, ((0, 16), (1, 2)))
    return dict(resid=resid, queries=queries, new_keys=new_keys, new_values=new_values, cache_keys=cache_keys, cache_values=cache_values, cached_len=cached_len, group_request=group_request, w_out=w_out, norm_gain=norm_gain, route_ids=route_ids, route_weights=route_weights, gate_w=gate_w, up_w=up_w, down_w=down_w)


def attend_group(operands):
    query_rows, key_new, value_new, key_cache, value_cache, length = operands
    score_scale = 1.0 / math.sqrt(HEAD_DIM)
    query_f = query_rows.astype(jnp.float32).reshape(NEW, HEADS, HEAD_DIM)
    key_all = jnp.concatenate([key_cache, key_new], axis=0).astype(jnp.float32).reshape(CACHE + NEW, HEADS, HEAD_DIM)
    value_all = jnp.concatenate([value_cache, value_new], axis=0).astype(jnp.float32).reshape(CACHE + NEW, HEADS, HEAD_DIM)
    scores = jnp.einsum('qhd,khd->qhk', query_f, key_all) * score_scale
    position = jnp.arange(CACHE + NEW, dtype=jnp.int32)
    usable = (position < length) | (position >= CACHE)
    scores = jnp.where(usable[None, None, :], scores, -jnp.inf)
    row_top = lax.optimization_barrier(jnp.max(scores, axis=-1, keepdims=True))
    expo = jnp.exp(scores - row_top)
    denom = lax.optimization_barrier(jnp.sum(expo, axis=-1))
    probs = lax.optimization_barrier(expo.astype(jnp.bfloat16)).astype(jnp.float32)
    summed = jnp.einsum('qhk,khd->qhd', probs, value_all)
    return (summed / denom[..., None]).reshape(NEW, HD).astype(jnp.bfloat16)

def reference(resid, queries, new_keys, new_values, cache_keys, cache_values, cached_len, group_request, w_out, norm_gain, route_ids, route_weights, gate_w, up_w, down_w):
    lengths = cached_len[group_request].astype(jnp.int32)
    attended = lax.map(attend_group, (queries, new_keys, new_values, cache_keys, cache_values, lengths))
    proj = jnp.dot(attended.reshape(REQS * NEW, HD), w_out, preferred_element_type=jnp.float32)
    hidden = (resid.reshape(REQS * NEW, D).astype(jnp.float32) + proj).astype(jnp.bfloat16)
    hidden_f = hidden.astype(jnp.float32)
    normed = (hidden_f * lax.rsqrt(lax.optimization_barrier(jnp.mean(hidden_f * hidden_f, axis=-1, keepdims=True)) + 1e-06) * norm_gain.astype(jnp.float32)).astype(jnp.bfloat16)
    flat_ids = route_ids.reshape(-1)
    flat_weights = route_weights.reshape(-1).astype(jnp.float32)
    bound = N_EP * N_KV * CAP

    def expert_step(total, expert):
        chosen = flat_ids == expert
        count = jnp.sum(chosen.astype(jnp.int32))
        picks = jnp.nonzero(chosen, size=bound, fill_value=0)[0].astype(jnp.int32)
        valid = jnp.arange(bound, dtype=jnp.int32) < count
        token_index = picks // TOP
        row_block = normed[token_index].astype(jnp.float32)
        gate_val = jnp.dot(row_block, gate_w[expert].astype(jnp.float32), preferred_element_type=jnp.float32)
        up_val = jnp.dot(row_block, up_w[expert].astype(jnp.float32), preferred_element_type=jnp.float32)
        act = (jax.nn.silu(gate_val) * up_val).astype(jnp.bfloat16)
        out_rows = jnp.dot(act.astype(jnp.float32), down_w[expert].astype(jnp.float32), preferred_element_type=jnp.float32).astype(jnp.bfloat16)
        factor = jnp.where(valid, flat_weights[picks], jnp.zeros_like(flat_weights[picks]))
        total = total.at[token_index].add(out_rows.astype(jnp.float32) * factor[:, None])
        return (total, None)
    start_total = jnp.zeros((REQS * NEW, D), jnp.float32)
    moe_sum, unused = lax.scan(expert_step, start_total, jnp.arange(EXPERTS, dtype=jnp.int32))
    return (hidden_f + moe_sum).astype(jnp.bfloat16).reshape(REQS, NEW, D)
```

```python
import functools
import math

import jax
import jax.numpy as jnp
from jax import lax
from jax.sharding import PartitionSpec as P

D = 2048
HEAD_DIM = 128
TOP = 8
EXP_DEV = 1


def combined_all(shard, axis, join):
    gathered = jax.tree.map(
        lambda a, kind: lax.all_gather(a.astype(kind), axis),
        shard,
        (jnp.bfloat16, jnp.bfloat16, jnp.bfloat16),
    )

    def take(source):
        return jax.tree.map(
            lambda a, own: lax.dynamic_index_in_dim(a, source, 0, False).astype(own.dtype),
            gathered,
            shard,
        )

    return lax.fori_loop(
        1, lax.axis_size(axis), lambda source, state: join(state, take(source)), take(0)
    )


def expert_full(row_block, gate_part, up_part, down_part):
    gate_val = jnp.einsum(
        "sjkd,jdf->sjkf", row_block, gate_part, preferred_element_type=jnp.float32
    )
    up_val = jnp.einsum("sjkd,jdf->sjkf", row_block, up_part, preferred_element_type=jnp.float32)
    act = (jax.nn.silu(gate_val) * up_val).astype(jnp.bfloat16)
    return jnp.einsum("sjkf,jfd->sjkd", act, down_part, preferred_element_type=jnp.float32)


def gather_stage(block, pairs_list):
    parts = [block] + [lax.ppermute(block, "ep", pairs) for pairs in pairs_list]
    return jax.tree.map(lambda *leaves: jnp.stack(leaves), *parts)


def scatter_stage(block, pairs_list):
    total = block[0]
    for index, pairs in enumerate(pairs_list, 1):
        back = [(target, source) for source, target in pairs]
        sent = lax.ppermute(block[index].astype(jnp.bfloat16), "ep", back)
        total = total + sent.astype(jnp.float32)
    return total


def dense_moe(plan, normed, route_ids, route_weights, gate_w, up_w, down_w):
    expert_count = EXP_DEV * lax.axis_size("ep")
    experts = jnp.arange(expert_count, dtype=jnp.int32)
    chosen = route_ids[:, :, None] == experts[None, None, :]
    weight_table = jnp.sum(jnp.where(chosen, route_weights[:, :, None], 0.0), axis=1)
    block = (normed, weight_table)
    for pairs_list in plan:
        block = gather_stage(block, pairs_list)
    rows, weights = block
    lead = rows.shape[:-2]
    rows = rows.reshape(-1, D)
    own = lax.axis_index("ep")
    weights = jnp.sum(jnp.where(experts == own, weights.reshape(-1, expert_count), 0.0), axis=1)
    full_gate = lax.all_gather(gate_w[0], "kv", axis=1, tiled=True)
    full_up = lax.all_gather(up_w[0], "kv", axis=1, tiled=True)
    full_down = lax.all_gather(down_w[0], "kv", axis=0, tiled=True)
    gate_val = jnp.dot(rows, full_gate, preferred_element_type=jnp.float32)
    up_val = jnp.dot(rows, full_up, preferred_element_type=jnp.float32)
    act = (jax.nn.silu(gate_val) * up_val).astype(jnp.bfloat16)
    out_rows = jnp.dot(act, full_down, preferred_element_type=jnp.float32).astype(jnp.bfloat16)
    partial = (out_rows.astype(jnp.float32) * weights[:, None]).reshape(*lead, -1, D)
    for pairs_list in reversed(plan):
        partial = scatter_stage(partial, pairs_list)
    return partial


def gather_plan(mesh, shapes):
    kv_count, ep_count = mesh.devices.shape
    rows = ep_count * shapes[0][1] // kv_count
    if EXP_DEV != 1 or shapes[12][0] != ep_count or rows > 4096:
        return None
    places = []
    for device in mesh.devices[0]:
        coords = getattr(device, "coords", None)
        core = getattr(device, "core_on_chip", None)
        if coords is None or core is None:
            return None
        places.append(tuple(coords) + (core,))
    width = len(places[0])
    values = [sorted({p[a] for p in places}) for a in range(width)]
    varying = [a for a in range(width) if len(values[a]) > 1]
    total = 1
    for a in varying:
        total *= len(values[a])
    if total != ep_count or len(set(places)) != ep_count:
        return None
    rank_of = {p: r for r, p in enumerate(places)}
    core_axis = width - 1
    order = sorted((a for a in varying if a != core_axis), key=lambda a: -len(values[a]))
    order += [a for a in varying if a == core_axis]
    plan = []
    for a in order:
        size = len(values[a])
        stage = []
        for shift in range(1, size):
            pairs = []
            for r, p in enumerate(places):
                moved = list(p)
                moved[a] = values[a][(values[a].index(p[a]) + shift) % size]
                pairs.append((r, rank_of[tuple(moved)]))
            stage.append(pairs)
        plan.append(stage)
    return plan


def shards(
    plan,
    resid,
    queries,
    new_keys,
    new_values,
    cache_keys,
    cache_values,
    cached_len,
    group_request,
    w_out,
    norm_gain,
    route_ids,
    route_weights,
    gate_w,
    up_w,
    down_w,
):
    kv_rank = lax.axis_index("kv")
    ep_count = lax.axis_size("ep")
    tok_dev = resid.shape[1]
    cl_dev = cache_keys.shape[1]
    feat = queries.shape[2]
    head_count = feat // HEAD_DIM
    score_scale = 1.0 / math.sqrt(HEAD_DIM)
    request_index = jnp.arange(cached_len.shape[0], dtype=jnp.int32)
    length = jnp.sum(jnp.where(request_index == group_request[0], cached_len, 0))
    every_query = lax.all_gather(queries[0], "kv", axis=0, tiled=True)
    new_total = every_query.shape[0]
    query_heads = every_query.reshape(new_total, head_count, HEAD_DIM)
    key_cache = cache_keys[0].reshape(cl_dev, head_count, HEAD_DIM)
    value_cache = cache_values[0].reshape(cl_dev, head_count, HEAD_DIM)
    key_new = new_keys[0].reshape(tok_dev, head_count, HEAD_DIM)
    value_new = new_values[0].reshape(tok_dev, head_count, HEAD_DIM)
    score_cache = (
        jnp.einsum("qhd,khd->qhk", query_heads, key_cache, preferred_element_type=jnp.float32)
        * score_scale
    )
    position = kv_rank * cl_dev + jnp.arange(cl_dev, dtype=jnp.int32)
    score_cache = jnp.where((position < length)[None, None, :], score_cache, -jnp.inf)
    score_new = (
        jnp.einsum("qhd,khd->qhk", query_heads, key_new, preferred_element_type=jnp.float32)
        * score_scale
    )
    local_top = jnp.maximum(jnp.max(score_cache, axis=-1), jnp.max(score_new, axis=-1))
    expo_cache = jnp.exp(score_cache - local_top[..., None])
    expo_new = jnp.exp(score_new - local_top[..., None])
    denom = jnp.sum(expo_cache, axis=-1) + jnp.sum(expo_new, axis=-1)
    summed = jnp.einsum(
        "qhk,khd->qhd",
        expo_cache.astype(jnp.bfloat16),
        value_cache,
        preferred_element_type=jnp.float32,
    )
    summed = summed + jnp.einsum(
        "qhk,khd->qhd", expo_new.astype(jnp.bfloat16), value_new, preferred_element_type=jnp.float32
    )
    summed, denom = (summed.reshape(new_total, feat), denom)

    def join(first, second):
        first_top, first_denom, first_sum = first
        second_top, second_denom, second_sum = second
        joint_top = jnp.maximum(first_top, second_top)
        first_factor = jnp.exp(first_top - joint_top)
        second_factor = jnp.exp(second_top - joint_top)
        rows_here = first_sum.shape[0]
        joint_sum = (
            first_sum.reshape(rows_here, head_count, HEAD_DIM) * first_factor[..., None]
            + second_sum.reshape(rows_here, head_count, HEAD_DIM) * second_factor[..., None]
        )
        return (
            joint_top,
            first_denom * first_factor + second_denom * second_factor,
            joint_sum.reshape(rows_here, feat),
        )

    joint_top, joint_denom, joint_sum = combined_all((local_top, denom, summed), "kv", join)
    row_start = kv_rank * tok_dev
    own_sum = lax.dynamic_slice_in_dim(joint_sum, row_start, tok_dev, 0)
    own_denom = lax.dynamic_slice_in_dim(joint_denom, row_start, tok_dev, 0)
    attended = (
        (own_sum.reshape(tok_dev, head_count, HEAD_DIM) / own_denom[..., None])
        .reshape(tok_dev, feat)
        .astype(jnp.bfloat16)
    )
    proj = jnp.dot(attended, w_out, preferred_element_type=jnp.float32)
    hidden = (resid[0].astype(jnp.float32) + proj).astype(jnp.bfloat16)
    hidden_f = hidden.astype(jnp.float32)
    normed = (
        hidden_f
        * lax.rsqrt(jnp.mean(hidden_f * hidden_f, axis=-1, keepdims=True) + 1e-06)
        * norm_gain.astype(jnp.float32)
    ).astype(jnp.bfloat16)
    if plan is not None:
        moe_sum = dense_moe(plan, normed, route_ids[0], route_weights[0], gate_w, up_w, down_w)
        return (hidden_f + moe_sum).astype(jnp.bfloat16)[None]
    expert_count = EXP_DEV * ep_count
    capacity = min(tok_dev, max(2, tok_dev * TOP * 3 // (2 * expert_count)))
    route_flat = route_ids[0].reshape(-1)
    one_hot = (route_flat[:, None] == jnp.arange(expert_count, dtype=jnp.int32)[None, :]).astype(
        jnp.int32
    )
    rank_in = jnp.sum((jnp.cumsum(one_hot, axis=0) - 1) * one_hot, axis=1)
    slot_of = route_flat * capacity + rank_in
    slot_index = jnp.arange(expert_count * capacity, dtype=jnp.int32)
    placing = jnp.sum(
        (slot_of.reshape(tok_dev, TOP)[None, :, :] == slot_index[:, None, None]).astype(jnp.int32),
        axis=-1,
    ).astype(jnp.bfloat16)
    outgoing = jnp.dot(placing, normed, preferred_element_type=jnp.float32).astype(jnp.bfloat16)
    outgoing = outgoing.reshape(ep_count, EXP_DEV, capacity, D)
    full_gate, full_up, full_down = (
        lax.all_gather(gate_w, "kv", axis=2, tiled=True),
        lax.all_gather(up_w, "kv", axis=2, tiled=True),
        lax.all_gather(down_w, "kv", axis=1, tiled=True),
    )
    expert_out = expert_full(
        lax.all_to_all(outgoing, "ep", split_axis=0, concat_axis=0, tiled=True),
        full_gate,
        full_up,
        full_down,
    ).astype(jnp.bfloat16)
    returned = lax.all_to_all(expert_out, "ep", split_axis=0, concat_axis=0, tiled=True).reshape(
        expert_count * capacity, D
    )
    picked = jnp.take(returned, slot_of, axis=0).reshape(tok_dev, TOP, D)
    moe_sum = jnp.sum(picked.astype(jnp.float32) * route_weights[0][..., None], axis=1)
    return (hidden_f + moe_sum).astype(jnp.bfloat16)[None]


def solution(mesh):
    placed = (
        P("ep", "kv", None),
        P("ep", "kv", None),
        P("ep", "kv", None),
        P("ep", "kv", None),
        P("ep", "kv", None),
        P("ep", "kv", None),
        P(),
        P("ep"),
        P(),
        P(),
        P("ep", "kv", None),
        P("ep", "kv", None),
        P("ep", None, "kv"),
        P("ep", None, "kv"),
        P("ep", "kv", None),
    )

    def run(*args):
        plan = gather_plan(mesh, [a.shape for a in args])
        body = functools.partial(shards, plan)
        return jax.shard_map(
            body, mesh=mesh, in_specs=placed, out_specs=P("ep", "kv", None), check_vma=False
        )(*args)

    return run
```

```python
import functools
import math

import jax
import jax.numpy as jnp
from jax import lax
from jax.sharding import PartitionSpec as P

D = 2048
HEAD_DIM = 128
TOP = 8
EXP_DEV = 1


def combined_all(shard, axis, join):
    gathered = jax.tree.map(
        lambda a, kind: lax.all_gather(a.astype(kind), axis),
        shard,
        (jnp.bfloat16, jnp.bfloat16, jnp.bfloat16),
    )

    def take(source):
        return jax.tree.map(
            lambda a, own: lax.dynamic_index_in_dim(a, source, 0, False).astype(own.dtype),
            gathered,
            shard,
        )

    return lax.fori_loop(
        1, lax.axis_size(axis), lambda source, state: join(state, take(source)), take(0)
    )


def expert_full(row_block, gate_part, up_part, down_part):
    gate_val = jnp.einsum(
        "sjkd,jdf->sjkf", row_block, gate_part, preferred_element_type=jnp.float32
    )
    up_val = jnp.einsum("sjkd,jdf->sjkf", row_block, up_part, preferred_element_type=jnp.float32)
    act = (jax.nn.silu(gate_val) * up_val).astype(jnp.bfloat16)
    return jnp.einsum("sjkf,jfd->sjkd", act, down_part, preferred_element_type=jnp.float32)


def full_weights(gate_w, up_w, down_w):
    kv_count = lax.axis_size("kv")
    if kv_count != 2:
        return (
            lax.all_gather(gate_w[0], "kv", axis=1, tiled=True),
            lax.all_gather(up_w[0], "kv", axis=1, tiled=True),
            lax.all_gather(down_w[0], "kv", axis=0, tiled=True),
        )
    mine = (gate_w[0], up_w[0], down_w[0])
    other = lax.ppermute(mine, "kv", [(0, 1), (1, 0)])
    first = lax.axis_index("kv") == 0
    joined = []
    for own, far, axis in zip(mine, other, (1, 1, 0)):
        low = jnp.where(first, own, far)
        high = jnp.where(first, far, own)
        joined.append(jnp.concatenate([low, high], axis=axis))
    return tuple(joined)


def dense_moe(plan, normed, route_ids, route_weights, gate_w, up_w, down_w):
    expert_count = EXP_DEV * lax.axis_size("ep")
    experts = jnp.arange(expert_count, dtype=jnp.int32)
    own_expert = lax.axis_index("ep")
    chosen = route_ids[:, :, None] == experts[None, None, :]
    weight_table = jnp.sum(jnp.where(chosen, route_weights[:, :, None], 0.0), axis=1)
    full_gate, full_up, full_down = full_weights(gate_w, up_w, down_w)

    def expert(block):
        rows, table = block
        lead = rows.shape[:-1]
        rows = rows.reshape(-1, D)
        weights = jnp.sum(
            jnp.where(experts == own_expert, table.reshape(-1, expert_count), 0.0), axis=1
        )
        gate_val = jnp.dot(rows, full_gate, preferred_element_type=jnp.float32)
        up_val = jnp.dot(rows, full_up, preferred_element_type=jnp.float32)
        act = (jax.nn.silu(gate_val) * up_val).astype(jnp.bfloat16)
        out_rows = jnp.dot(act, full_down, preferred_element_type=jnp.float32)
        out_rows = out_rows.astype(jnp.bfloat16).astype(jnp.float32)
        return (out_rows * weights[:, None]).reshape(*lead, D)

    current = (normed, weight_table)
    arrived = []
    for pairs_list in plan:
        received = [lax.ppermute(current, "ep", pairs) for pairs in pairs_list]
        arrived.append(jax.tree.map(lambda *leaves: jnp.stack(leaves), *received))
        current = jax.tree.map(lambda *leaves: jnp.stack(leaves), current, *received)
    own_part = expert((normed, weight_table))
    new_parts = [expert(block) for block in arrived]
    pending = None
    for stage in reversed(range(len(plan))):
        pairs_list = plan[stage]
        total = None if pending is None else pending[0]
        for index, pairs in enumerate(pairs_list, 1):
            outgoing = new_parts[stage][index - 1]
            if pending is not None:
                outgoing = outgoing + pending[index]
            back = [(target, source) for source, target in pairs]
            sent = lax.ppermute(outgoing.astype(jnp.bfloat16), "ep", back).astype(jnp.float32)
            total = sent if total is None else total + sent
        pending = total
    return own_part + pending


def gather_plan(mesh, shapes):
    kv_count, ep_count = mesh.devices.shape
    rows = ep_count * shapes[0][1] // kv_count
    if EXP_DEV != 1 or shapes[12][0] != ep_count or rows > 4096:
        return None
    places = []
    for device in mesh.devices[0]:
        coords = getattr(device, "coords", None)
        core = getattr(device, "core_on_chip", None)
        if coords is None or core is None:
            return None
        places.append(tuple(coords) + (core,))
    width = len(places[0])
    values = [sorted({p[a] for p in places}) for a in range(width)]
    varying = [a for a in range(width) if len(values[a]) > 1]
    total = 1
    for a in varying:
        total *= len(values[a])
    if total != ep_count or len(set(places)) != ep_count:
        return None
    rank_of = {p: r for r, p in enumerate(places)}
    core_axis = width - 1
    order = sorted((a for a in varying if a != core_axis), key=lambda a: -len(values[a]))
    order += [a for a in varying if a == core_axis]
    plan = []
    for a in order:
        size = len(values[a])
        stage = []
        for shift in range(1, size):
            pairs = []
            for r, p in enumerate(places):
                moved = list(p)
                moved[a] = values[a][(values[a].index(p[a]) + shift) % size]
                pairs.append((r, rank_of[tuple(moved)]))
            stage.append(pairs)
        plan.append(stage)
    return plan


def shards(
    plan,
    resid,
    queries,
    new_keys,
    new_values,
    cache_keys,
    cache_values,
    cached_len,
    group_request,
    w_out,
    norm_gain,
    route_ids,
    route_weights,
    gate_w,
    up_w,
    down_w,
):
    kv_rank = lax.axis_index("kv")
    ep_count = lax.axis_size("ep")
    tok_dev = resid.shape[1]
    cl_dev = cache_keys.shape[1]
    feat = queries.shape[2]
    head_count = feat // HEAD_DIM
    score_scale = 1.0 / math.sqrt(HEAD_DIM)
    request_index = jnp.arange(cached_len.shape[0], dtype=jnp.int32)
    length = jnp.sum(jnp.where(request_index == group_request[0], cached_len, 0))
    every_query = lax.all_gather(queries[0], "kv", axis=0, tiled=True)
    new_total = every_query.shape[0]
    query_heads = every_query.reshape(new_total, head_count, HEAD_DIM)
    key_cache = cache_keys[0].reshape(cl_dev, head_count, HEAD_DIM)
    value_cache = cache_values[0].reshape(cl_dev, head_count, HEAD_DIM)
    key_new = new_keys[0].reshape(tok_dev, head_count, HEAD_DIM)
    value_new = new_values[0].reshape(tok_dev, head_count, HEAD_DIM)
    score_cache = (
        jnp.einsum("qhd,khd->qhk", query_heads, key_cache, preferred_element_type=jnp.float32)
        * score_scale
    )
    position = kv_rank * cl_dev + jnp.arange(cl_dev, dtype=jnp.int32)
    score_cache = jnp.where((position < length)[None, None, :], score_cache, -jnp.inf)
    score_new = (
        jnp.einsum("qhd,khd->qhk", query_heads, key_new, preferred_element_type=jnp.float32)
        * score_scale
    )
    local_top = jnp.maximum(jnp.max(score_cache, axis=-1), jnp.max(score_new, axis=-1))
    expo_cache = jnp.exp(score_cache - local_top[..., None])
    expo_new = jnp.exp(score_new - local_top[..., None])
    denom = jnp.sum(expo_cache, axis=-1) + jnp.sum(expo_new, axis=-1)
    summed = jnp.einsum(
        "qhk,khd->qhd",
        expo_cache.astype(jnp.bfloat16),
        value_cache,
        preferred_element_type=jnp.float32,
    )
    summed = summed + jnp.einsum(
        "qhk,khd->qhd", expo_new.astype(jnp.bfloat16), value_new, preferred_element_type=jnp.float32
    )
    summed, denom = (summed.reshape(new_total, feat), denom)

    def join(first, second):
        first_top, first_denom, first_sum = first
        second_top, second_denom, second_sum = second
        joint_top = jnp.maximum(first_top, second_top)
        first_factor = jnp.exp(first_top - joint_top)
        second_factor = jnp.exp(second_top - joint_top)
        rows_here = first_sum.shape[0]
        joint_sum = (
            first_sum.reshape(rows_here, head_count, HEAD_DIM) * first_factor[..., None]
            + second_sum.reshape(rows_here, head_count, HEAD_DIM) * second_factor[..., None]
        )
        return (
            joint_top,
            first_denom * first_factor + second_denom * second_factor,
            joint_sum.reshape(rows_here, feat),
        )

    joint_top, joint_denom, joint_sum = combined_all((local_top, denom, summed), "kv", join)
    row_start = kv_rank * tok_dev
    own_sum = lax.dynamic_slice_in_dim(joint_sum, row_start, tok_dev, 0)
    own_denom = lax.dynamic_slice_in_dim(joint_denom, row_start, tok_dev, 0)
    attended = (
        (own_sum.reshape(tok_dev, head_count, HEAD_DIM) / own_denom[..., None])
        .reshape(tok_dev, feat)
        .astype(jnp.bfloat16)
    )
    proj = jnp.dot(attended, w_out, preferred_element_type=jnp.float32)
    hidden = (resid[0].astype(jnp.float32) + proj).astype(jnp.bfloat16)
    hidden_f = hidden.astype(jnp.float32)
    normed = (
        hidden_f
        * lax.rsqrt(jnp.mean(hidden_f * hidden_f, axis=-1, keepdims=True) + 1e-06)
        * norm_gain.astype(jnp.float32)
    ).astype(jnp.bfloat16)
    if plan is not None:
        moe_sum = dense_moe(plan, normed, route_ids[0], route_weights[0], gate_w, up_w, down_w)
        return (hidden_f + moe_sum).astype(jnp.bfloat16)[None]
    expert_count = EXP_DEV * ep_count
    capacity = min(tok_dev, max(2, tok_dev * TOP * 3 // (2 * expert_count)))
    route_flat = route_ids[0].reshape(-1)
    one_hot = (route_flat[:, None] == jnp.arange(expert_count, dtype=jnp.int32)[None, :]).astype(
        jnp.int32
    )
    rank_in = jnp.sum((jnp.cumsum(one_hot, axis=0) - 1) * one_hot, axis=1)
    slot_of = route_flat * capacity + rank_in
    slot_index = jnp.arange(expert_count * capacity, dtype=jnp.int32)
    placing = jnp.sum(
        (slot_of.reshape(tok_dev, TOP)[None, :, :] == slot_index[:, None, None]).astype(jnp.int32),
        axis=-1,
    ).astype(jnp.bfloat16)
    outgoing = jnp.dot(placing, normed, preferred_element_type=jnp.float32).astype(jnp.bfloat16)
    outgoing = outgoing.reshape(ep_count, EXP_DEV, capacity, D)
    full_gate, full_up, full_down = (
        lax.all_gather(gate_w, "kv", axis=2, tiled=True),
        lax.all_gather(up_w, "kv", axis=2, tiled=True),
        lax.all_gather(down_w, "kv", axis=1, tiled=True),
    )
    expert_out = expert_full(
        lax.all_to_all(outgoing, "ep", split_axis=0, concat_axis=0, tiled=True),
        full_gate,
        full_up,
        full_down,
    ).astype(jnp.bfloat16)
    returned = lax.all_to_all(expert_out, "ep", split_axis=0, concat_axis=0, tiled=True).reshape(
        expert_count * capacity, D
    )
    picked = jnp.take(returned, slot_of, axis=0).reshape(tok_dev, TOP, D)
    moe_sum = jnp.sum(picked.astype(jnp.float32) * route_weights[0][..., None], axis=1)
    return (hidden_f + moe_sum).astype(jnp.bfloat16)[None]


def solution(mesh):
    placed = (
        P("ep", "kv", None),
        P("ep", "kv", None),
        P("ep", "kv", None),
        P("ep", "kv", None),
        P("ep", "kv", None),
        P("ep", "kv", None),
        P(),
        P("ep"),
        P(),
        P(),
        P("ep", "kv", None),
        P("ep", "kv", None),
        P("ep", None, "kv"),
        P("ep", None, "kv"),
        P("ep", "kv", None),
    )

    def run(*args):
        plan = gather_plan(mesh, [a.shape for a in args])
        body = functools.partial(shards, plan)
        return jax.shard_map(
            body, mesh=mesh, in_specs=placed, out_specs=P("ep", "kv", None), check_vma=False
        )(*args)

    return run
```

```python
import functools
import math

import jax
import jax.numpy as jnp
import numpy as np
from jax import lax
from jax.sharding import PartitionSpec as P

D = 2048
HEAD_DIM = 128
TOP = 8
EXP_DEV = 1


def combined_all(shard, axis, join):
    gathered = jax.tree.map(
        lambda a, kind: lax.all_gather(a.astype(kind), axis),
        shard,
        (jnp.bfloat16, jnp.bfloat16, jnp.bfloat16),
    )

    def take(source):
        return jax.tree.map(
            lambda a, own: lax.dynamic_index_in_dim(a, source, 0, False).astype(own.dtype),
            gathered,
            shard,
        )

    return lax.fori_loop(
        1, lax.axis_size(axis), lambda source, state: join(state, take(source)), take(0)
    )


def expert_full(row_block, gate_part, up_part, down_part):
    gate_val = jnp.einsum(
        "sjkd,jdf->sjkf", row_block, gate_part, preferred_element_type=jnp.float32
    )
    up_val = jnp.einsum("sjkd,jdf->sjkf", row_block, up_part, preferred_element_type=jnp.float32)
    act = (jax.nn.silu(gate_val) * up_val).astype(jnp.bfloat16)
    return jnp.einsum("sjkf,jfd->sjkd", act, down_part, preferred_element_type=jnp.float32)


def full_weights(gate_w, up_w, down_w):
    kv_count = lax.axis_size("kv")
    if kv_count != 2:
        return (
            lax.all_gather(gate_w[0], "kv", axis=1, tiled=True),
            lax.all_gather(up_w[0], "kv", axis=1, tiled=True),
            lax.all_gather(down_w[0], "kv", axis=0, tiled=True),
        )
    mine = (gate_w[0], up_w[0], down_w[0])
    other = lax.ppermute(mine, "kv", [(0, 1), (1, 0)])
    first = lax.axis_index("kv") == 0
    joined = []
    for own, far, axis in zip(mine, other, (1, 1, 0)):
        low = jnp.where(first, own, far)
        high = jnp.where(first, far, own)
        joined.append(jnp.concatenate([low, high], axis=axis))
    return tuple(joined)


def dense_moe(plan, normed, route_ids, route_weights, gate_w, up_w, down_w):
    tok_dev = normed.shape[0]
    expert_count = EXP_DEV * lax.axis_size("ep")
    experts = jnp.arange(expert_count, dtype=jnp.int32)
    own_expert = lax.axis_index("ep")
    chosen = route_ids[:, :, None] == experts[None, None, :]
    weight_table = jnp.sum(jnp.where(chosen, route_weights[:, :, None], 0.0), axis=1)
    own_weight = jnp.sum(jnp.where(experts == own_expert, weight_table, 0.0), axis=1)
    every_table = lax.all_gather(weight_table, "ep", axis=0, tiled=True)
    full_gate, full_up, full_down = full_weights(gate_w, up_w, down_w)
    normed, full_gate, full_up, full_down = lax.optimization_barrier(
        (normed, full_gate, full_up, full_down)
    )
    ep_count = lax.axis_size("ep")

    def expert(rows, origin):
        if origin is None:
            weights = own_weight
        else:
            source = jnp.asarray(origin, jnp.int32)[own_expert]
            table = lax.dynamic_slice_in_dim(every_table, source * tok_dev, tok_dev, 0)
            weights = jnp.sum(jnp.where(experts == own_expert, table, 0.0), axis=1)
        gate_val = jnp.dot(rows, full_gate, preferred_element_type=jnp.float32)
        up_val = jnp.dot(rows, full_up, preferred_element_type=jnp.float32)
        act = (jax.nn.silu(gate_val) * up_val).astype(jnp.bfloat16)
        out_rows = jnp.dot(act, full_down, preferred_element_type=jnp.float32)
        out_rows = out_rows.astype(jnp.bfloat16).astype(jnp.float32)
        return out_rows * weights[:, None]

    pieces = [(normed, np.arange(ep_count), None, None)]
    for pairs_list in plan:
        grown = []
        for parent, (rows, origin, _, _) in enumerate(pieces):
            for pairs in pairs_list:
                moved = np.zeros_like(origin)
                for source, target in pairs:
                    moved[target] = origin[source]
                grown.append((lax.ppermute(rows, "ep", pairs), moved, parent, pairs))
        pieces = pieces + grown
    partial = [expert(rows, None if index == 0 else origin) for index, (rows, origin, _, _) in enumerate(pieces)]
    for index in reversed(range(1, len(pieces))):
        _, _, parent, pairs = pieces[index]
        back = [(target, source) for source, target in pairs]
        sent = lax.ppermute(partial[index].astype(jnp.bfloat16), "ep", back)
        partial[parent] = partial[parent] + sent.astype(jnp.float32)
    return partial[0]


def gather_plan(mesh, shapes):
    kv_count, ep_count = mesh.devices.shape
    rows = ep_count * shapes[0][1] // kv_count
    if EXP_DEV != 1 or shapes[12][0] != ep_count or rows > 4096:
        return None
    places = []
    for device in mesh.devices[0]:
        coords = getattr(device, "coords", None)
        core = getattr(device, "core_on_chip", None)
        if coords is None or core is None:
            return None
        places.append(tuple(coords) + (core,))
    width = len(places[0])
    values = [sorted({p[a] for p in places}) for a in range(width)]
    varying = [a for a in range(width) if len(values[a]) > 1]
    total = 1
    for a in varying:
        total *= len(values[a])
    if total != ep_count or len(set(places)) != ep_count:
        return None
    rank_of = {p: r for r, p in enumerate(places)}
    core_axis = width - 1
    order = sorted((a for a in varying if a != core_axis), key=lambda a: -len(values[a]))
    order += [a for a in varying if a == core_axis]
    plan = []
    for a in order:
        size = len(values[a])
        stage = []
        for shift in range(1, size):
            pairs = []
            for r, p in enumerate(places):
                moved = list(p)
                moved[a] = values[a][(values[a].index(p[a]) + shift) % size]
                pairs.append((r, rank_of[tuple(moved)]))
            stage.append(pairs)
        plan.append(stage)
    return plan


def shards(
    plan,
    resid,
    queries,
    new_keys,
    new_values,
    cache_keys,
    cache_values,
    cached_len,
    group_request,
    w_out,
    norm_gain,
    route_ids,
    route_weights,
    gate_w,
    up_w,
    down_w,
):
    kv_rank = lax.axis_index("kv")
    ep_count = lax.axis_size("ep")
    tok_dev = resid.shape[1]
    cl_dev = cache_keys.shape[1]
    feat = queries.shape[2]
    head_count = feat // HEAD_DIM
    score_scale = 1.0 / math.sqrt(HEAD_DIM)
    request_index = jnp.arange(cached_len.shape[0], dtype=jnp.int32)
    length = jnp.sum(jnp.where(request_index == group_request[0], cached_len, 0))
    every_query = lax.all_gather(queries[0], "kv", axis=0, tiled=True)
    new_total = every_query.shape[0]
    query_heads = every_query.reshape(new_total, head_count, HEAD_DIM)
    key_cache = cache_keys[0].reshape(cl_dev, head_count, HEAD_DIM)
    value_cache = cache_values[0].reshape(cl_dev, head_count, HEAD_DIM)
    key_new = new_keys[0].reshape(tok_dev, head_count, HEAD_DIM)
    value_new = new_values[0].reshape(tok_dev, head_count, HEAD_DIM)
    score_cache = (
        jnp.einsum("qhd,khd->qhk", query_heads, key_cache, preferred_element_type=jnp.float32)
        * score_scale
    )
    position = kv_rank * cl_dev + jnp.arange(cl_dev, dtype=jnp.int32)
    score_cache = jnp.where((position < length)[None, None, :], score_cache, -jnp.inf)
    score_new = (
        jnp.einsum("qhd,khd->qhk", query_heads, key_new, preferred_element_type=jnp.float32)
        * score_scale
    )
    local_top = jnp.maximum(jnp.max(score_cache, axis=-1), jnp.max(score_new, axis=-1))
    expo_cache = jnp.exp(score_cache - local_top[..., None])
    expo_new = jnp.exp(score_new - local_top[..., None])
    denom = jnp.sum(expo_cache, axis=-1) + jnp.sum(expo_new, axis=-1)
    summed = jnp.einsum(
        "qhk,khd->qhd",
        expo_cache.astype(jnp.bfloat16),
        value_cache,
        preferred_element_type=jnp.float32,
    )
    summed = summed + jnp.einsum(
        "qhk,khd->qhd", expo_new.astype(jnp.bfloat16), value_new, preferred_element_type=jnp.float32
    )
    summed, denom = (summed.reshape(new_total, feat), denom)

    def join(first, second):
        first_top, first_denom, first_sum = first
        second_top, second_denom, second_sum = second
        joint_top = jnp.maximum(first_top, second_top)
        first_factor = jnp.exp(first_top - joint_top)
        second_factor = jnp.exp(second_top - joint_top)
        rows_here = first_sum.shape[0]
        joint_sum = (
            first_sum.reshape(rows_here, head_count, HEAD_DIM) * first_factor[..., None]
            + second_sum.reshape(rows_here, head_count, HEAD_DIM) * second_factor[..., None]
        )
        return (
            joint_top,
            first_denom * first_factor + second_denom * second_factor,
            joint_sum.reshape(rows_here, feat),
        )

    joint_top, joint_denom, joint_sum = combined_all((local_top, denom, summed), "kv", join)
    row_start = kv_rank * tok_dev
    own_sum = lax.dynamic_slice_in_dim(joint_sum, row_start, tok_dev, 0)
    own_denom = lax.dynamic_slice_in_dim(joint_denom, row_start, tok_dev, 0)
    attended = (
        (own_sum.reshape(tok_dev, head_count, HEAD_DIM) / own_denom[..., None])
        .reshape(tok_dev, feat)
        .astype(jnp.bfloat16)
    )
    proj = jnp.dot(attended, w_out, preferred_element_type=jnp.float32)
    hidden = (resid[0].astype(jnp.float32) + proj).astype(jnp.bfloat16)
    hidden_f = hidden.astype(jnp.float32)
    normed = (
        hidden_f
        * lax.rsqrt(jnp.mean(hidden_f * hidden_f, axis=-1, keepdims=True) + 1e-06)
        * norm_gain.astype(jnp.float32)
    ).astype(jnp.bfloat16)
    if plan is not None:
        moe_sum = dense_moe(plan, normed, route_ids[0], route_weights[0], gate_w, up_w, down_w)
        return (hidden_f + moe_sum).astype(jnp.bfloat16)[None]
    expert_count = EXP_DEV * ep_count
    capacity = min(tok_dev, max(2, tok_dev * TOP * 3 // (2 * expert_count)))
    route_flat = route_ids[0].reshape(-1)
    one_hot = (route_flat[:, None] == jnp.arange(expert_count, dtype=jnp.int32)[None, :]).astype(
        jnp.int32
    )
    rank_in = jnp.sum((jnp.cumsum(one_hot, axis=0) - 1) * one_hot, axis=1)
    slot_of = route_flat * capacity + rank_in
    slot_index = jnp.arange(expert_count * capacity, dtype=jnp.int32)
    placing = jnp.sum(
        (slot_of.reshape(tok_dev, TOP)[None, :, :] == slot_index[:, None, None]).astype(jnp.int32),
        axis=-1,
    ).astype(jnp.bfloat16)
    outgoing = jnp.dot(placing, normed, preferred_element_type=jnp.float32).astype(jnp.bfloat16)
    outgoing = outgoing.reshape(ep_count, EXP_DEV, capacity, D)
    full_gate, full_up, full_down = (
        lax.all_gather(gate_w, "kv", axis=2, tiled=True),
        lax.all_gather(up_w, "kv", axis=2, tiled=True),
        lax.all_gather(down_w, "kv", axis=1, tiled=True),
    )
    expert_out = expert_full(
        lax.all_to_all(outgoing, "ep", split_axis=0, concat_axis=0, tiled=True),
        full_gate,
        full_up,
        full_down,
    ).astype(jnp.bfloat16)
    returned = lax.all_to_all(expert_out, "ep", split_axis=0, concat_axis=0, tiled=True).reshape(
        expert_count * capacity, D
    )
    picked = jnp.take(returned, slot_of, axis=0).reshape(tok_dev, TOP, D)
    moe_sum = jnp.sum(picked.astype(jnp.float32) * route_weights[0][..., None], axis=1)
    return (hidden_f + moe_sum).astype(jnp.bfloat16)[None]


def solution(mesh):
    placed = (
        P("ep", "kv", None),
        P("ep", "kv", None),
        P("ep", "kv", None),
        P("ep", "kv", None),
        P("ep", "kv", None),
        P("ep", "kv", None),
        P(),
        P("ep"),
        P(),
        P(),
        P("ep", "kv", None),
        P("ep", "kv", None),
        P("ep", None, "kv"),
        P("ep", None, "kv"),
        P("ep", "kv", None),
    )

    def run(*args):
        plan = gather_plan(mesh, [a.shape for a in args])
        body = functools.partial(shards, plan)
        return jax.shard_map(
            body, mesh=mesh, in_specs=placed, out_specs=P("ep", "kv", None), check_vma=False
        )(*args)

    return run
```

```python
import functools
import math

import jax
import jax.numpy as jnp
import numpy as np
from jax import lax
from jax.sharding import PartitionSpec as P

D = 2048
HEAD_DIM = 128
TOP = 8
EXP_DEV = 1


def combined_all(shard, axis, join):
    gathered = jax.tree.map(
        lambda a, kind: lax.all_gather(a.astype(kind), axis),
        shard,
        (jnp.bfloat16, jnp.bfloat16, jnp.bfloat16),
    )

    def take(source):
        return jax.tree.map(
            lambda a, own: lax.dynamic_index_in_dim(a, source, 0, False).astype(own.dtype),
            gathered,
            shard,
        )

    return lax.fori_loop(
        1, lax.axis_size(axis), lambda source, state: join(state, take(source)), take(0)
    )


def expert_full(row_block, gate_part, up_part, down_part):
    gate_val = jnp.einsum(
        "sjkd,jdf->sjkf", row_block, gate_part, preferred_element_type=jnp.float32
    )
    up_val = jnp.einsum("sjkd,jdf->sjkf", row_block, up_part, preferred_element_type=jnp.float32)
    act = (jax.nn.silu(gate_val) * up_val).astype(jnp.bfloat16)
    return jnp.einsum("sjkf,jfd->sjkd", act, down_part, preferred_element_type=jnp.float32)


def full_weights(gate_w, up_w, down_w):
    kv_count = lax.axis_size("kv")
    if kv_count != 2:
        return (
            lax.all_gather(gate_w[0], "kv", axis=1, tiled=True),
            lax.all_gather(up_w[0], "kv", axis=1, tiled=True),
            lax.all_gather(down_w[0], "kv", axis=0, tiled=True),
        )
    mine = (gate_w[0], up_w[0], down_w[0])
    other = lax.ppermute(mine, "kv", [(0, 1), (1, 0)])
    first = lax.axis_index("kv") == 0
    joined = []
    for own, far, axis in zip(mine, other, (1, 1, 0)):
        low = jnp.where(first, own, far)
        high = jnp.where(first, far, own)
        joined.append(jnp.concatenate([low, high], axis=axis))
    return tuple(joined)


def dense_moe(plan, normed, route_ids, route_weights, weight_parts, anchor):
    expert_count = EXP_DEV * lax.axis_size("ep")
    experts = jnp.arange(expert_count, dtype=jnp.int32)
    own_expert = lax.axis_index("ep")
    chosen = route_ids[:, :, None] == experts[None, None, :]
    weight_table = jnp.sum(jnp.where(chosen, route_weights[:, :, None], 0.0), axis=1)
    weight_parts, anchor = lax.optimization_barrier((weight_parts, anchor))
    full = list(full_weights(*weight_parts))

    def expert(rows, table):
        weights = jnp.sum(jnp.where(experts == own_expert, table, 0.0), axis=1)
        gate_val = jnp.dot(rows, full[0], preferred_element_type=jnp.float32)
        up_val = jnp.dot(rows, full[1], preferred_element_type=jnp.float32)
        act = (jax.nn.silu(gate_val) * up_val).astype(jnp.bfloat16)
        out_rows = jnp.dot(act, full[2], preferred_element_type=jnp.float32)
        out_rows = out_rows.astype(jnp.bfloat16).astype(jnp.float32)
        return out_rows * weights[:, None]

    pieces = [((normed, weight_table), None, None)]
    for number, pairs_list in enumerate(plan):
        grown = []
        for parent, (block, _, _) in enumerate(pieces):
            for pairs in pairs_list:
                grown.append((lax.ppermute(block, "ep", pairs), parent, pairs))
        if number == 1:
            tied = lax.optimization_barrier((tuple(full), [piece[0] for piece in grown]))
            full = list(tied[0])
            grown = [(block, parent, pairs) for block, (_, parent, pairs) in zip(tied[1], grown)]
        pieces = pieces + grown
    partial = [expert(*block) for block, _, _ in pieces]
    for index in reversed(range(1, len(pieces))):
        _, parent, pairs = pieces[index]
        back = [(target, source) for source, target in pairs]
        sent = lax.ppermute(partial[index].astype(jnp.bfloat16), "ep", back)
        partial[parent] = partial[parent] + sent.astype(jnp.float32)
    return partial[0], anchor


def gather_plan(mesh, shapes):
    kv_count, ep_count = mesh.devices.shape
    rows = ep_count * shapes[0][1] // kv_count
    if EXP_DEV != 1 or shapes[12][0] != ep_count or rows > 4096:
        return None
    places = []
    for device in mesh.devices[0]:
        coords = getattr(device, "coords", None)
        core = getattr(device, "core_on_chip", None)
        if coords is None or core is None:
            return None
        places.append(tuple(coords) + (core,))
    width = len(places[0])
    values = [sorted({p[a] for p in places}) for a in range(width)]
    varying = [a for a in range(width) if len(values[a]) > 1]
    total = 1
    for a in varying:
        total *= len(values[a])
    if total != ep_count or len(set(places)) != ep_count:
        return None
    rank_of = {p: r for r, p in enumerate(places)}
    core_axis = width - 1
    order = sorted((a for a in varying if a != core_axis), key=lambda a: -len(values[a]))
    order += [a for a in varying if a == core_axis]
    plan = []
    for a in order:
        size = len(values[a])
        stage = []
        for shift in range(1, size):
            pairs = []
            for r, p in enumerate(places):
                moved = list(p)
                moved[a] = values[a][(values[a].index(p[a]) + shift) % size]
                pairs.append((r, rank_of[tuple(moved)]))
            stage.append(pairs)
        plan.append(stage)
    return plan


def shards(
    plan,
    resid,
    queries,
    new_keys,
    new_values,
    cache_keys,
    cache_values,
    cached_len,
    group_request,
    w_out,
    norm_gain,
    route_ids,
    route_weights,
    gate_w,
    up_w,
    down_w,
):
    kv_rank = lax.axis_index("kv")
    ep_count = lax.axis_size("ep")
    tok_dev = resid.shape[1]
    cl_dev = cache_keys.shape[1]
    feat = queries.shape[2]
    head_count = feat // HEAD_DIM
    score_scale = 1.0 / math.sqrt(HEAD_DIM)
    request_index = jnp.arange(cached_len.shape[0], dtype=jnp.int32)
    length = jnp.sum(jnp.where(request_index == group_request[0], cached_len, 0))
    every_query = lax.all_gather(queries[0], "kv", axis=0, tiled=True)
    new_total = every_query.shape[0]
    query_heads = every_query.reshape(new_total, head_count, HEAD_DIM)
    key_cache = cache_keys[0].reshape(cl_dev, head_count, HEAD_DIM)
    value_cache = cache_values[0].reshape(cl_dev, head_count, HEAD_DIM)
    key_new = new_keys[0].reshape(tok_dev, head_count, HEAD_DIM)
    value_new = new_values[0].reshape(tok_dev, head_count, HEAD_DIM)
    score_cache = (
        jnp.einsum("qhd,khd->qhk", query_heads, key_cache, preferred_element_type=jnp.float32)
        * score_scale
    )
    position = kv_rank * cl_dev + jnp.arange(cl_dev, dtype=jnp.int32)
    score_cache = jnp.where((position < length)[None, None, :], score_cache, -jnp.inf)
    score_new = (
        jnp.einsum("qhd,khd->qhk", query_heads, key_new, preferred_element_type=jnp.float32)
        * score_scale
    )
    local_top = jnp.maximum(jnp.max(score_cache, axis=-1), jnp.max(score_new, axis=-1))
    expo_cache = jnp.exp(score_cache - local_top[..., None])
    expo_new = jnp.exp(score_new - local_top[..., None])
    denom = jnp.sum(expo_cache, axis=-1) + jnp.sum(expo_new, axis=-1)
    summed = jnp.einsum(
        "qhk,khd->qhd",
        expo_cache.astype(jnp.bfloat16),
        value_cache,
        preferred_element_type=jnp.float32,
    )
    summed = summed + jnp.einsum(
        "qhk,khd->qhd", expo_new.astype(jnp.bfloat16), value_new, preferred_element_type=jnp.float32
    )
    summed, denom = (summed.reshape(new_total, feat), denom)

    def join(first, second):
        first_top, first_denom, first_sum = first
        second_top, second_denom, second_sum = second
        joint_top = jnp.maximum(first_top, second_top)
        first_factor = jnp.exp(first_top - joint_top)
        second_factor = jnp.exp(second_top - joint_top)
        rows_here = first_sum.shape[0]
        joint_sum = (
            first_sum.reshape(rows_here, head_count, HEAD_DIM) * first_factor[..., None]
            + second_sum.reshape(rows_here, head_count, HEAD_DIM) * second_factor[..., None]
        )
        return (
            joint_top,
            first_denom * first_factor + second_denom * second_factor,
            joint_sum.reshape(rows_here, feat),
        )

    joint_top, joint_denom, joint_sum = combined_all((local_top, denom, summed), "kv", join)
    row_start = kv_rank * tok_dev
    own_sum = lax.dynamic_slice_in_dim(joint_sum, row_start, tok_dev, 0)
    own_denom = lax.dynamic_slice_in_dim(joint_denom, row_start, tok_dev, 0)
    attended = (
        (own_sum.reshape(tok_dev, head_count, HEAD_DIM) / own_denom[..., None])
        .reshape(tok_dev, feat)
        .astype(jnp.bfloat16)
    )
    proj = jnp.dot(attended, w_out, preferred_element_type=jnp.float32)
    hidden = (resid[0].astype(jnp.float32) + proj).astype(jnp.bfloat16)
    hidden_f = hidden.astype(jnp.float32)
    normed = (
        hidden_f
        * lax.rsqrt(jnp.mean(hidden_f * hidden_f, axis=-1, keepdims=True) + 1e-06)
        * norm_gain.astype(jnp.float32)
    ).astype(jnp.bfloat16)
    if plan is not None:
        moe_sum, _ = dense_moe(
            plan, normed, route_ids[0], route_weights[0], (gate_w, up_w, down_w), joint_denom
        )
        return (hidden_f + moe_sum).astype(jnp.bfloat16)[None]
    expert_count = EXP_DEV * ep_count
    capacity = min(tok_dev, max(2, tok_dev * TOP * 3 // (2 * expert_count)))
    route_flat = route_ids[0].reshape(-1)
    one_hot = (route_flat[:, None] == jnp.arange(expert_count, dtype=jnp.int32)[None, :]).astype(
        jnp.int32
    )
    rank_in = jnp.sum((jnp.cumsum(one_hot, axis=0) - 1) * one_hot, axis=1)
    slot_of = route_flat * capacity + rank_in
    slot_index = jnp.arange(expert_count * capacity, dtype=jnp.int32)
    placing = jnp.sum(
        (slot_of.reshape(tok_dev, TOP)[None, :, :] == slot_index[:, None, None]).astype(jnp.int32),
        axis=-1,
    ).astype(jnp.bfloat16)
    outgoing = jnp.dot(placing, normed, preferred_element_type=jnp.float32).astype(jnp.bfloat16)
    outgoing = outgoing.reshape(ep_count, EXP_DEV, capacity, D)
    full_gate, full_up, full_down = (
        lax.all_gather(gate_w, "kv", axis=2, tiled=True),
        lax.all_gather(up_w, "kv", axis=2, tiled=True),
        lax.all_gather(down_w, "kv", axis=1, tiled=True),
    )
    expert_out = expert_full(
        lax.all_to_all(outgoing, "ep", split_axis=0, concat_axis=0, tiled=True),
        full_gate,
        full_up,
        full_down,
    ).astype(jnp.bfloat16)
    returned = lax.all_to_all(expert_out, "ep", split_axis=0, concat_axis=0, tiled=True).reshape(
        expert_count * capacity, D
    )
    picked = jnp.take(returned, slot_of, axis=0).reshape(tok_dev, TOP, D)
    moe_sum = jnp.sum(picked.astype(jnp.float32) * route_weights[0][..., None], axis=1)
    return (hidden_f + moe_sum).astype(jnp.bfloat16)[None]


def solution(mesh):
    placed = (
        P("ep", "kv", None),
        P("ep", "kv", None),
        P("ep", "kv", None),
        P("ep", "kv", None),
        P("ep", "kv", None),
        P("ep", "kv", None),
        P(),
        P("ep"),
        P(),
        P(),
        P("ep", "kv", None),
        P("ep", "kv", None),
        P("ep", None, "kv"),
        P("ep", None, "kv"),
        P("ep", "kv", None),
    )

    def run(*args):
        plan = gather_plan(mesh, [a.shape for a in args])
        body = functools.partial(shards, plan)
        return jax.shard_map(
            body, mesh=mesh, in_specs=placed, out_specs=P("ep", "kv", None), check_vma=False
        )(*args)

    return run
```

```python
import functools
import math

import jax
import jax.numpy as jnp
import numpy as np
from jax import lax
from jax.sharding import PartitionSpec as P

D = 2048
HEAD_DIM = 128
TOP = 8
EXP_DEV = 1


def combined_all(shard, axis, join):
    gathered = jax.tree.map(
        lambda a, kind: lax.all_gather(a.astype(kind), axis),
        shard,
        (jnp.bfloat16, jnp.bfloat16, jnp.bfloat16),
    )

    def take(source):
        return jax.tree.map(
            lambda a, own: lax.dynamic_index_in_dim(a, source, 0, False).astype(own.dtype),
            gathered,
            shard,
        )

    return lax.fori_loop(
        1, lax.axis_size(axis), lambda source, state: join(state, take(source)), take(0)
    )


def expert_full(row_block, gate_part, up_part, down_part):
    gate_val = jnp.einsum(
        "sjkd,jdf->sjkf", row_block, gate_part, preferred_element_type=jnp.float32
    )
    up_val = jnp.einsum("sjkd,jdf->sjkf", row_block, up_part, preferred_element_type=jnp.float32)
    act = (jax.nn.silu(gate_val) * up_val).astype(jnp.bfloat16)
    return jnp.einsum("sjkf,jfd->sjkd", act, down_part, preferred_element_type=jnp.float32)


def full_weights(gate_w, up_w, down_w):
    kv_count = lax.axis_size("kv")
    if kv_count != 2:
        return (
            lax.all_gather(gate_w[0], "kv", axis=1, tiled=True),
            lax.all_gather(up_w[0], "kv", axis=1, tiled=True),
            lax.all_gather(down_w[0], "kv", axis=0, tiled=True),
        )
    mine = (gate_w[0], up_w[0], down_w[0])
    other = lax.ppermute(mine, "kv", [(0, 1), (1, 0)])
    first = lax.axis_index("kv") == 0
    joined = []
    for own, far, axis in zip(mine, other, (1, 1, 0)):
        low = jnp.where(first, own, far)
        high = jnp.where(first, far, own)
        joined.append(jnp.concatenate([low, high], axis=axis))
    return tuple(joined)


def dense_moe(plan, normed, route_ids, route_weights, weight_parts, anchor):
    expert_count = EXP_DEV * lax.axis_size("ep")
    experts = jnp.arange(expert_count, dtype=jnp.int32)
    own_expert = lax.axis_index("ep")
    chosen = route_ids[:, :, None] == experts[None, None, :]
    weight_table = jnp.sum(jnp.where(chosen, route_weights[:, :, None], 0.0), axis=1)
    weight_parts, anchor = lax.optimization_barrier((weight_parts, anchor))
    full = list(full_weights(*weight_parts))

    def expert(rows, table):
        weights = jnp.sum(jnp.where(experts == own_expert, table, 0.0), axis=1)
        gate_val = jnp.dot(rows, full[0], preferred_element_type=jnp.float32)
        up_val = jnp.dot(rows, full[1], preferred_element_type=jnp.float32)
        act = (jax.nn.silu(gate_val) * up_val).astype(jnp.bfloat16)
        out_rows = jnp.dot(act, full[2], preferred_element_type=jnp.float32)
        out_rows = out_rows.astype(jnp.bfloat16).astype(jnp.float32)
        return out_rows * weights[:, None]

    pieces = [((normed, weight_table), None, None)]
    for number, pairs_list in enumerate(plan):
        grown = []
        for parent, (block, _, _) in enumerate(pieces):
            for pairs in pairs_list:
                grown.append((lax.ppermute(block, "ep", pairs), parent, pairs))
        if number == 1:
            tied = lax.optimization_barrier((tuple(full), [piece[0] for piece in grown]))
            full = list(tied[0])
            grown = [(block, parent, pairs) for block, (_, parent, pairs) in zip(tied[1], grown)]
        pieces = pieces + grown
    partial = [None] * len(pieces)
    counts = [1]
    for pairs_list in plan:
        counts.append(counts[-1] * (len(pairs_list) + 1))
    for low, high in zip([0] + counts[1:-1], counts[1:]):
        rows = jnp.concatenate([pieces[i][0][0] for i in range(low, high)], axis=0)
        table = jnp.concatenate([pieces[i][0][1] for i in range(low, high)], axis=0)
        out = expert(rows, table)
        size = pieces[0][0][0].shape[0]
        for offset, i in enumerate(range(low, high)):
            partial[i] = out[offset * size:(offset + 1) * size]
    for index in reversed(range(1, len(pieces))):
        _, parent, pairs = pieces[index]
        back = [(target, source) for source, target in pairs]
        sent = lax.ppermute(partial[index].astype(jnp.bfloat16), "ep", back)
        partial[parent] = partial[parent] + sent.astype(jnp.float32)
    return partial[0], anchor


def gather_plan(mesh, shapes):
    kv_count, ep_count = mesh.devices.shape
    rows = ep_count * shapes[0][1] // kv_count
    if EXP_DEV != 1 or shapes[12][0] != ep_count or rows > 4096:
        return None
    places = []
    for device in mesh.devices[0]:
        coords = getattr(device, "coords", None)
        core = getattr(device, "core_on_chip", None)
        if coords is None or core is None:
            return None
        places.append(tuple(coords) + (core,))
    width = len(places[0])
    values = [sorted({p[a] for p in places}) for a in range(width)]
    varying = [a for a in range(width) if len(values[a]) > 1]
    total = 1
    for a in varying:
        total *= len(values[a])
    if total != ep_count or len(set(places)) != ep_count:
        return None
    rank_of = {p: r for r, p in enumerate(places)}
    core_axis = width - 1
    order = sorted((a for a in varying if a != core_axis), key=lambda a: -len(values[a]))
    order += [a for a in varying if a == core_axis]
    plan = []
    for a in order:
        size = len(values[a])
        stage = []
        for shift in range(1, size):
            pairs = []
            for r, p in enumerate(places):
                moved = list(p)
                moved[a] = values[a][(values[a].index(p[a]) + shift) % size]
                pairs.append((r, rank_of[tuple(moved)]))
            stage.append(pairs)
        plan.append(stage)
    return plan


def shards(
    plan,
    resid,
    queries,
    new_keys,
    new_values,
    cache_keys,
    cache_values,
    cached_len,
    group_request,
    w_out,
    norm_gain,
    route_ids,
    route_weights,
    gate_w,
    up_w,
    down_w,
):
    kv_rank = lax.axis_index("kv")
    ep_count = lax.axis_size("ep")
    tok_dev = resid.shape[1]
    cl_dev = cache_keys.shape[1]
    feat = queries.shape[2]
    head_count = feat // HEAD_DIM
    score_scale = 1.0 / math.sqrt(HEAD_DIM)
    request_index = jnp.arange(cached_len.shape[0], dtype=jnp.int32)
    length = jnp.sum(jnp.where(request_index == group_request[0], cached_len, 0))
    every_query = lax.all_gather(queries[0], "kv", axis=0, tiled=True)
    new_total = every_query.shape[0]
    query_heads = every_query.reshape(new_total, head_count, HEAD_DIM)
    key_cache = cache_keys[0].reshape(cl_dev, head_count, HEAD_DIM)
    value_cache = cache_values[0].reshape(cl_dev, head_count, HEAD_DIM)
    key_new = new_keys[0].reshape(tok_dev, head_count, HEAD_DIM)
    value_new = new_values[0].reshape(tok_dev, head_count, HEAD_DIM)
    score_cache = (
        jnp.einsum("qhd,khd->qhk", query_heads, key_cache, preferred_element_type=jnp.float32)
        * score_scale
    )
    position = kv_rank * cl_dev + jnp.arange(cl_dev, dtype=jnp.int32)
    score_cache = jnp.where((position < length)[None, None, :], score_cache, -jnp.inf)
    score_new = (
        jnp.einsum("qhd,khd->qhk", query_heads, key_new, preferred_element_type=jnp.float32)
        * score_scale
    )
    local_top = jnp.maximum(jnp.max(score_cache, axis=-1), jnp.max(score_new, axis=-1))
    expo_cache = jnp.exp(score_cache - local_top[..., None])
    expo_new = jnp.exp(score_new - local_top[..., None])
    denom = jnp.sum(expo_cache, axis=-1) + jnp.sum(expo_new, axis=-1)
    summed = jnp.einsum(
        "qhk,khd->qhd",
        expo_cache.astype(jnp.bfloat16),
        value_cache,
        preferred_element_type=jnp.float32,
    )
    summed = summed + jnp.einsum(
        "qhk,khd->qhd", expo_new.astype(jnp.bfloat16), value_new, preferred_element_type=jnp.float32
    )
    summed, denom = (summed.reshape(new_total, feat), denom)

    def join(first, second):
        first_top, first_denom, first_sum = first
        second_top, second_denom, second_sum = second
        joint_top = jnp.maximum(first_top, second_top)
        first_factor = jnp.exp(first_top - joint_top)
        second_factor = jnp.exp(second_top - joint_top)
        rows_here = first_sum.shape[0]
        joint_sum = (
            first_sum.reshape(rows_here, head_count, HEAD_DIM) * first_factor[..., None]
            + second_sum.reshape(rows_here, head_count, HEAD_DIM) * second_factor[..., None]
        )
        return (
            joint_top,
            first_denom * first_factor + second_denom * second_factor,
            joint_sum.reshape(rows_here, feat),
        )

    joint_top, joint_denom, joint_sum = combined_all((local_top, denom, summed), "kv", join)
    row_start = kv_rank * tok_dev
    own_sum = lax.dynamic_slice_in_dim(joint_sum, row_start, tok_dev, 0)
    own_denom = lax.dynamic_slice_in_dim(joint_denom, row_start, tok_dev, 0)
    attended = (
        (own_sum.reshape(tok_dev, head_count, HEAD_DIM) / own_denom[..., None])
        .reshape(tok_dev, feat)
        .astype(jnp.bfloat16)
    )
    proj = jnp.dot(attended, w_out, preferred_element_type=jnp.float32)
    hidden = (resid[0].astype(jnp.float32) + proj).astype(jnp.bfloat16)
    hidden_f = hidden.astype(jnp.float32)
    normed = (
        hidden_f
        * lax.rsqrt(jnp.mean(hidden_f * hidden_f, axis=-1, keepdims=True) + 1e-06)
        * norm_gain.astype(jnp.float32)
    ).astype(jnp.bfloat16)
    if plan is not None:
        moe_sum, _ = dense_moe(
            plan, normed, route_ids[0], route_weights[0], (gate_w, up_w, down_w), joint_denom
        )
        return (hidden_f + moe_sum).astype(jnp.bfloat16)[None]
    expert_count = EXP_DEV * ep_count
    capacity = min(tok_dev, max(2, tok_dev * TOP * 3 // (2 * expert_count)))
    route_flat = route_ids[0].reshape(-1)
    one_hot = (route_flat[:, None] == jnp.arange(expert_count, dtype=jnp.int32)[None, :]).astype(
        jnp.int32
    )
    rank_in = jnp.sum((jnp.cumsum(one_hot, axis=0) - 1) * one_hot, axis=1)
    slot_of = route_flat * capacity + rank_in
    slot_index = jnp.arange(expert_count * capacity, dtype=jnp.int32)
    placing = jnp.sum(
        (slot_of.reshape(tok_dev, TOP)[None, :, :] == slot_index[:, None, None]).astype(jnp.int32),
        axis=-1,
    ).astype(jnp.bfloat16)
    outgoing = jnp.dot(placing, normed, preferred_element_type=jnp.float32).astype(jnp.bfloat16)
    outgoing = outgoing.reshape(ep_count, EXP_DEV, capacity, D)
    full_gate, full_up, full_down = (
        lax.all_gather(gate_w, "kv", axis=2, tiled=True),
        lax.all_gather(up_w, "kv", axis=2, tiled=True),
        lax.all_gather(down_w, "kv", axis=1, tiled=True),
    )
    expert_out = expert_full(
        lax.all_to_all(outgoing, "ep", split_axis=0, concat_axis=0, tiled=True),
        full_gate,
        full_up,
        full_down,
    ).astype(jnp.bfloat16)
    returned = lax.all_to_all(expert_out, "ep", split_axis=0, concat_axis=0, tiled=True).reshape(
        expert_count * capacity, D
    )
    picked = jnp.take(returned, slot_of, axis=0).reshape(tok_dev, TOP, D)
    moe_sum = jnp.sum(picked.astype(jnp.float32) * route_weights[0][..., None], axis=1)
    return (hidden_f + moe_sum).astype(jnp.bfloat16)[None]


def solution(mesh):
    placed = (
        P("ep", "kv", None),
        P("ep", "kv", None),
        P("ep", "kv", None),
        P("ep", "kv", None),
        P("ep", "kv", None),
        P("ep", "kv", None),
        P(),
        P("ep"),
        P(),
        P(),
        P("ep", "kv", None),
        P("ep", "kv", None),
        P("ep", None, "kv"),
        P("ep", None, "kv"),
        P("ep", "kv", None),
    )

    def run(*args):
        plan = gather_plan(mesh, [a.shape for a in args])
        body = functools.partial(shards, plan)
        return jax.shard_map(
            body, mesh=mesh, in_specs=placed, out_specs=P("ep", "kv", None), check_vma=False
        )(*args)

    return run
```

```python
import functools
import math

import jax
import jax.numpy as jnp
import numpy as np
from jax import lax
from jax.sharding import PartitionSpec as P

D = 2048
HEAD_DIM = 128
TOP = 8
EXP_DEV = 1


def combined_all(shard, axis, join):
    gathered = jax.tree.map(
        lambda a, kind: lax.all_gather(a.astype(kind), axis),
        shard,
        (jnp.bfloat16, jnp.bfloat16, jnp.bfloat16),
    )

    def take(source):
        return jax.tree.map(
            lambda a, own: lax.dynamic_index_in_dim(a, source, 0, False).astype(own.dtype),
            gathered,
            shard,
        )

    return lax.fori_loop(
        1, lax.axis_size(axis), lambda source, state: join(state, take(source)), take(0)
    )


def expert_full(row_block, gate_part, up_part, down_part):
    gate_val = jnp.einsum(
        "sjkd,jdf->sjkf", row_block, gate_part, preferred_element_type=jnp.float32
    )
    up_val = jnp.einsum("sjkd,jdf->sjkf", row_block, up_part, preferred_element_type=jnp.float32)
    act = (jax.nn.silu(gate_val) * up_val).astype(jnp.bfloat16)
    return jnp.einsum("sjkf,jfd->sjkd", act, down_part, preferred_element_type=jnp.float32)


def full_weights(gate_w, up_w, down_w):
    kv_count = lax.axis_size("kv")
    if kv_count != 2:
        return (
            lax.all_gather(gate_w[0], "kv", axis=1, tiled=True),
            lax.all_gather(up_w[0], "kv", axis=1, tiled=True),
            lax.all_gather(down_w[0], "kv", axis=0, tiled=True),
        )
    hidden = gate_w.shape[2]
    packed = jnp.stack([gate_w[0], up_w[0], down_w[0].reshape(-1, hidden)])
    other = lax.ppermute(packed, "kv", [(0, 1), (1, 0)])
    first = lax.axis_index("kv") == 0
    joined = []
    for slot, axis in zip(range(3), (1, 1, 0)):
        own, far = packed[slot], other[slot]
        if axis == 0:
            own, far = own.reshape(hidden, -1), far.reshape(hidden, -1)
        low = jnp.where(first, own, far)
        high = jnp.where(first, far, own)
        joined.append(jnp.concatenate([low, high], axis=axis))
    return tuple(joined)


def dense_moe(plan, normed, route_ids, route_weights, weight_parts, anchor):
    expert_count = EXP_DEV * lax.axis_size("ep")
    experts = jnp.arange(expert_count, dtype=jnp.int32)
    own_expert = lax.axis_index("ep")
    chosen = route_ids[:, :, None] == experts[None, None, :]
    weight_table = jnp.sum(jnp.where(chosen, route_weights[:, :, None], 0.0), axis=1)
    weight_parts, anchor = lax.optimization_barrier((weight_parts, anchor))
    full = list(full_weights(*weight_parts))

    def expert(rows, table):
        weights = jnp.sum(jnp.where(experts == own_expert, table, 0.0), axis=1)
        gate_val = jnp.dot(rows, full[0], preferred_element_type=jnp.float32)
        up_val = jnp.dot(rows, full[1], preferred_element_type=jnp.float32)
        act = (jax.nn.silu(gate_val) * up_val).astype(jnp.bfloat16)
        out_rows = jnp.dot(act, full[2], preferred_element_type=jnp.float32)
        out_rows = out_rows.astype(jnp.bfloat16).astype(jnp.float32)
        return out_rows * weights[:, None]

    pieces = [((normed, weight_table), None, None)]
    groups = []
    low = 0
    tie_at = next((n + 1 for n, (_, ends) in enumerate(plan) if ends), 0)
    for number, (pairs_list, ends) in enumerate(plan):
        grown = []
        for parent, (block, _, _) in enumerate(pieces):
            for pairs in pairs_list:
                grown.append((lax.ppermute(block, "ep", pairs), parent, pairs))
        if number == tie_at:
            tied = lax.optimization_barrier((tuple(full), [piece[0] for piece in grown]))
            full = list(tied[0])
            grown = [(block, parent, pairs) for block, (_, parent, pairs) in zip(tied[1], grown)]
        pieces = pieces + grown
        if ends:
            groups.append((low, len(pieces)))
            low = len(pieces)
    if low < len(pieces) or not groups:
        groups.append((low, len(pieces)))
    partial = [None] * len(pieces)
    size = normed.shape[0]
    for low, high in groups:
        rows = jnp.concatenate([pieces[i][0][0] for i in range(low, high)], axis=0)
        table = jnp.concatenate([pieces[i][0][1] for i in range(low, high)], axis=0)
        out = expert(rows, table)
        for offset, i in enumerate(range(low, high)):
            partial[i] = out[offset * size:(offset + 1) * size]
    for index in reversed(range(1, len(pieces))):
        _, parent, pairs = pieces[index]
        back = [(target, source) for source, target in pairs]
        sent = lax.ppermute(partial[index].astype(jnp.bfloat16), "ep", back)
        partial[parent] = partial[parent] + sent.astype(jnp.float32)
    return partial[0], anchor


def gather_plan(mesh, shapes):
    kv_count, ep_count = mesh.devices.shape
    rows = ep_count * shapes[0][1] // kv_count
    if EXP_DEV != 1 or shapes[12][0] != ep_count or rows > 4096:
        return None
    places = []
    for device in mesh.devices[0]:
        coords = getattr(device, "coords", None)
        core = getattr(device, "core_on_chip", None)
        if coords is None or core is None:
            return None
        places.append(tuple(coords) + (core,))
    width = len(places[0])
    values = [sorted({p[a] for p in places}) for a in range(width)]
    varying = [a for a in range(width) if len(values[a]) > 1]
    total = 1
    for a in varying:
        total *= len(values[a])
    if total != ep_count or len(set(places)) != ep_count:
        return None
    rank_of = {p: r for r, p in enumerate(places)}
    core_axis = width - 1
    order = sorted((a for a in varying if a != core_axis), key=lambda a: -len(values[a]))
    order += [a for a in varying if a == core_axis]
    plan = []
    for a in order:
        size = len(values[a])
        if size & (size - 1) == 0:
            steps = []
            span = size // 2
            while span:
                steps.append(("xor", span))
                span //= 2
        else:
            steps = [("shift", shift) for shift in range(1, size)]
            steps = [steps]
        for number, step in enumerate(steps):
            group = step if isinstance(step, list) else [step]
            stage = []
            for kind, amount in group:
                pairs = []
                for r, p in enumerate(places):
                    index = values[a].index(p[a])
                    moved = list(p)
                    moved[a] = values[a][index ^ amount if kind == "xor" else (index + amount) % size]
                    pairs.append((r, rank_of[tuple(moved)]))
                stage.append(pairs)
            plan.append((stage, number == len(steps) - 1))
    return plan


def shards(
    plan,
    resid,
    queries,
    new_keys,
    new_values,
    cache_keys,
    cache_values,
    cached_len,
    group_request,
    w_out,
    norm_gain,
    route_ids,
    route_weights,
    gate_w,
    up_w,
    down_w,
):
    kv_rank = lax.axis_index("kv")
    ep_count = lax.axis_size("ep")
    tok_dev = resid.shape[1]
    cl_dev = cache_keys.shape[1]
    feat = queries.shape[2]
    head_count = feat // HEAD_DIM
    score_scale = 1.0 / math.sqrt(HEAD_DIM)
    request_index = jnp.arange(cached_len.shape[0], dtype=jnp.int32)
    length = jnp.sum(jnp.where(request_index == group_request[0], cached_len, 0))
    every_query = lax.all_gather(queries[0], "kv", axis=0, tiled=True)
    new_total = every_query.shape[0]
    query_heads = every_query.reshape(new_total, head_count, HEAD_DIM)
    key_cache = cache_keys[0].reshape(cl_dev, head_count, HEAD_DIM)
    value_cache = cache_values[0].reshape(cl_dev, head_count, HEAD_DIM)
    key_new = new_keys[0].reshape(tok_dev, head_count, HEAD_DIM)
    value_new = new_values[0].reshape(tok_dev, head_count, HEAD_DIM)
    score_cache = (
        jnp.einsum("qhd,khd->qhk", query_heads, key_cache, preferred_element_type=jnp.float32)
        * score_scale
    )
    position = kv_rank * cl_dev + jnp.arange(cl_dev, dtype=jnp.int32)
    score_cache = jnp.where((position < length)[None, None, :], score_cache, -jnp.inf)
    score_new = (
        jnp.einsum("qhd,khd->qhk", query_heads, key_new, preferred_element_type=jnp.float32)
        * score_scale
    )
    local_top = jnp.maximum(jnp.max(score_cache, axis=-1), jnp.max(score_new, axis=-1))
    expo_cache = jnp.exp(score_cache - local_top[..., None])
    expo_new = jnp.exp(score_new - local_top[..., None])
    denom = jnp.sum(expo_cache, axis=-1) + jnp.sum(expo_new, axis=-1)
    summed = jnp.einsum(
        "qhk,khd->qhd",
        expo_cache.astype(jnp.bfloat16),
        value_cache,
        preferred_element_type=jnp.float32,
    )
    summed = summed + jnp.einsum(
        "qhk,khd->qhd", expo_new.astype(jnp.bfloat16), value_new, preferred_element_type=jnp.float32
    )
    summed, denom = (summed.reshape(new_total, feat), denom)

    def join(first, second):
        first_top, first_denom, first_sum = first
        second_top, second_denom, second_sum = second
        joint_top = jnp.maximum(first_top, second_top)
        first_factor = jnp.exp(first_top - joint_top)
        second_factor = jnp.exp(second_top - joint_top)
        rows_here = first_sum.shape[0]
        joint_sum = (
            first_sum.reshape(rows_here, head_count, HEAD_DIM) * first_factor[..., None]
            + second_sum.reshape(rows_here, head_count, HEAD_DIM) * second_factor[..., None]
        )
        return (
            joint_top,
            first_denom * first_factor + second_denom * second_factor,
            joint_sum.reshape(rows_here, feat),
        )

    joint_top, joint_denom, joint_sum = combined_all((local_top, denom, summed), "kv", join)
    row_start = kv_rank * tok_dev
    own_sum = lax.dynamic_slice_in_dim(joint_sum, row_start, tok_dev, 0)
    own_denom = lax.dynamic_slice_in_dim(joint_denom, row_start, tok_dev, 0)
    attended = (
        (own_sum.reshape(tok_dev, head_count, HEAD_DIM) / own_denom[..., None])
        .reshape(tok_dev, feat)
        .astype(jnp.bfloat16)
    )
    proj = jnp.dot(attended, w_out, preferred_element_type=jnp.float32)
    hidden = (resid[0].astype(jnp.float32) + proj).astype(jnp.bfloat16)
    hidden_f = hidden.astype(jnp.float32)
    normed = (
        hidden_f
        * lax.rsqrt(jnp.mean(hidden_f * hidden_f, axis=-1, keepdims=True) + 1e-06)
        * norm_gain.astype(jnp.float32)
    ).astype(jnp.bfloat16)
    if plan is not None:
        moe_sum, _ = dense_moe(
            plan, normed, route_ids[0], route_weights[0], (gate_w, up_w, down_w), joint_denom
        )
        return (hidden_f + moe_sum).astype(jnp.bfloat16)[None]
    expert_count = EXP_DEV * ep_count
    capacity = min(tok_dev, max(2, tok_dev * TOP * 3 // (2 * expert_count)))
    route_flat = route_ids[0].reshape(-1)
    one_hot = (route_flat[:, None] == jnp.arange(expert_count, dtype=jnp.int32)[None, :]).astype(
        jnp.int32
    )
    rank_in = jnp.sum((jnp.cumsum(one_hot, axis=0) - 1) * one_hot, axis=1)
    slot_of = route_flat * capacity + rank_in
    slot_index = jnp.arange(expert_count * capacity, dtype=jnp.int32)
    placing = jnp.sum(
        (slot_of.reshape(tok_dev, TOP)[None, :, :] == slot_index[:, None, None]).astype(jnp.int32),
        axis=-1,
    ).astype(jnp.bfloat16)
    outgoing = jnp.dot(placing, normed, preferred_element_type=jnp.float32).astype(jnp.bfloat16)
    outgoing = outgoing.reshape(ep_count, EXP_DEV, capacity, D)
    full_gate, full_up, full_down = (
        lax.all_gather(gate_w, "kv", axis=2, tiled=True),
        lax.all_gather(up_w, "kv", axis=2, tiled=True),
        lax.all_gather(down_w, "kv", axis=1, tiled=True),
    )
    expert_out = expert_full(
        lax.all_to_all(outgoing, "ep", split_axis=0, concat_axis=0, tiled=True),
        full_gate,
        full_up,
        full_down,
    ).astype(jnp.bfloat16)
    returned = lax.all_to_all(expert_out, "ep", split_axis=0, concat_axis=0, tiled=True).reshape(
        expert_count * capacity, D
    )
    picked = jnp.take(returned, slot_of, axis=0).reshape(tok_dev, TOP, D)
    moe_sum = jnp.sum(picked.astype(jnp.float32) * route_weights[0][..., None], axis=1)
    return (hidden_f + moe_sum).astype(jnp.bfloat16)[None]


def solution(mesh):
    placed = (
        P("ep", "kv", None),
        P("ep", "kv", None),
        P("ep", "kv", None),
        P("ep", "kv", None),
        P("ep", "kv", None),
        P("ep", "kv", None),
        P(),
        P("ep"),
        P(),
        P(),
        P("ep", "kv", None),
        P("ep", "kv", None),
        P("ep", None, "kv"),
        P("ep", None, "kv"),
        P("ep", "kv", None),
    )

    def run(*args):
        plan = gather_plan(mesh, [a.shape for a in args])
        body = functools.partial(shards, plan)
        return jax.shard_map(
            body, mesh=mesh, in_specs=placed, out_specs=P("ep", "kv", None), check_vma=False
        )(*args)

    return run
```

```python
import functools
import math

import jax
import jax.numpy as jnp
import numpy as np
from jax import lax
from jax.sharding import PartitionSpec as P

D = 2048
HEAD_DIM = 128
TOP = 8
EXP_DEV = 1


def combined_all(shard, axis, join):
    gathered = jax.tree.map(
        lambda a, kind: lax.all_gather(a.astype(kind), axis),
        shard,
        (jnp.bfloat16, jnp.bfloat16, jnp.bfloat16),
    )

    def take(source):
        return jax.tree.map(
            lambda a, own: lax.dynamic_index_in_dim(a, source, 0, False).astype(own.dtype),
            gathered,
            shard,
        )

    return lax.fori_loop(
        1, lax.axis_size(axis), lambda source, state: join(state, take(source)), take(0)
    )


def expert_full(row_block, gate_part, up_part, down_part):
    gate_val = jnp.einsum(
        "sjkd,jdf->sjkf", row_block, gate_part, preferred_element_type=jnp.float32
    )
    up_val = jnp.einsum("sjkd,jdf->sjkf", row_block, up_part, preferred_element_type=jnp.float32)
    act = (jax.nn.silu(gate_val) * up_val).astype(jnp.bfloat16)
    return jnp.einsum("sjkf,jfd->sjkd", act, down_part, preferred_element_type=jnp.float32)


def full_weights(gate_w, up_w, down_w):
    kv_count = lax.axis_size("kv")
    if kv_count != 2:
        return (
            lax.all_gather(gate_w[0], "kv", axis=1, tiled=True),
            lax.all_gather(up_w[0], "kv", axis=1, tiled=True),
            lax.all_gather(down_w[0], "kv", axis=0, tiled=True),
        )
    hidden = gate_w.shape[2]
    packed = jnp.stack([gate_w[0], up_w[0], down_w[0].reshape(-1, hidden)])
    other = lax.ppermute(packed, "kv", [(0, 1), (1, 0)])
    first = lax.axis_index("kv") == 0
    joined = []
    for slot, axis in zip(range(3), (1, 1, 0)):
        own, far = packed[slot], other[slot]
        if axis == 0:
            own, far = own.reshape(hidden, -1), far.reshape(hidden, -1)
        low = jnp.where(first, own, far)
        high = jnp.where(first, far, own)
        joined.append(jnp.concatenate([low, high], axis=axis))
    return tuple(joined)


def dense_moe(plan, normed, route_ids, route_weights, weight_parts, anchor):
    expert_count = EXP_DEV * lax.axis_size("ep")
    experts = jnp.arange(expert_count, dtype=jnp.int32)
    own_expert = lax.axis_index("ep")
    chosen = route_ids[:, :, None] == experts[None, None, :]
    weight_table = jnp.sum(jnp.where(chosen, route_weights[:, :, None], 0.0), axis=1)
    weight_parts, anchor = lax.optimization_barrier((weight_parts, anchor))
    full = list(full_weights(*weight_parts))

    def expert(rows, table):
        weights = jnp.sum(jnp.where(experts == own_expert, table, 0.0), axis=1)
        gate_val = jnp.dot(rows, full[0], preferred_element_type=jnp.float32)
        up_val = jnp.dot(rows, full[1], preferred_element_type=jnp.float32)
        act = (jax.nn.silu(gate_val) * up_val).astype(jnp.bfloat16)
        out_rows = jnp.dot(act, full[2], preferred_element_type=jnp.float32)
        out_rows = out_rows.astype(jnp.bfloat16).astype(jnp.float32)
        return out_rows * weights[:, None]

    pieces = [((normed, weight_table), None, None)]
    groups = []
    low = 0
    tie_at = next((n + 1 for n, (_, ends) in enumerate(plan) if ends), 0)
    for number, (pairs_list, ends) in enumerate(plan):
        grown = []
        for parent, (block, _, _) in enumerate(pieces):
            for pairs in pairs_list:
                grown.append((lax.ppermute(block, "ep", pairs), parent, pairs))
        if number == tie_at:
            tied = lax.optimization_barrier((tuple(full), [piece[0] for piece in grown]))
            full = list(tied[0])
            grown = [(block, parent, pairs) for block, (_, parent, pairs) in zip(tied[1], grown)]
        pieces = pieces + grown
        if ends:
            groups.append((low, len(pieces)))
            low = len(pieces)
    if low < len(pieces) or not groups:
        groups.append((low, len(pieces)))
    partial = [None] * len(pieces)
    size = normed.shape[0]
    for low, high in groups:
        rows = jnp.concatenate([pieces[i][0][0] for i in range(low, high)], axis=0)
        table = jnp.concatenate([pieces[i][0][1] for i in range(low, high)], axis=0)
        out = expert(rows, table)
        for offset, i in enumerate(range(low, high)):
            partial[i] = out[offset * size:(offset + 1) * size]
    for index in reversed(range(1, len(pieces))):
        _, parent, pairs = pieces[index]
        back = [(target, source) for source, target in pairs]
        sent = lax.ppermute(partial[index].astype(jnp.bfloat16), "ep", back)
        partial[parent] = partial[parent] + sent.astype(jnp.float32)
    return partial[0], anchor


def gather_plan(mesh, shapes):
    kv_count, ep_count = mesh.devices.shape
    rows = ep_count * shapes[0][1] // kv_count
    if EXP_DEV != 1 or shapes[12][0] != ep_count or rows > 4096:
        return None
    places = []
    for device in mesh.devices[0]:
        coords = getattr(device, "coords", None)
        core = getattr(device, "core_on_chip", None)
        if coords is None or core is None:
            return None
        places.append(tuple(coords) + (core,))
    width = len(places[0])
    values = [sorted({p[a] for p in places}) for a in range(width)]
    varying = [a for a in range(width) if len(values[a]) > 1]
    total = 1
    for a in varying:
        total *= len(values[a])
    if total != ep_count or len(set(places)) != ep_count:
        return None
    rank_of = {p: r for r, p in enumerate(places)}
    core_axis = width - 1
    order = sorted((a for a in varying if a != core_axis), key=lambda a: -len(values[a]))
    order += [a for a in varying if a == core_axis]
    plan = []
    for a in order:
        size = len(values[a])
        if size & (size - 1) == 0:
            steps = []
            span = size // 2
            while span:
                steps.append(("xor", span))
                span //= 2
        else:
            steps = [("shift", shift) for shift in range(1, size)]
            steps = [steps]
        for number, step in enumerate(steps):
            group = step if isinstance(step, list) else [step]
            stage = []
            for kind, amount in group:
                pairs = []
                for r, p in enumerate(places):
                    index = values[a].index(p[a])
                    moved = list(p)
                    moved[a] = values[a][index ^ amount if kind == "xor" else (index + amount) % size]
                    pairs.append((r, rank_of[tuple(moved)]))
                stage.append(pairs)
            plan.append((stage, number == len(steps) - 1))
    return plan


def joined_attention(queries, new_keys, new_values, cache_keys, cache_values, length):
    kv_rank = lax.axis_index("kv")
    tok_dev = queries.shape[1]
    cl_dev = cache_keys.shape[1]
    feat = queries.shape[2]
    head_count = feat // HEAD_DIM
    score_scale = 1.0 / math.sqrt(HEAD_DIM)
    every_query = lax.all_gather(queries[0], "kv", axis=0, tiled=True)
    new_total = every_query.shape[0]
    query_heads = every_query.reshape(new_total, head_count, HEAD_DIM)
    key_cache = cache_keys[0].reshape(cl_dev, head_count, HEAD_DIM)
    value_cache = cache_values[0].reshape(cl_dev, head_count, HEAD_DIM)
    key_new = new_keys[0].reshape(tok_dev, head_count, HEAD_DIM)
    value_new = new_values[0].reshape(tok_dev, head_count, HEAD_DIM)
    score_cache = (
        jnp.einsum("qhd,khd->qhk", query_heads, key_cache, preferred_element_type=jnp.float32)
        * score_scale
    )
    position = kv_rank * cl_dev + jnp.arange(cl_dev, dtype=jnp.int32)
    score_cache = jnp.where((position < length)[None, None, :], score_cache, -jnp.inf)
    score_new = (
        jnp.einsum("qhd,khd->qhk", query_heads, key_new, preferred_element_type=jnp.float32)
        * score_scale
    )
    local_top = jnp.maximum(jnp.max(score_cache, axis=-1), jnp.max(score_new, axis=-1))
    expo_cache = jnp.exp(score_cache - local_top[..., None])
    expo_new = jnp.exp(score_new - local_top[..., None])
    denom = jnp.sum(expo_cache, axis=-1) + jnp.sum(expo_new, axis=-1)
    summed = jnp.einsum(
        "qhk,khd->qhd",
        expo_cache.astype(jnp.bfloat16),
        value_cache,
        preferred_element_type=jnp.float32,
    )
    summed = summed + jnp.einsum(
        "qhk,khd->qhd", expo_new.astype(jnp.bfloat16), value_new, preferred_element_type=jnp.float32
    )
    summed, denom = (summed.reshape(new_total, feat), denom)

    def join(first, second):
        first_top, first_denom, first_sum = first
        second_top, second_denom, second_sum = second
        joint_top = jnp.maximum(first_top, second_top)
        first_factor = jnp.exp(first_top - joint_top)
        second_factor = jnp.exp(second_top - joint_top)
        rows_here = first_sum.shape[0]
        joint_sum = (
            first_sum.reshape(rows_here, head_count, HEAD_DIM) * first_factor[..., None]
            + second_sum.reshape(rows_here, head_count, HEAD_DIM) * second_factor[..., None]
        )
        return (
            joint_top,
            first_denom * first_factor + second_denom * second_factor,
            joint_sum.reshape(rows_here, feat),
        )

    joint_top, joint_denom, joint_sum = combined_all((local_top, denom, summed), "kv", join)
    row_start = kv_rank * tok_dev
    own_sum = lax.dynamic_slice_in_dim(joint_sum, row_start, tok_dev, 0)
    own_denom = lax.dynamic_slice_in_dim(joint_denom, row_start, tok_dev, 0)
    attended = (
        (own_sum.reshape(tok_dev, head_count, HEAD_DIM) / own_denom[..., None])
        .reshape(tok_dev, feat)
        .astype(jnp.bfloat16)
    )
    return attended


def partial_softmax(query_rows, key_cache, value_cache, key_new, value_new, usable):
    rows, feat = query_rows.shape
    head_count = feat // HEAD_DIM
    score_scale = 1.0 / math.sqrt(HEAD_DIM)
    query_heads = query_rows.reshape(rows, head_count, HEAD_DIM)
    score_cache = (
        jnp.einsum("qhd,khd->qhk", query_heads, key_cache, preferred_element_type=jnp.float32)
        * score_scale
    )
    score_cache = jnp.where(usable[None, None, :], score_cache, -jnp.inf)
    score_new = (
        jnp.einsum("qhd,khd->qhk", query_heads, key_new, preferred_element_type=jnp.float32)
        * score_scale
    )
    top = jnp.maximum(jnp.max(score_cache, axis=-1), jnp.max(score_new, axis=-1))
    expo_cache = jnp.exp(score_cache - top[..., None])
    expo_new = jnp.exp(score_new - top[..., None])
    denom = jnp.sum(expo_cache, axis=-1) + jnp.sum(expo_new, axis=-1)
    summed = jnp.einsum(
        "qhk,khd->qhd", expo_cache.astype(jnp.bfloat16), value_cache,
        preferred_element_type=jnp.float32,
    )
    summed = summed + jnp.einsum(
        "qhk,khd->qhd", expo_new.astype(jnp.bfloat16), value_new, preferred_element_type=jnp.float32
    )
    return top, denom, summed


def paired_attention(own_queries, key_new, value_new, key_cache, value_cache, length):
    kv_rank = lax.axis_index("kv")
    swap = [(0, 1), (1, 0)]
    tok_dev, feat = own_queries.shape
    cl_dev = key_cache.shape[0]
    head_count = feat // HEAD_DIM
    far_queries = lax.ppermute(own_queries, "kv", swap)
    key_cache = key_cache.reshape(cl_dev, head_count, HEAD_DIM)
    value_cache = value_cache.reshape(cl_dev, head_count, HEAD_DIM)
    key_new = key_new.reshape(tok_dev, head_count, HEAD_DIM)
    value_new = value_new.reshape(tok_dev, head_count, HEAD_DIM)
    position = kv_rank * cl_dev + jnp.arange(cl_dev, dtype=jnp.int32)
    usable = position < length
    operands = (key_cache, value_cache, key_new, value_new, usable)
    own_top, own_denom, own_sum = partial_softmax(own_queries, *operands)
    far_top, far_denom, far_sum = partial_softmax(far_queries, *operands)
    back_top, back_denom, back_sum = lax.ppermute(
        (far_top, far_denom, far_sum.astype(jnp.bfloat16)), "kv", swap
    )
    joint_top = jnp.maximum(own_top, back_top)
    own_factor = jnp.exp(own_top - joint_top)
    back_factor = jnp.exp(back_top - joint_top)
    joint_sum = own_sum * own_factor[..., None] + back_sum.astype(jnp.float32) * back_factor[..., None]
    joint_denom = own_denom * own_factor + back_denom * back_factor
    return (joint_sum / joint_denom[..., None]).reshape(tok_dev, feat).astype(jnp.bfloat16)


def shards(
    plan,
    resid,
    queries,
    new_keys,
    new_values,
    cache_keys,
    cache_values,
    cached_len,
    group_request,
    w_out,
    norm_gain,
    route_ids,
    route_weights,
    gate_w,
    up_w,
    down_w,
):
    kv_rank = lax.axis_index("kv")
    ep_count = lax.axis_size("ep")
    tok_dev = resid.shape[1]
    cl_dev = cache_keys.shape[1]
    feat = queries.shape[2]
    head_count = feat // HEAD_DIM
    score_scale = 1.0 / math.sqrt(HEAD_DIM)
    request_index = jnp.arange(cached_len.shape[0], dtype=jnp.int32)
    length = jnp.sum(jnp.where(request_index == group_request[0], cached_len, 0))
    if lax.axis_size("kv") == 2 and plan is not None:
        attended = paired_attention(
            queries[0], new_keys[0], new_values[0], cache_keys[0], cache_values[0], length
        )
    else:
        attended = joined_attention(
            queries, new_keys, new_values, cache_keys, cache_values, length
        )
    proj = jnp.dot(attended, w_out, preferred_element_type=jnp.float32)
    hidden = (resid[0].astype(jnp.float32) + proj).astype(jnp.bfloat16)
    hidden_f = hidden.astype(jnp.float32)
    normed = (
        hidden_f
        * lax.rsqrt(jnp.mean(hidden_f * hidden_f, axis=-1, keepdims=True) + 1e-06)
        * norm_gain.astype(jnp.float32)
    ).astype(jnp.bfloat16)
    if plan is not None:
        moe_sum, _ = dense_moe(
            plan, normed, route_ids[0], route_weights[0], (gate_w, up_w, down_w), attended
        )
        return (hidden_f + moe_sum).astype(jnp.bfloat16)[None]
    expert_count = EXP_DEV * ep_count
    capacity = min(tok_dev, max(2, tok_dev * TOP * 3 // (2 * expert_count)))
    route_flat = route_ids[0].reshape(-1)
    one_hot = (route_flat[:, None] == jnp.arange(expert_count, dtype=jnp.int32)[None, :]).astype(
        jnp.int32
    )
    rank_in = jnp.sum((jnp.cumsum(one_hot, axis=0) - 1) * one_hot, axis=1)
    slot_of = route_flat * capacity + rank_in
    slot_index = jnp.arange(expert_count * capacity, dtype=jnp.int32)
    placing = jnp.sum(
        (slot_of.reshape(tok_dev, TOP)[None, :, :] == slot_index[:, None, None]).astype(jnp.int32),
        axis=-1,
    ).astype(jnp.bfloat16)
    outgoing = jnp.dot(placing, normed, preferred_element_type=jnp.float32).astype(jnp.bfloat16)
    outgoing = outgoing.reshape(ep_count, EXP_DEV, capacity, D)
    full_gate, full_up, full_down = (
        lax.all_gather(gate_w, "kv", axis=2, tiled=True),
        lax.all_gather(up_w, "kv", axis=2, tiled=True),
        lax.all_gather(down_w, "kv", axis=1, tiled=True),
    )
    expert_out = expert_full(
        lax.all_to_all(outgoing, "ep", split_axis=0, concat_axis=0, tiled=True),
        full_gate,
        full_up,
        full_down,
    ).astype(jnp.bfloat16)
    returned = lax.all_to_all(expert_out, "ep", split_axis=0, concat_axis=0, tiled=True).reshape(
        expert_count * capacity, D
    )
    picked = jnp.take(returned, slot_of, axis=0).reshape(tok_dev, TOP, D)
    moe_sum = jnp.sum(picked.astype(jnp.float32) * route_weights[0][..., None], axis=1)
    return (hidden_f + moe_sum).astype(jnp.bfloat16)[None]


def solution(mesh):
    placed = (
        P("ep", "kv", None),
        P("ep", "kv", None),
        P("ep", "kv", None),
        P("ep", "kv", None),
        P("ep", "kv", None),
        P("ep", "kv", None),
        P(),
        P("ep"),
        P(),
        P(),
        P("ep", "kv", None),
        P("ep", "kv", None),
        P("ep", None, "kv"),
        P("ep", None, "kv"),
        P("ep", "kv", None),
    )

    def run(*args):
        plan = gather_plan(mesh, [a.shape for a in args])
        body = functools.partial(shards, plan)
        return jax.shard_map(
            body, mesh=mesh, in_specs=placed, out_specs=P("ep", "kv", None), check_vma=False
        )(*args)

    return run
```

```python
import functools
import math

import jax
import jax.numpy as jnp
import numpy as np
from jax import lax
from jax.sharding import PartitionSpec as P

D = 2048
HEAD_DIM = 128
TOP = 8
EXP_DEV = 1


def combined_all(shard, axis, join):
    gathered = jax.tree.map(
        lambda a, kind: lax.all_gather(a.astype(kind), axis),
        shard,
        (jnp.bfloat16, jnp.bfloat16, jnp.bfloat16),
    )

    def take(source):
        return jax.tree.map(
            lambda a, own: lax.dynamic_index_in_dim(a, source, 0, False).astype(own.dtype),
            gathered,
            shard,
        )

    return lax.fori_loop(
        1, lax.axis_size(axis), lambda source, state: join(state, take(source)), take(0)
    )


def expert_full(row_block, gate_part, up_part, down_part):
    gate_val = jnp.einsum(
        "sjkd,jdf->sjkf", row_block, gate_part, preferred_element_type=jnp.float32
    )
    up_val = jnp.einsum("sjkd,jdf->sjkf", row_block, up_part, preferred_element_type=jnp.float32)
    act = (jax.nn.silu(gate_val) * up_val).astype(jnp.bfloat16)
    return jnp.einsum("sjkf,jfd->sjkd", act, down_part, preferred_element_type=jnp.float32)


def full_weights(gate_w, up_w, down_w):
    kv_count = lax.axis_size("kv")
    if kv_count != 2:
        return (
            lax.all_gather(gate_w[0], "kv", axis=1, tiled=True),
            lax.all_gather(up_w[0], "kv", axis=1, tiled=True),
            lax.all_gather(down_w[0], "kv", axis=0, tiled=True),
        )
    hidden = gate_w.shape[2]
    packed = jnp.stack([gate_w[0], up_w[0], down_w[0].reshape(-1, hidden)])
    other = lax.ppermute(packed, "kv", [(0, 1), (1, 0)])
    first = lax.axis_index("kv") == 0
    joined = []
    for slot, axis in zip(range(3), (1, 1, 0)):
        own, far = packed[slot], other[slot]
        if axis == 0:
            own, far = own.reshape(hidden, -1), far.reshape(hidden, -1)
        low = jnp.where(first, own, far)
        high = jnp.where(first, far, own)
        joined.append(jnp.concatenate([low, high], axis=axis))
    return tuple(joined)


def dense_moe(plan, normed, route_ids, route_weights, weight_parts, anchor):
    expert_count = EXP_DEV * lax.axis_size("ep")
    experts = jnp.arange(expert_count, dtype=jnp.int32)
    own_expert = lax.axis_index("ep")
    chosen = route_ids[:, :, None] == experts[None, None, :]
    weight_table = jnp.sum(jnp.where(chosen, route_weights[:, :, None], 0.0), axis=1)
    weight_parts, anchor = lax.optimization_barrier((weight_parts, anchor))
    full = list(full_weights(*weight_parts))

    def expert(rows, table):
        weights = jnp.sum(jnp.where(experts == own_expert, table, 0.0), axis=1)
        gate_val = jnp.dot(rows, full[0], preferred_element_type=jnp.float32)
        up_val = jnp.dot(rows, full[1], preferred_element_type=jnp.float32)
        act = (jax.nn.silu(gate_val) * up_val).astype(jnp.bfloat16)
        out_rows = jnp.dot(act, full[2], preferred_element_type=jnp.float32)
        out_rows = out_rows.astype(jnp.bfloat16).astype(jnp.float32)
        return out_rows * weights[:, None]

    pieces = [((normed, weight_table), None, None, -1)]
    waves = [[0]]
    tie_at = min(2, len(plan) - 1)
    while True:
        fresh = []
        for parent in waves[-1]:
            block, _, _, last = pieces[parent]
            for stage in range(last + 1, len(plan)):
                for pairs in plan[stage][0]:
                    fresh.append((lax.ppermute(block, "ep", pairs), parent, pairs, stage))
        if not fresh:
            break
        blocks = [piece[0] for piece in fresh]
        if len(waves) == tie_at + 1:
            full, blocks = lax.optimization_barrier((tuple(full), blocks))
            full = list(full)
        else:
            blocks = lax.optimization_barrier(blocks)
        waves.append(list(range(len(pieces), len(pieces) + len(fresh))))
        pieces += [(b,) + piece[1:] for b, piece in zip(blocks, fresh)]
    partial = [None] * len(pieces)
    size = normed.shape[0]
    groups = [[0] + waves[1]] + waves[2:] if len(waves) > 1 else [[0]]
    for group in groups:
        rows = jnp.concatenate([pieces[i][0][0] for i in group], axis=0)
        table = jnp.concatenate([pieces[i][0][1] for i in group], axis=0)
        out = expert(rows, table)
        for offset, i in enumerate(group):
            partial[i] = out[offset * size:(offset + 1) * size]
    for wave in reversed(waves[1:]):
        sent = []
        for index in wave:
            _, parent, pairs, _ = pieces[index]
            back = [(target, source) for source, target in pairs]
            sent.append(lax.ppermute(partial[index].astype(jnp.bfloat16), "ep", back))
        sent = lax.optimization_barrier(sent)
        for index, value in zip(wave, sent):
            parent = pieces[index][1]
            partial[parent] = partial[parent] + value.astype(jnp.float32)
    return partial[0], anchor


def gather_plan(mesh, shapes):
    kv_count, ep_count = mesh.devices.shape
    rows = ep_count * shapes[0][1] // kv_count
    if EXP_DEV != 1 or shapes[12][0] != ep_count or rows > 4096:
        return None
    places = []
    for device in mesh.devices[0]:
        coords = getattr(device, "coords", None)
        core = getattr(device, "core_on_chip", None)
        if coords is None or core is None:
            return None
        places.append(tuple(coords) + (core,))
    width = len(places[0])
    values = [sorted({p[a] for p in places}) for a in range(width)]
    varying = [a for a in range(width) if len(values[a]) > 1]
    total = 1
    for a in varying:
        total *= len(values[a])
    if total != ep_count or len(set(places)) != ep_count:
        return None
    rank_of = {p: r for r, p in enumerate(places)}
    core_axis = width - 1
    order = sorted((a for a in varying if a != core_axis), key=lambda a: -len(values[a]))
    order += [a for a in varying if a == core_axis]
    plan = []
    for a in order:
        size = len(values[a])
        if size & (size - 1) == 0:
            steps = []
            span = size // 2
            while span:
                steps.append(("xor", span))
                span //= 2
        else:
            steps = [("shift", shift) for shift in range(1, size)]
            steps = [steps]
        for number, step in enumerate(steps):
            group = step if isinstance(step, list) else [step]
            stage = []
            for kind, amount in group:
                pairs = []
                for r, p in enumerate(places):
                    index = values[a].index(p[a])
                    moved = list(p)
                    moved[a] = values[a][index ^ amount if kind == "xor" else (index + amount) % size]
                    pairs.append((r, rank_of[tuple(moved)]))
                stage.append(pairs)
            plan.append((stage, number == len(steps) - 1))
    return plan


def joined_attention(queries, new_keys, new_values, cache_keys, cache_values, length):
    kv_rank = lax.axis_index("kv")
    tok_dev = queries.shape[1]
    cl_dev = cache_keys.shape[1]
    feat = queries.shape[2]
    head_count = feat // HEAD_DIM
    score_scale = 1.0 / math.sqrt(HEAD_DIM)
    every_query = lax.all_gather(queries[0], "kv", axis=0, tiled=True)
    new_total = every_query.shape[0]
    query_heads = every_query.reshape(new_total, head_count, HEAD_DIM)
    key_cache = cache_keys[0].reshape(cl_dev, head_count, HEAD_DIM)
    value_cache = cache_values[0].reshape(cl_dev, head_count, HEAD_DIM)
    key_new = new_keys[0].reshape(tok_dev, head_count, HEAD_DIM)
    value_new = new_values[0].reshape(tok_dev, head_count, HEAD_DIM)
    score_cache = (
        jnp.einsum("qhd,khd->qhk", query_heads, key_cache, preferred_element_type=jnp.float32)
        * score_scale
    )
    position = kv_rank * cl_dev + jnp.arange(cl_dev, dtype=jnp.int32)
    score_cache = jnp.where((position < length)[None, None, :], score_cache, -jnp.inf)
    score_new = (
        jnp.einsum("qhd,khd->qhk", query_heads, key_new, preferred_element_type=jnp.float32)
        * score_scale
    )
    local_top = jnp.maximum(jnp.max(score_cache, axis=-1), jnp.max(score_new, axis=-1))
    expo_cache = jnp.exp(score_cache - local_top[..., None])
    expo_new = jnp.exp(score_new - local_top[..., None])
    denom = jnp.sum(expo_cache, axis=-1) + jnp.sum(expo_new, axis=-1)
    summed = jnp.einsum(
        "qhk,khd->qhd",
        expo_cache.astype(jnp.bfloat16),
        value_cache,
        preferred_element_type=jnp.float32,
    )
    summed = summed + jnp.einsum(
        "qhk,khd->qhd", expo_new.astype(jnp.bfloat16), value_new, preferred_element_type=jnp.float32
    )
    summed, denom = (summed.reshape(new_total, feat), denom)

    def join(first, second):
        first_top, first_denom, first_sum = first
        second_top, second_denom, second_sum = second
        joint_top = jnp.maximum(first_top, second_top)
        first_factor = jnp.exp(first_top - joint_top)
        second_factor = jnp.exp(second_top - joint_top)
        rows_here = first_sum.shape[0]
        joint_sum = (
            first_sum.reshape(rows_here, head_count, HEAD_DIM) * first_factor[..., None]
            + second_sum.reshape(rows_here, head_count, HEAD_DIM) * second_factor[..., None]
        )
        return (
            joint_top,
            first_denom * first_factor + second_denom * second_factor,
            joint_sum.reshape(rows_here, feat),
        )

    joint_top, joint_denom, joint_sum = combined_all((local_top, denom, summed), "kv", join)
    row_start = kv_rank * tok_dev
    own_sum = lax.dynamic_slice_in_dim(joint_sum, row_start, tok_dev, 0)
    own_denom = lax.dynamic_slice_in_dim(joint_denom, row_start, tok_dev, 0)
    attended = (
        (own_sum.reshape(tok_dev, head_count, HEAD_DIM) / own_denom[..., None])
        .reshape(tok_dev, feat)
        .astype(jnp.bfloat16)
    )
    return attended


def partial_softmax(query_rows, key_cache, value_cache, key_new, value_new, usable):
    rows, feat = query_rows.shape
    head_count = feat // HEAD_DIM
    score_scale = 1.0 / math.sqrt(HEAD_DIM)
    query_heads = query_rows.reshape(rows, head_count, HEAD_DIM)
    score_cache = (
        jnp.einsum("qhd,khd->qhk", query_heads, key_cache, preferred_element_type=jnp.float32)
        * score_scale
    )
    score_cache = jnp.where(usable[None, None, :], score_cache, -jnp.inf)
    score_new = (
        jnp.einsum("qhd,khd->qhk", query_heads, key_new, preferred_element_type=jnp.float32)
        * score_scale
    )
    top = jnp.maximum(jnp.max(score_cache, axis=-1), jnp.max(score_new, axis=-1))
    expo_cache = jnp.exp(score_cache - top[..., None])
    expo_new = jnp.exp(score_new - top[..., None])
    denom = jnp.sum(expo_cache, axis=-1) + jnp.sum(expo_new, axis=-1)
    summed = jnp.einsum(
        "qhk,khd->qhd", expo_cache.astype(jnp.bfloat16), value_cache,
        preferred_element_type=jnp.float32,
    )
    summed = summed + jnp.einsum(
        "qhk,khd->qhd", expo_new.astype(jnp.bfloat16), value_new, preferred_element_type=jnp.float32
    )
    return top, denom, summed


def paired_attention(own_queries, key_new, value_new, key_cache, value_cache, length):
    kv_rank = lax.axis_index("kv")
    swap = [(0, 1), (1, 0)]
    tok_dev, feat = own_queries.shape
    cl_dev = key_cache.shape[0]
    head_count = feat // HEAD_DIM
    far_queries = lax.ppermute(own_queries, "kv", swap)
    key_cache = key_cache.reshape(cl_dev, head_count, HEAD_DIM)
    value_cache = value_cache.reshape(cl_dev, head_count, HEAD_DIM)
    key_new = key_new.reshape(tok_dev, head_count, HEAD_DIM)
    value_new = value_new.reshape(tok_dev, head_count, HEAD_DIM)
    position = kv_rank * cl_dev + jnp.arange(cl_dev, dtype=jnp.int32)
    usable = position < length
    operands = (key_cache, value_cache, key_new, value_new, usable)
    own_top, own_denom, own_sum = partial_softmax(own_queries, *operands)
    far_top, far_denom, far_sum = partial_softmax(far_queries, *operands)
    back_top, back_denom, back_sum = lax.ppermute(
        (far_top, far_denom, far_sum.astype(jnp.bfloat16)), "kv", swap
    )
    joint_top = jnp.maximum(own_top, back_top)
    own_factor = jnp.exp(own_top - joint_top)
    back_factor = jnp.exp(back_top - joint_top)
    joint_sum = own_sum * own_factor[..., None] + back_sum.astype(jnp.float32) * back_factor[..., None]
    joint_denom = own_denom * own_factor + back_denom * back_factor
    return (joint_sum / joint_denom[..., None]).reshape(tok_dev, feat).astype(jnp.bfloat16)


def shards(
    plan,
    resid,
    queries,
    new_keys,
    new_values,
    cache_keys,
    cache_values,
    cached_len,
    group_request,
    w_out,
    norm_gain,
    route_ids,
    route_weights,
    gate_w,
    up_w,
    down_w,
):
    kv_rank = lax.axis_index("kv")
    ep_count = lax.axis_size("ep")
    tok_dev = resid.shape[1]
    cl_dev = cache_keys.shape[1]
    feat = queries.shape[2]
    head_count = feat // HEAD_DIM
    score_scale = 1.0 / math.sqrt(HEAD_DIM)
    request_index = jnp.arange(cached_len.shape[0], dtype=jnp.int32)
    length = jnp.sum(jnp.where(request_index == group_request[0], cached_len, 0))
    if lax.axis_size("kv") == 2 and plan is not None:
        attended = paired_attention(
            queries[0], new_keys[0], new_values[0], cache_keys[0], cache_values[0], length
        )
    else:
        attended = joined_attention(
            queries, new_keys, new_values, cache_keys, cache_values, length
        )
    proj = jnp.dot(attended, w_out, preferred_element_type=jnp.float32)
    hidden = (resid[0].astype(jnp.float32) + proj).astype(jnp.bfloat16)
    hidden_f = hidden.astype(jnp.float32)
    normed = (
        hidden_f
        * lax.rsqrt(jnp.mean(hidden_f * hidden_f, axis=-1, keepdims=True) + 1e-06)
        * norm_gain.astype(jnp.float32)
    ).astype(jnp.bfloat16)
    if plan is not None:
        moe_sum, _ = dense_moe(
            plan, normed, route_ids[0], route_weights[0], (gate_w, up_w, down_w), attended
        )
        return (hidden_f + moe_sum).astype(jnp.bfloat16)[None]
    expert_count = EXP_DEV * ep_count
    capacity = min(tok_dev, max(2, tok_dev * TOP * 3 // (2 * expert_count)))
    route_flat = route_ids[0].reshape(-1)
    one_hot = (route_flat[:, None] == jnp.arange(expert_count, dtype=jnp.int32)[None, :]).astype(
        jnp.int32
    )
    rank_in = jnp.sum((jnp.cumsum(one_hot, axis=0) - 1) * one_hot, axis=1)
    slot_of = route_flat * capacity + rank_in
    slot_index = jnp.arange(expert_count * capacity, dtype=jnp.int32)
    placing = jnp.sum(
        (slot_of.reshape(tok_dev, TOP)[None, :, :] == slot_index[:, None, None]).astype(jnp.int32),
        axis=-1,
    ).astype(jnp.bfloat16)
    outgoing = jnp.dot(placing, normed, preferred_element_type=jnp.float32).astype(jnp.bfloat16)
    outgoing = outgoing.reshape(ep_count, EXP_DEV, capacity, D)
    full_gate, full_up, full_down = (
        lax.all_gather(gate_w, "kv", axis=2, tiled=True),
        lax.all_gather(up_w, "kv", axis=2, tiled=True),
        lax.all_gather(down_w, "kv", axis=1, tiled=True),
    )
    expert_out = expert_full(
        lax.all_to_all(outgoing, "ep", split_axis=0, concat_axis=0, tiled=True),
        full_gate,
        full_up,
        full_down,
    ).astype(jnp.bfloat16)
    returned = lax.all_to_all(expert_out, "ep", split_axis=0, concat_axis=0, tiled=True).reshape(
        expert_count * capacity, D
    )
    picked = jnp.take(returned, slot_of, axis=0).reshape(tok_dev, TOP, D)
    moe_sum = jnp.sum(picked.astype(jnp.float32) * route_weights[0][..., None], axis=1)
    return (hidden_f + moe_sum).astype(jnp.bfloat16)[None]


def solution(mesh):
    placed = (
        P("ep", "kv", None),
        P("ep", "kv", None),
        P("ep", "kv", None),
        P("ep", "kv", None),
        P("ep", "kv", None),
        P("ep", "kv", None),
        P(),
        P("ep"),
        P(),
        P(),
        P("ep", "kv", None),
        P("ep", "kv", None),
        P("ep", None, "kv"),
        P("ep", None, "kv"),
        P("ep", "kv", None),
    )

    def run(*args):
        plan = gather_plan(mesh, [a.shape for a in args])
        body = functools.partial(shards, plan)
        return jax.shard_map(
            body, mesh=mesh, in_specs=placed, out_specs=P("ep", "kv", None), check_vma=False
        )(*args)

    return run
```

```python
import functools
import math

import jax
import jax.numpy as jnp
import numpy as np
from jax import lax
from jax.sharding import PartitionSpec as P

D = 2048
HEAD_DIM = 128
TOP = 8
EXP_DEV = 1


def combined_all(shard, axis, join):
    gathered = jax.tree.map(
        lambda a, kind: lax.all_gather(a.astype(kind), axis),
        shard,
        (jnp.bfloat16, jnp.bfloat16, jnp.bfloat16),
    )

    def take(source):
        return jax.tree.map(
            lambda a, own: lax.dynamic_index_in_dim(a, source, 0, False).astype(own.dtype),
            gathered,
            shard,
        )

    return lax.fori_loop(
        1, lax.axis_size(axis), lambda source, state: join(state, take(source)), take(0)
    )


def expert_full(row_block, gate_part, up_part, down_part):
    gate_val = jnp.einsum(
        "sjkd,jdf->sjkf", row_block, gate_part, preferred_element_type=jnp.float32
    )
    up_val = jnp.einsum("sjkd,jdf->sjkf", row_block, up_part, preferred_element_type=jnp.float32)
    act = (jax.nn.silu(gate_val) * up_val).astype(jnp.bfloat16)
    return jnp.einsum("sjkf,jfd->sjkd", act, down_part, preferred_element_type=jnp.float32)


def full_weights(gate_w, up_w, down_w):
    kv_count = lax.axis_size("kv")
    if kv_count != 2:
        return (
            lax.all_gather(gate_w[0], "kv", axis=1, tiled=True),
            lax.all_gather(up_w[0], "kv", axis=1, tiled=True),
            lax.all_gather(down_w[0], "kv", axis=0, tiled=True),
        )
    hidden = gate_w.shape[2]
    packed = jnp.stack([gate_w[0], up_w[0], down_w[0].reshape(-1, hidden)])
    other = lax.ppermute(packed, "kv", [(0, 1), (1, 0)])
    first = lax.axis_index("kv") == 0
    joined = []
    for slot, axis in zip(range(3), (1, 1, 0)):
        own, far = packed[slot], other[slot]
        if axis == 0:
            own, far = own.reshape(hidden, -1), far.reshape(hidden, -1)
        low = jnp.where(first, own, far)
        high = jnp.where(first, far, own)
        joined.append(jnp.concatenate([low, high], axis=axis))
    return tuple(joined)


def dense_moe(plan, normed, route_ids, route_weights, weight_parts, anchor):
    expert_count = EXP_DEV * lax.axis_size("ep")
    experts = jnp.arange(expert_count, dtype=jnp.int32)
    own_expert = lax.axis_index("ep")
    chosen = route_ids[:, :, None] == experts[None, None, :]
    weight_table = jnp.sum(jnp.where(chosen, route_weights[:, :, None], 0.0), axis=1)
    full = list(full_weights(*weight_parts))

    def expert(rows, table):
        weights = jnp.sum(jnp.where(experts == own_expert, table, 0.0), axis=1)
        gate_val = jnp.dot(rows, full[0], preferred_element_type=jnp.float32)
        up_val = jnp.dot(rows, full[1], preferred_element_type=jnp.float32)
        act = (jax.nn.silu(gate_val) * up_val).astype(jnp.bfloat16)
        out_rows = jnp.dot(act, full[2], preferred_element_type=jnp.float32)
        out_rows = out_rows.astype(jnp.bfloat16).astype(jnp.float32)
        return out_rows * weights[:, None]

    pieces = [((normed, weight_table), None, None, -1)]
    waves = [[0]]
    tie_at = min(1, len(plan) - 1)
    while True:
        fresh = []
        for parent in waves[-1]:
            block, _, _, last = pieces[parent]
            for stage in range(last + 1, len(plan)):
                for pairs in plan[stage][0]:
                    fresh.append((lax.ppermute(block, "ep", pairs), parent, pairs, stage))
        if not fresh:
            break
        blocks = [piece[0] for piece in fresh]
        if len(waves) == tie_at + 1:
            full, blocks = lax.optimization_barrier((tuple(full), blocks))
            full = list(full)
        else:
            blocks = lax.optimization_barrier(blocks)
        waves.append(list(range(len(pieces), len(pieces) + len(fresh))))
        pieces += [(b,) + piece[1:] for b, piece in zip(blocks, fresh)]
    partial = [None] * len(pieces)
    size = normed.shape[0]
    groups = [[0] + waves[1]] + waves[2:] if len(waves) > 1 else [[0]]
    for group in groups:
        rows = jnp.concatenate([pieces[i][0][0] for i in group], axis=0)
        table = jnp.concatenate([pieces[i][0][1] for i in group], axis=0)
        out = expert(rows, table)
        for offset, i in enumerate(group):
            partial[i] = out[offset * size:(offset + 1) * size]
    for wave in reversed(waves[1:]):
        sent = []
        for index in wave:
            _, parent, pairs, _ = pieces[index]
            back = [(target, source) for source, target in pairs]
            sent.append(lax.ppermute(partial[index].astype(jnp.bfloat16), "ep", back))
        sent = lax.optimization_barrier(sent)
        for index, value in zip(wave, sent):
            parent = pieces[index][1]
            partial[parent] = partial[parent] + value.astype(jnp.float32)
    return partial[0], anchor


def gather_plan(mesh, shapes):
    kv_count, ep_count = mesh.devices.shape
    rows = ep_count * shapes[0][1] // kv_count
    if EXP_DEV != 1 or shapes[12][0] != ep_count or rows > 4096:
        return None
    places = []
    for device in mesh.devices[0]:
        coords = getattr(device, "coords", None)
        core = getattr(device, "core_on_chip", None)
        if coords is None or core is None:
            return None
        places.append(tuple(coords) + (core,))
    width = len(places[0])
    values = [sorted({p[a] for p in places}) for a in range(width)]
    varying = [a for a in range(width) if len(values[a]) > 1]
    total = 1
    for a in varying:
        total *= len(values[a])
    if total != ep_count or len(set(places)) != ep_count:
        return None
    rank_of = {p: r for r, p in enumerate(places)}
    core_axis = width - 1
    order = sorted((a for a in varying if a != core_axis), key=lambda a: -len(values[a]))
    order += [a for a in varying if a == core_axis]
    plan = []
    for a in order:
        size = len(values[a])
        if size & (size - 1) == 0:
            steps = []
            span = size // 2
            while span:
                steps.append(("xor", span))
                span //= 2
        else:
            steps = [("shift", shift) for shift in range(1, size)]
            steps = [steps]
        for number, step in enumerate(steps):
            group = step if isinstance(step, list) else [step]
            stage = []
            for kind, amount in group:
                pairs = []
                for r, p in enumerate(places):
                    index = values[a].index(p[a])
                    moved = list(p)
                    moved[a] = values[a][index ^ amount if kind == "xor" else (index + amount) % size]
                    pairs.append((r, rank_of[tuple(moved)]))
                stage.append(pairs)
            plan.append((stage, number == len(steps) - 1))
    return plan


def joined_attention(queries, new_keys, new_values, cache_keys, cache_values, length):
    kv_rank = lax.axis_index("kv")
    tok_dev = queries.shape[1]
    cl_dev = cache_keys.shape[1]
    feat = queries.shape[2]
    head_count = feat // HEAD_DIM
    score_scale = 1.0 / math.sqrt(HEAD_DIM)
    every_query = lax.all_gather(queries[0], "kv", axis=0, tiled=True)
    new_total = every_query.shape[0]
    query_heads = every_query.reshape(new_total, head_count, HEAD_DIM)
    key_cache = cache_keys[0].reshape(cl_dev, head_count, HEAD_DIM)
    value_cache = cache_values[0].reshape(cl_dev, head_count, HEAD_DIM)
    key_new = new_keys[0].reshape(tok_dev, head_count, HEAD_DIM)
    value_new = new_values[0].reshape(tok_dev, head_count, HEAD_DIM)
    score_cache = (
        jnp.einsum("qhd,khd->qhk", query_heads, key_cache, preferred_element_type=jnp.float32)
        * score_scale
    )
    position = kv_rank * cl_dev + jnp.arange(cl_dev, dtype=jnp.int32)
    score_cache = jnp.where((position < length)[None, None, :], score_cache, -jnp.inf)
    score_new = (
        jnp.einsum("qhd,khd->qhk", query_heads, key_new, preferred_element_type=jnp.float32)
        * score_scale
    )
    local_top = jnp.maximum(jnp.max(score_cache, axis=-1), jnp.max(score_new, axis=-1))
    expo_cache = jnp.exp(score_cache - local_top[..., None])
    expo_new = jnp.exp(score_new - local_top[..., None])
    denom = jnp.sum(expo_cache, axis=-1) + jnp.sum(expo_new, axis=-1)
    summed = jnp.einsum(
        "qhk,khd->qhd",
        expo_cache.astype(jnp.bfloat16),
        value_cache,
        preferred_element_type=jnp.float32,
    )
    summed = summed + jnp.einsum(
        "qhk,khd->qhd", expo_new.astype(jnp.bfloat16), value_new, preferred_element_type=jnp.float32
    )
    summed, denom = (summed.reshape(new_total, feat), denom)

    def join(first, second):
        first_top, first_denom, first_sum = first
        second_top, second_denom, second_sum = second
        joint_top = jnp.maximum(first_top, second_top)
        first_factor = jnp.exp(first_top - joint_top)
        second_factor = jnp.exp(second_top - joint_top)
        rows_here = first_sum.shape[0]
        joint_sum = (
            first_sum.reshape(rows_here, head_count, HEAD_DIM) * first_factor[..., None]
            + second_sum.reshape(rows_here, head_count, HEAD_DIM) * second_factor[..., None]
        )
        return (
            joint_top,
            first_denom * first_factor + second_denom * second_factor,
            joint_sum.reshape(rows_here, feat),
        )

    joint_top, joint_denom, joint_sum = combined_all((local_top, denom, summed), "kv", join)
    row_start = kv_rank * tok_dev
    own_sum = lax.dynamic_slice_in_dim(joint_sum, row_start, tok_dev, 0)
    own_denom = lax.dynamic_slice_in_dim(joint_denom, row_start, tok_dev, 0)
    attended = (
        (own_sum.reshape(tok_dev, head_count, HEAD_DIM) / own_denom[..., None])
        .reshape(tok_dev, feat)
        .astype(jnp.bfloat16)
    )
    return attended


def partial_softmax(query_rows, key_cache, value_cache, key_new, value_new, usable):
    rows, feat = query_rows.shape
    head_count = feat // HEAD_DIM
    score_scale = 1.0 / math.sqrt(HEAD_DIM)
    query_heads = query_rows.reshape(rows, head_count, HEAD_DIM)
    score_cache = (
        jnp.einsum("qhd,khd->qhk", query_heads, key_cache, preferred_element_type=jnp.float32)
        * score_scale
    )
    score_cache = jnp.where(usable[None, None, :], score_cache, -jnp.inf)
    score_new = (
        jnp.einsum("qhd,khd->qhk", query_heads, key_new, preferred_element_type=jnp.float32)
        * score_scale
    )
    top = jnp.maximum(jnp.max(score_cache, axis=-1), jnp.max(score_new, axis=-1))
    expo_cache = jnp.exp(score_cache - top[..., None])
    expo_new = jnp.exp(score_new - top[..., None])
    denom = jnp.sum(expo_cache, axis=-1) + jnp.sum(expo_new, axis=-1)
    summed = jnp.einsum(
        "qhk,khd->qhd", expo_cache.astype(jnp.bfloat16), value_cache,
        preferred_element_type=jnp.float32,
    )
    summed = summed + jnp.einsum(
        "qhk,khd->qhd", expo_new.astype(jnp.bfloat16), value_new, preferred_element_type=jnp.float32
    )
    return top, denom, summed


def paired_attention(own_queries, key_new, value_new, key_cache, value_cache, length):
    kv_rank = lax.axis_index("kv")
    swap = [(0, 1), (1, 0)]
    tok_dev, feat = own_queries.shape
    cl_dev = key_cache.shape[0]
    head_count = feat // HEAD_DIM
    far_queries = lax.ppermute(own_queries, "kv", swap)
    key_cache = key_cache.reshape(cl_dev, head_count, HEAD_DIM)
    value_cache = value_cache.reshape(cl_dev, head_count, HEAD_DIM)
    key_new = key_new.reshape(tok_dev, head_count, HEAD_DIM)
    value_new = value_new.reshape(tok_dev, head_count, HEAD_DIM)
    position = kv_rank * cl_dev + jnp.arange(cl_dev, dtype=jnp.int32)
    usable = position < length
    operands = (key_cache, value_cache, key_new, value_new, usable)
    own_top, own_denom, own_sum = partial_softmax(own_queries, *operands)
    far_top, far_denom, far_sum = partial_softmax(far_queries, *operands)
    back_top, back_denom, back_sum = lax.ppermute(
        (far_top, far_denom, far_sum.astype(jnp.bfloat16)), "kv", swap
    )
    joint_top = jnp.maximum(own_top, back_top)
    own_factor = jnp.exp(own_top - joint_top)
    back_factor = jnp.exp(back_top - joint_top)
    joint_sum = own_sum * own_factor[..., None] + back_sum.astype(jnp.float32) * back_factor[..., None]
    joint_denom = own_denom * own_factor + back_denom * back_factor
    return (joint_sum / joint_denom[..., None]).reshape(tok_dev, feat).astype(jnp.bfloat16)


def shards(
    plan,
    resid,
    queries,
    new_keys,
    new_values,
    cache_keys,
    cache_values,
    cached_len,
    group_request,
    w_out,
    norm_gain,
    route_ids,
    route_weights,
    gate_w,
    up_w,
    down_w,
):
    kv_rank = lax.axis_index("kv")
    ep_count = lax.axis_size("ep")
    tok_dev = resid.shape[1]
    cl_dev = cache_keys.shape[1]
    feat = queries.shape[2]
    head_count = feat // HEAD_DIM
    score_scale = 1.0 / math.sqrt(HEAD_DIM)
    request_index = jnp.arange(cached_len.shape[0], dtype=jnp.int32)
    length = jnp.sum(jnp.where(request_index == group_request[0], cached_len, 0))
    if lax.axis_size("kv") == 2 and plan is not None:
        attended = paired_attention(
            queries[0], new_keys[0], new_values[0], cache_keys[0], cache_values[0], length
        )
    else:
        attended = joined_attention(
            queries, new_keys, new_values, cache_keys, cache_values, length
        )
    proj = jnp.dot(attended, w_out, preferred_element_type=jnp.float32)
    hidden = (resid[0].astype(jnp.float32) + proj).astype(jnp.bfloat16)
    hidden_f = hidden.astype(jnp.float32)
    normed = (
        hidden_f
        * lax.rsqrt(jnp.mean(hidden_f * hidden_f, axis=-1, keepdims=True) + 1e-06)
        * norm_gain.astype(jnp.float32)
    ).astype(jnp.bfloat16)
    if plan is not None:
        moe_sum, _ = dense_moe(
            plan, normed, route_ids[0], route_weights[0], (gate_w, up_w, down_w), attended
        )
        return (hidden_f + moe_sum).astype(jnp.bfloat16)[None]
    expert_count = EXP_DEV * ep_count
    capacity = min(tok_dev, max(2, tok_dev * TOP * 3 // (2 * expert_count)))
    route_flat = route_ids[0].reshape(-1)
    one_hot = (route_flat[:, None] == jnp.arange(expert_count, dtype=jnp.int32)[None, :]).astype(
        jnp.int32
    )
    rank_in = jnp.sum((jnp.cumsum(one_hot, axis=0) - 1) * one_hot, axis=1)
    slot_of = route_flat * capacity + rank_in
    slot_index = jnp.arange(expert_count * capacity, dtype=jnp.int32)
    placing = jnp.sum(
        (slot_of.reshape(tok_dev, TOP)[None, :, :] == slot_index[:, None, None]).astype(jnp.int32),
        axis=-1,
    ).astype(jnp.bfloat16)
    outgoing = jnp.dot(placing, normed, preferred_element_type=jnp.float32).astype(jnp.bfloat16)
    outgoing = outgoing.reshape(ep_count, EXP_DEV, capacity, D)
    full_gate, full_up, full_down = (
        lax.all_gather(gate_w, "kv", axis=2, tiled=True),
        lax.all_gather(up_w, "kv", axis=2, tiled=True),
        lax.all_gather(down_w, "kv", axis=1, tiled=True),
    )
    expert_out = expert_full(
        lax.all_to_all(outgoing, "ep", split_axis=0, concat_axis=0, tiled=True),
        full_gate,
        full_up,
        full_down,
    ).astype(jnp.bfloat16)
    returned = lax.all_to_all(expert_out, "ep", split_axis=0, concat_axis=0, tiled=True).reshape(
        expert_count * capacity, D
    )
    picked = jnp.take(returned, slot_of, axis=0).reshape(tok_dev, TOP, D)
    moe_sum = jnp.sum(picked.astype(jnp.float32) * route_weights[0][..., None], axis=1)
    return (hidden_f + moe_sum).astype(jnp.bfloat16)[None]


def solution(mesh):
    placed = (
        P("ep", "kv", None),
        P("ep", "kv", None),
        P("ep", "kv", None),
        P("ep", "kv", None),
        P("ep", "kv", None),
        P("ep", "kv", None),
        P(),
        P("ep"),
        P(),
        P(),
        P("ep", "kv", None),
        P("ep", "kv", None),
        P("ep", None, "kv"),
        P("ep", None, "kv"),
        P("ep", "kv", None),
    )

    def run(*args):
        plan = gather_plan(mesh, [a.shape for a in args])
        body = functools.partial(shards, plan)
        return jax.shard_map(
            body, mesh=mesh, in_specs=placed, out_specs=P("ep", "kv", None), check_vma=False
        )(*args)

    return run
```

```python
import functools
import math

import jax
import jax.numpy as jnp
import numpy as np
from jax import lax
from jax.sharding import PartitionSpec as P

D = 2048
HEAD_DIM = 128
TOP = 8
EXP_DEV = 1


def combined_all(shard, axis, join):
    gathered = jax.tree.map(
        lambda a, kind: lax.all_gather(a.astype(kind), axis),
        shard,
        (jnp.bfloat16, jnp.bfloat16, jnp.bfloat16),
    )

    def take(source):
        return jax.tree.map(
            lambda a, own: lax.dynamic_index_in_dim(a, source, 0, False).astype(own.dtype),
            gathered,
            shard,
        )

    return lax.fori_loop(
        1, lax.axis_size(axis), lambda source, state: join(state, take(source)), take(0)
    )


def expert_full(row_block, gate_part, up_part, down_part):
    gate_val = jnp.einsum(
        "sjkd,jdf->sjkf", row_block, gate_part, preferred_element_type=jnp.float32
    )
    up_val = jnp.einsum("sjkd,jdf->sjkf", row_block, up_part, preferred_element_type=jnp.float32)
    act = (jax.nn.silu(gate_val) * up_val).astype(jnp.bfloat16)
    return jnp.einsum("sjkf,jfd->sjkd", act, down_part, preferred_element_type=jnp.float32)


def full_weights(gate_w, up_w, down_w):
    kv_count = lax.axis_size("kv")
    if kv_count != 2:
        return (
            lax.all_gather(gate_w[0], "kv", axis=1, tiled=True),
            lax.all_gather(up_w[0], "kv", axis=1, tiled=True),
            lax.all_gather(down_w[0], "kv", axis=0, tiled=True),
        )
    hidden = gate_w.shape[2]
    packed = jnp.stack([gate_w[0], up_w[0], down_w[0].reshape(-1, hidden)])
    other = lax.ppermute(packed, "kv", [(0, 1), (1, 0)])
    first = lax.axis_index("kv") == 0
    joined = []
    for slot, axis in zip(range(3), (1, 1, 0)):
        own, far = packed[slot], other[slot]
        if axis == 0:
            own, far = own.reshape(hidden, -1), far.reshape(hidden, -1)
        low = jnp.where(first, own, far)
        high = jnp.where(first, far, own)
        joined.append(jnp.concatenate([low, high], axis=axis))
    return tuple(joined)


def dense_moe(plan, normed, route_ids, route_weights, weight_parts, anchor):
    expert_count = EXP_DEV * lax.axis_size("ep")
    experts = jnp.arange(expert_count, dtype=jnp.int32)
    own_expert = lax.axis_index("ep")
    chosen = route_ids[:, :, None] == experts[None, None, :]
    weight_table = jnp.sum(jnp.where(chosen, route_weights[:, :, None], 0.0), axis=1)
    weight_parts, anchor = lax.optimization_barrier((weight_parts, anchor))
    full = list(full_weights(*weight_parts))

    def expert(rows, table):
        weights = jnp.sum(jnp.where(experts == own_expert, table, 0.0), axis=1)
        gate_val = jnp.dot(rows, full[0], preferred_element_type=jnp.float32)
        up_val = jnp.dot(rows, full[1], preferred_element_type=jnp.float32)
        act = (jax.nn.silu(gate_val) * up_val).astype(jnp.bfloat16)
        out_rows = jnp.dot(act, full[2], preferred_element_type=jnp.float32)
        out_rows = out_rows.astype(jnp.bfloat16).astype(jnp.float32)
        return out_rows * weights[:, None]

    pieces = [((normed, weight_table), None, None)]
    groups = []
    low = 0
    tie_at = next((n + 1 for n, (_, ends) in enumerate(plan) if ends), 0)
    first_wave = [
        [lax.ppermute(pieces[0][0], "ep", pairs) for pairs in pairs_list] for pairs_list, _ in plan
    ]
    first_wave = lax.optimization_barrier(first_wave)
    for number, (pairs_list, ends) in enumerate(plan):
        grown = []
        for parent, (block, _, _) in enumerate(pieces):
            for slot, pairs in enumerate(pairs_list):
                if parent == 0:
                    grown.append((first_wave[number][slot], parent, pairs))
                else:
                    grown.append((lax.ppermute(block, "ep", pairs), parent, pairs))
        if number == tie_at:
            tied = lax.optimization_barrier((tuple(full), [piece[0] for piece in grown]))
            full = list(tied[0])
            grown = [(block, parent, pairs) for block, (_, parent, pairs) in zip(tied[1], grown)]
        pieces = pieces + grown
        if ends:
            groups.append((low, len(pieces)))
            low = len(pieces)
    if low < len(pieces) or not groups:
        groups.append((low, len(pieces)))
    partial = [None] * len(pieces)
    size = normed.shape[0]
    for low, high in groups:
        rows = jnp.concatenate([pieces[i][0][0] for i in range(low, high)], axis=0)
        table = jnp.concatenate([pieces[i][0][1] for i in range(low, high)], axis=0)
        out = expert(rows, table)
        for offset, i in enumerate(range(low, high)):
            partial[i] = out[offset * size:(offset + 1) * size]
    for index in reversed(range(1, len(pieces))):
        _, parent, pairs = pieces[index]
        back = [(target, source) for source, target in pairs]
        sent = lax.ppermute(partial[index].astype(jnp.bfloat16), "ep", back)
        partial[parent] = partial[parent] + sent.astype(jnp.float32)
    return partial[0], anchor


def gather_plan(mesh, shapes):
    kv_count, ep_count = mesh.devices.shape
    rows = ep_count * shapes[0][1] // kv_count
    if EXP_DEV != 1 or shapes[12][0] != ep_count or rows > 4096:
        return None
    places = []
    for device in mesh.devices[0]:
        coords = getattr(device, "coords", None)
        core = getattr(device, "core_on_chip", None)
        if coords is None or core is None:
            return None
        places.append(tuple(coords) + (core,))
    width = len(places[0])
    values = [sorted({p[a] for p in places}) for a in range(width)]
    varying = [a for a in range(width) if len(values[a]) > 1]
    total = 1
    for a in varying:
        total *= len(values[a])
    if total != ep_count or len(set(places)) != ep_count:
        return None
    rank_of = {p: r for r, p in enumerate(places)}
    core_axis = width - 1
    order = sorted((a for a in varying if a != core_axis), key=lambda a: -len(values[a]))
    order += [a for a in varying if a == core_axis]
    plan = []
    for a in order:
        size = len(values[a])
        if size & (size - 1) == 0:
            steps = []
            span = size // 2
            while span:
                steps.append(("xor", span))
                span //= 2
        else:
            steps = [("shift", shift) for shift in range(1, size)]
            steps = [steps]
        for number, step in enumerate(steps):
            group = step if isinstance(step, list) else [step]
            stage = []
            for kind, amount in group:
                pairs = []
                for r, p in enumerate(places):
                    index = values[a].index(p[a])
                    moved = list(p)
                    moved[a] = values[a][index ^ amount if kind == "xor" else (index + amount) % size]
                    pairs.append((r, rank_of[tuple(moved)]))
                stage.append(pairs)
            plan.append((stage, number == len(steps) - 1))
    return plan


def joined_attention(queries, new_keys, new_values, cache_keys, cache_values, length):
    kv_rank = lax.axis_index("kv")
    tok_dev = queries.shape[1]
    cl_dev = cache_keys.shape[1]
    feat = queries.shape[2]
    head_count = feat // HEAD_DIM
    score_scale = 1.0 / math.sqrt(HEAD_DIM)
    every_query = lax.all_gather(queries[0], "kv", axis=0, tiled=True)
    new_total = every_query.shape[0]
    query_heads = every_query.reshape(new_total, head_count, HEAD_DIM)
    key_cache = cache_keys[0].reshape(cl_dev, head_count, HEAD_DIM)
    value_cache = cache_values[0].reshape(cl_dev, head_count, HEAD_DIM)
    key_new = new_keys[0].reshape(tok_dev, head_count, HEAD_DIM)
    value_new = new_values[0].reshape(tok_dev, head_count, HEAD_DIM)
    score_cache = (
        jnp.einsum("qhd,khd->qhk", query_heads, key_cache, preferred_element_type=jnp.float32)
        * score_scale
    )
    position = kv_rank * cl_dev + jnp.arange(cl_dev, dtype=jnp.int32)
    score_cache = jnp.where((position < length)[None, None, :], score_cache, -jnp.inf)
    score_new = (
        jnp.einsum("qhd,khd->qhk", query_heads, key_new, preferred_element_type=jnp.float32)
        * score_scale
    )
    local_top = jnp.maximum(jnp.max(score_cache, axis=-1), jnp.max(score_new, axis=-1))
    expo_cache = jnp.exp(score_cache - local_top[..., None])
    expo_new = jnp.exp(score_new - local_top[..., None])
    denom = jnp.sum(expo_cache, axis=-1) + jnp.sum(expo_new, axis=-1)
    summed = jnp.einsum(
        "qhk,khd->qhd",
        expo_cache.astype(jnp.bfloat16),
        value_cache,
        preferred_element_type=jnp.float32,
    )
    summed = summed + jnp.einsum(
        "qhk,khd->qhd", expo_new.astype(jnp.bfloat16), value_new, preferred_element_type=jnp.float32
    )
    summed, denom = (summed.reshape(new_total, feat), denom)

    def join(first, second):
        first_top, first_denom, first_sum = first
        second_top, second_denom, second_sum = second
        joint_top = jnp.maximum(first_top, second_top)
        first_factor = jnp.exp(first_top - joint_top)
        second_factor = jnp.exp(second_top - joint_top)
        rows_here = first_sum.shape[0]
        joint_sum = (
            first_sum.reshape(rows_here, head_count, HEAD_DIM) * first_factor[..., None]
            + second_sum.reshape(rows_here, head_count, HEAD_DIM) * second_factor[..., None]
        )
        return (
            joint_top,
            first_denom * first_factor + second_denom * second_factor,
            joint_sum.reshape(rows_here, feat),
        )

    joint_top, joint_denom, joint_sum = combined_all((local_top, denom, summed), "kv", join)
    row_start = kv_rank * tok_dev
    own_sum = lax.dynamic_slice_in_dim(joint_sum, row_start, tok_dev, 0)
    own_denom = lax.dynamic_slice_in_dim(joint_denom, row_start, tok_dev, 0)
    attended = (
        (own_sum.reshape(tok_dev, head_count, HEAD_DIM) / own_denom[..., None])
        .reshape(tok_dev, feat)
        .astype(jnp.bfloat16)
    )
    return attended


def partial_softmax(query_rows, key_cache, value_cache, key_new, value_new, usable):
    rows, feat = query_rows.shape
    head_count = feat // HEAD_DIM
    score_scale = 1.0 / math.sqrt(HEAD_DIM)
    query_heads = query_rows.reshape(rows, head_count, HEAD_DIM)
    score_cache = (
        jnp.einsum("qhd,khd->qhk", query_heads, key_cache, preferred_element_type=jnp.float32)
        * score_scale
    )
    score_cache = jnp.where(usable[None, None, :], score_cache, -jnp.inf)
    score_new = (
        jnp.einsum("qhd,khd->qhk", query_heads, key_new, preferred_element_type=jnp.float32)
        * score_scale
    )
    top = jnp.maximum(jnp.max(score_cache, axis=-1), jnp.max(score_new, axis=-1))
    expo_cache = jnp.exp(score_cache - top[..., None])
    expo_new = jnp.exp(score_new - top[..., None])
    denom = jnp.sum(expo_cache, axis=-1) + jnp.sum(expo_new, axis=-1)
    summed = jnp.einsum(
        "qhk,khd->qhd", expo_cache.astype(jnp.bfloat16), value_cache,
        preferred_element_type=jnp.float32,
    )
    summed = summed + jnp.einsum(
        "qhk,khd->qhd", expo_new.astype(jnp.bfloat16), value_new, preferred_element_type=jnp.float32
    )
    return top, denom, summed


def paired_attention(own_queries, key_new, value_new, key_cache, value_cache, length):
    kv_rank = lax.axis_index("kv")
    swap = [(0, 1), (1, 0)]
    tok_dev, feat = own_queries.shape
    cl_dev = key_cache.shape[0]
    head_count = feat // HEAD_DIM
    far_queries = lax.ppermute(own_queries, "kv", swap)
    key_cache = key_cache.reshape(cl_dev, head_count, HEAD_DIM)
    value_cache = value_cache.reshape(cl_dev, head_count, HEAD_DIM)
    key_new = key_new.reshape(tok_dev, head_count, HEAD_DIM)
    value_new = value_new.reshape(tok_dev, head_count, HEAD_DIM)
    position = kv_rank * cl_dev + jnp.arange(cl_dev, dtype=jnp.int32)
    usable = position < length
    operands = (key_cache, value_cache, key_new, value_new, usable)
    own_top, own_denom, own_sum = partial_softmax(own_queries, *operands)
    far_top, far_denom, far_sum = partial_softmax(far_queries, *operands)
    back_top, back_denom, back_sum = lax.ppermute(
        (far_top, far_denom, far_sum.astype(jnp.bfloat16)), "kv", swap
    )
    joint_top = jnp.maximum(own_top, back_top)
    own_factor = jnp.exp(own_top - joint_top)
    back_factor = jnp.exp(back_top - joint_top)
    joint_sum = own_sum * own_factor[..., None] + back_sum.astype(jnp.float32) * back_factor[..., None]
    joint_denom = own_denom * own_factor + back_denom * back_factor
    return (joint_sum / joint_denom[..., None]).reshape(tok_dev, feat).astype(jnp.bfloat16)


def shards(
    plan,
    resid,
    queries,
    new_keys,
    new_values,
    cache_keys,
    cache_values,
    cached_len,
    group_request,
    w_out,
    norm_gain,
    route_ids,
    route_weights,
    gate_w,
    up_w,
    down_w,
):
    kv_rank = lax.axis_index("kv")
    ep_count = lax.axis_size("ep")
    tok_dev = resid.shape[1]
    cl_dev = cache_keys.shape[1]
    feat = queries.shape[2]
    head_count = feat // HEAD_DIM
    score_scale = 1.0 / math.sqrt(HEAD_DIM)
    request_index = jnp.arange(cached_len.shape[0], dtype=jnp.int32)
    length = jnp.sum(jnp.where(request_index == group_request[0], cached_len, 0))
    if lax.axis_size("kv") == 2 and plan is not None:
        attended = paired_attention(
            queries[0], new_keys[0], new_values[0], cache_keys[0], cache_values[0], length
        )
    else:
        attended = joined_attention(
            queries, new_keys, new_values, cache_keys, cache_values, length
        )
    proj = jnp.dot(attended, w_out, preferred_element_type=jnp.float32)
    hidden = (resid[0].astype(jnp.float32) + proj).astype(jnp.bfloat16)
    hidden_f = hidden.astype(jnp.float32)
    normed = (
        hidden_f
        * lax.rsqrt(jnp.mean(hidden_f * hidden_f, axis=-1, keepdims=True) + 1e-06)
        * norm_gain.astype(jnp.float32)
    ).astype(jnp.bfloat16)
    if plan is not None:
        moe_sum, _ = dense_moe(
            plan, normed, route_ids[0], route_weights[0], (gate_w, up_w, down_w), attended
        )
        return (hidden_f + moe_sum).astype(jnp.bfloat16)[None]
    expert_count = EXP_DEV * ep_count
    capacity = min(tok_dev, max(2, tok_dev * TOP * 3 // (2 * expert_count)))
    route_flat = route_ids[0].reshape(-1)
    one_hot = (route_flat[:, None] == jnp.arange(expert_count, dtype=jnp.int32)[None, :]).astype(
        jnp.int32
    )
    rank_in = jnp.sum((jnp.cumsum(one_hot, axis=0) - 1) * one_hot, axis=1)
    slot_of = route_flat * capacity + rank_in
    slot_index = jnp.arange(expert_count * capacity, dtype=jnp.int32)
    placing = jnp.sum(
        (slot_of.reshape(tok_dev, TOP)[None, :, :] == slot_index[:, None, None]).astype(jnp.int32),
        axis=-1,
    ).astype(jnp.bfloat16)
    outgoing = jnp.dot(placing, normed, preferred_element_type=jnp.float32).astype(jnp.bfloat16)
    outgoing = outgoing.reshape(ep_count, EXP_DEV, capacity, D)
    full_gate, full_up, full_down = (
        lax.all_gather(gate_w, "kv", axis=2, tiled=True),
        lax.all_gather(up_w, "kv", axis=2, tiled=True),
        lax.all_gather(down_w, "kv", axis=1, tiled=True),
    )
    expert_out = expert_full(
        lax.all_to_all(outgoing, "ep", split_axis=0, concat_axis=0, tiled=True),
        full_gate,
        full_up,
        full_down,
    ).astype(jnp.bfloat16)
    returned = lax.all_to_all(expert_out, "ep", split_axis=0, concat_axis=0, tiled=True).reshape(
        expert_count * capacity, D
    )
    picked = jnp.take(returned, slot_of, axis=0).reshape(tok_dev, TOP, D)
    moe_sum = jnp.sum(picked.astype(jnp.float32) * route_weights[0][..., None], axis=1)
    return (hidden_f + moe_sum).astype(jnp.bfloat16)[None]


def solution(mesh):
    placed = (
        P("ep", "kv", None),
        P("ep", "kv", None),
        P("ep", "kv", None),
        P("ep", "kv", None),
        P("ep", "kv", None),
        P("ep", "kv", None),
        P(),
        P("ep"),
        P(),
        P(),
        P("ep", "kv", None),
        P("ep", "kv", None),
        P("ep", None, "kv"),
        P("ep", None, "kv"),
        P("ep", "kv", None),
    )

    def run(*args):
        plan = gather_plan(mesh, [a.shape for a in args])
        body = functools.partial(shards, plan)
        return jax.shard_map(
            body, mesh=mesh, in_specs=placed, out_specs=P("ep", "kv", None), check_vma=False
        )(*args)

    return run
```

```python
import functools
import math

import jax
import jax.numpy as jnp
import numpy as np
from jax import lax
from jax.sharding import PartitionSpec as P

D = 2048
HEAD_DIM = 128
TOP = 8
EXP_DEV = 1


def combined_all(shard, axis, join):
    gathered = jax.tree.map(
        lambda a, kind: lax.all_gather(a.astype(kind), axis),
        shard,
        (jnp.bfloat16, jnp.bfloat16, jnp.bfloat16),
    )

    def take(source):
        return jax.tree.map(
            lambda a, own: lax.dynamic_index_in_dim(a, source, 0, False).astype(own.dtype),
            gathered,
            shard,
        )

    return lax.fori_loop(
        1, lax.axis_size(axis), lambda source, state: join(state, take(source)), take(0)
    )


def expert_full(row_block, gate_part, up_part, down_part):
    gate_val = jnp.einsum(
        "sjkd,jdf->sjkf", row_block, gate_part, preferred_element_type=jnp.float32
    )
    up_val = jnp.einsum("sjkd,jdf->sjkf", row_block, up_part, preferred_element_type=jnp.float32)
    act = (jax.nn.silu(gate_val) * up_val).astype(jnp.bfloat16)
    return jnp.einsum("sjkf,jfd->sjkd", act, down_part, preferred_element_type=jnp.float32)


def full_weights(gate_w, up_w, down_w):
    kv_count = lax.axis_size("kv")
    if kv_count != 2:
        return (
            lax.all_gather(gate_w[0], "kv", axis=1, tiled=True),
            lax.all_gather(up_w[0], "kv", axis=1, tiled=True),
            lax.all_gather(down_w[0], "kv", axis=0, tiled=True),
        )
    hidden = gate_w.shape[2]
    packed = jnp.stack([gate_w[0], up_w[0], down_w[0].reshape(-1, hidden)])
    other = lax.ppermute(packed, "kv", [(0, 1), (1, 0)])
    first = lax.axis_index("kv") == 0
    joined = []
    for slot, axis in zip(range(3), (1, 1, 0)):
        own, far = packed[slot], other[slot]
        if axis == 0:
            own, far = own.reshape(hidden, -1), far.reshape(hidden, -1)
        low = jnp.where(first, own, far)
        high = jnp.where(first, far, own)
        joined.append(jnp.concatenate([low, high], axis=axis))
    return tuple(joined)


def dense_moe(plan, normed, route_ids, route_weights, weight_parts, anchor):
    expert_count = EXP_DEV * lax.axis_size("ep")
    experts = jnp.arange(expert_count, dtype=jnp.int32)
    own_expert = lax.axis_index("ep")
    chosen = route_ids[:, :, None] == experts[None, None, :]
    weight_table = jnp.sum(jnp.where(chosen, route_weights[:, :, None], 0.0), axis=1)
    weight_parts, anchor = lax.optimization_barrier((weight_parts, anchor))
    full = list(full_weights(*weight_parts))

    def expert(rows, table):
        weights = jnp.sum(jnp.where(experts == own_expert, table, 0.0), axis=1)
        gate_val = jnp.dot(rows, full[0], preferred_element_type=jnp.float32)
        up_val = jnp.dot(rows, full[1], preferred_element_type=jnp.float32)
        act = (jax.nn.silu(gate_val) * up_val).astype(jnp.bfloat16)
        out_rows = jnp.dot(act, full[2], preferred_element_type=jnp.float32)
        out_rows = out_rows.astype(jnp.bfloat16).astype(jnp.float32)
        return out_rows * weights[:, None]

    pieces = [((normed, weight_table), None, None)]
    groups = []
    low = 0
    tie_at = next((n + 1 for n, (_, ends) in enumerate(plan) if ends), 0)
    first_wave = [
        [lax.ppermute(pieces[0][0], "ep", pairs) for pairs in pairs_list] for pairs_list, _ in plan
    ]
    first_wave = lax.optimization_barrier(first_wave)
    for number, (pairs_list, ends) in enumerate(plan):
        grown = []
        for parent, (block, _, _) in enumerate(pieces):
            for slot, pairs in enumerate(pairs_list):
                if parent == 0:
                    grown.append((first_wave[number][slot], parent, pairs))
                else:
                    grown.append((lax.ppermute(block, "ep", pairs), parent, pairs))
        if number == tie_at:
            tied = lax.optimization_barrier((tuple(full), [piece[0] for piece in grown]))
            full = list(tied[0])
            grown = [(block, parent, pairs) for block, (_, parent, pairs) in zip(tied[1], grown)]
        pieces = pieces + grown
        if ends:
            groups.append((low, len(pieces)))
            low = len(pieces)
    if low < len(pieces) or not groups:
        groups.append((low, len(pieces)))
    partial = [None] * len(pieces)
    size = normed.shape[0]
    ordered = []
    for low, high in reversed(groups):
        members = list(range(low, high))
        if len(members) >= 8:
            half = len(members) // 2
            ordered += [members[:half], members[half:]]
        else:
            ordered.append(members)
    for members in ordered:
        rows = jnp.concatenate([pieces[i][0][0] for i in members], axis=0)
        table = jnp.concatenate([pieces[i][0][1] for i in members], axis=0)
        out = expert(rows, table)
        for offset, i in enumerate(members):
            partial[i] = out[offset * size:(offset + 1) * size]
    for index in reversed(range(1, len(pieces))):
        _, parent, pairs = pieces[index]
        back = [(target, source) for source, target in pairs]
        sent = lax.ppermute(partial[index].astype(jnp.bfloat16), "ep", back)
        partial[parent] = partial[parent] + sent.astype(jnp.float32)
    return partial[0], anchor


def gather_plan(mesh, shapes):
    kv_count, ep_count = mesh.devices.shape
    rows = ep_count * shapes[0][1] // kv_count
    if EXP_DEV != 1 or shapes[12][0] != ep_count or rows > 4096:
        return None
    places = []
    for device in mesh.devices[0]:
        coords = getattr(device, "coords", None)
        core = getattr(device, "core_on_chip", None)
        if coords is None or core is None:
            return None
        places.append(tuple(coords) + (core,))
    width = len(places[0])
    values = [sorted({p[a] for p in places}) for a in range(width)]
    varying = [a for a in range(width) if len(values[a]) > 1]
    total = 1
    for a in varying:
        total *= len(values[a])
    if total != ep_count or len(set(places)) != ep_count:
        return None
    rank_of = {p: r for r, p in enumerate(places)}
    core_axis = width - 1
    order = sorted((a for a in varying if a != core_axis), key=lambda a: -len(values[a]))
    order += [a for a in varying if a == core_axis]
    plan = []
    for a in order:
        size = len(values[a])
        if size & (size - 1) == 0:
            steps = []
            span = size // 2
            while span:
                steps.append(("xor", span))
                span //= 2
        else:
            steps = [("shift", shift) for shift in range(1, size)]
            steps = [steps]
        for number, step in enumerate(steps):
            group = step if isinstance(step, list) else [step]
            stage = []
            for kind, amount in group:
                pairs = []
                for r, p in enumerate(places):
                    index = values[a].index(p[a])
                    moved = list(p)
                    moved[a] = values[a][index ^ amount if kind == "xor" else (index + amount) % size]
                    pairs.append((r, rank_of[tuple(moved)]))
                stage.append(pairs)
            plan.append((stage, number == len(steps) - 1))
    return plan


def joined_attention(queries, new_keys, new_values, cache_keys, cache_values, length):
    kv_rank = lax.axis_index("kv")
    tok_dev = queries.shape[1]
    cl_dev = cache_keys.shape[1]
    feat = queries.shape[2]
    head_count = feat // HEAD_DIM
    score_scale = 1.0 / math.sqrt(HEAD_DIM)
    every_query = lax.all_gather(queries[0], "kv", axis=0, tiled=True)
    new_total = every_query.shape[0]
    query_heads = every_query.reshape(new_total, head_count, HEAD_DIM)
    key_cache = cache_keys[0].reshape(cl_dev, head_count, HEAD_DIM)
    value_cache = cache_values[0].reshape(cl_dev, head_count, HEAD_DIM)
    key_new = new_keys[0].reshape(tok_dev, head_count, HEAD_DIM)
    value_new = new_values[0].reshape(tok_dev, head_count, HEAD_DIM)
    score_cache = (
        jnp.einsum("qhd,khd->qhk", query_heads, key_cache, preferred_element_type=jnp.float32)
        * score_scale
    )
    position = kv_rank * cl_dev + jnp.arange(cl_dev, dtype=jnp.int32)
    score_cache = jnp.where((position < length)[None, None, :], score_cache, -jnp.inf)
    score_new = (
        jnp.einsum("qhd,khd->qhk", query_heads, key_new, preferred_element_type=jnp.float32)
        * score_scale
    )
    local_top = jnp.maximum(jnp.max(score_cache, axis=-1), jnp.max(score_new, axis=-1))
    expo_cache = jnp.exp(score_cache - local_top[..., None])
    expo_new = jnp.exp(score_new - local_top[..., None])
    denom = jnp.sum(expo_cache, axis=-1) + jnp.sum(expo_new, axis=-1)
    summed = jnp.einsum(
        "qhk,khd->qhd",
        expo_cache.astype(jnp.bfloat16),
        value_cache,
        preferred_element_type=jnp.float32,
    )
    summed = summed + jnp.einsum(
        "qhk,khd->qhd", expo_new.astype(jnp.bfloat16), value_new, preferred_element_type=jnp.float32
    )
    summed, denom = (summed.reshape(new_total, feat), denom)

    def join(first, second):
        first_top, first_denom, first_sum = first
        second_top, second_denom, second_sum = second
        joint_top = jnp.maximum(first_top, second_top)
        first_factor = jnp.exp(first_top - joint_top)
        second_factor = jnp.exp(second_top - joint_top)
        rows_here = first_sum.shape[0]
        joint_sum = (
            first_sum.reshape(rows_here, head_count, HEAD_DIM) * first_factor[..., None]
            + second_sum.reshape(rows_here, head_count, HEAD_DIM) * second_factor[..., None]
        )
        return (
            joint_top,
            first_denom * first_factor + second_denom * second_factor,
            joint_sum.reshape(rows_here, feat),
        )

    joint_top, joint_denom, joint_sum = combined_all((local_top, denom, summed), "kv", join)
    row_start = kv_rank * tok_dev
    own_sum = lax.dynamic_slice_in_dim(joint_sum, row_start, tok_dev, 0)
    own_denom = lax.dynamic_slice_in_dim(joint_denom, row_start, tok_dev, 0)
    attended = (
        (own_sum.reshape(tok_dev, head_count, HEAD_DIM) / own_denom[..., None])
        .reshape(tok_dev, feat)
        .astype(jnp.bfloat16)
    )
    return attended


def partial_softmax(query_rows, key_cache, value_cache, key_new, value_new, usable):
    rows, feat = query_rows.shape
    head_count = feat // HEAD_DIM
    score_scale = 1.0 / math.sqrt(HEAD_DIM)
    query_heads = query_rows.reshape(rows, head_count, HEAD_DIM)
    score_cache = (
        jnp.einsum("qhd,khd->qhk", query_heads, key_cache, preferred_element_type=jnp.float32)
        * score_scale
    )
    score_cache = jnp.where(usable[None, None, :], score_cache, -jnp.inf)
    score_new = (
        jnp.einsum("qhd,khd->qhk", query_heads, key_new, preferred_element_type=jnp.float32)
        * score_scale
    )
    top = jnp.maximum(jnp.max(score_cache, axis=-1), jnp.max(score_new, axis=-1))
    expo_cache = jnp.exp(score_cache - top[..., None])
    expo_new = jnp.exp(score_new - top[..., None])
    denom = jnp.sum(expo_cache, axis=-1) + jnp.sum(expo_new, axis=-1)
    summed = jnp.einsum(
        "qhk,khd->qhd", expo_cache.astype(jnp.bfloat16), value_cache,
        preferred_element_type=jnp.float32,
    )
    summed = summed + jnp.einsum(
        "qhk,khd->qhd", expo_new.astype(jnp.bfloat16), value_new, preferred_element_type=jnp.float32
    )
    return top, denom, summed


def paired_attention(own_queries, key_new, value_new, key_cache, value_cache, length):
    kv_rank = lax.axis_index("kv")
    swap = [(0, 1), (1, 0)]
    tok_dev, feat = own_queries.shape
    cl_dev = key_cache.shape[0]
    head_count = feat // HEAD_DIM
    far_queries = lax.ppermute(own_queries, "kv", swap)
    key_cache = key_cache.reshape(cl_dev, head_count, HEAD_DIM)
    value_cache = value_cache.reshape(cl_dev, head_count, HEAD_DIM)
    key_new = key_new.reshape(tok_dev, head_count, HEAD_DIM)
    value_new = value_new.reshape(tok_dev, head_count, HEAD_DIM)
    position = kv_rank * cl_dev + jnp.arange(cl_dev, dtype=jnp.int32)
    usable = position < length
    operands = (key_cache, value_cache, key_new, value_new, usable)
    own_top, own_denom, own_sum = partial_softmax(own_queries, *operands)
    far_top, far_denom, far_sum = partial_softmax(far_queries, *operands)
    back_top, back_denom, back_sum = lax.ppermute(
        (far_top, far_denom, far_sum.astype(jnp.bfloat16)), "kv", swap
    )
    joint_top = jnp.maximum(own_top, back_top)
    own_factor = jnp.exp(own_top - joint_top)
    back_factor = jnp.exp(back_top - joint_top)
    joint_sum = own_sum * own_factor[..., None] + back_sum.astype(jnp.float32) * back_factor[..., None]
    joint_denom = own_denom * own_factor + back_denom * back_factor
    return (joint_sum / joint_denom[..., None]).reshape(tok_dev, feat).astype(jnp.bfloat16)


def shards(
    plan,
    resid,
    queries,
    new_keys,
    new_values,
    cache_keys,
    cache_values,
    cached_len,
    group_request,
    w_out,
    norm_gain,
    route_ids,
    route_weights,
    gate_w,
    up_w,
    down_w,
):
    kv_rank = lax.axis_index("kv")
    ep_count = lax.axis_size("ep")
    tok_dev = resid.shape[1]
    cl_dev = cache_keys.shape[1]
    feat = queries.shape[2]
    head_count = feat // HEAD_DIM
    score_scale = 1.0 / math.sqrt(HEAD_DIM)
    request_index = jnp.arange(cached_len.shape[0], dtype=jnp.int32)
    length = jnp.sum(jnp.where(request_index == group_request[0], cached_len, 0))
    if lax.axis_size("kv") == 2 and plan is not None:
        attended = paired_attention(
            queries[0], new_keys[0], new_values[0], cache_keys[0], cache_values[0], length
        )
    else:
        attended = joined_attention(
            queries, new_keys, new_values, cache_keys, cache_values, length
        )
    proj = jnp.dot(attended, w_out, preferred_element_type=jnp.float32)
    hidden = (resid[0].astype(jnp.float32) + proj).astype(jnp.bfloat16)
    hidden_f = hidden.astype(jnp.float32)
    normed = (
        hidden_f
        * lax.rsqrt(jnp.mean(hidden_f * hidden_f, axis=-1, keepdims=True) + 1e-06)
        * norm_gain.astype(jnp.float32)
    ).astype(jnp.bfloat16)
    if plan is not None:
        moe_sum, _ = dense_moe(
            plan, normed, route_ids[0], route_weights[0], (gate_w, up_w, down_w), attended
        )
        return (hidden_f + moe_sum).astype(jnp.bfloat16)[None]
    expert_count = EXP_DEV * ep_count
    capacity = min(tok_dev, max(2, tok_dev * TOP * 3 // (2 * expert_count)))
    route_flat = route_ids[0].reshape(-1)
    one_hot = (route_flat[:, None] == jnp.arange(expert_count, dtype=jnp.int32)[None, :]).astype(
        jnp.int32
    )
    rank_in = jnp.sum((jnp.cumsum(one_hot, axis=0) - 1) * one_hot, axis=1)
    slot_of = route_flat * capacity + rank_in
    slot_index = jnp.arange(expert_count * capacity, dtype=jnp.int32)
    placing = jnp.sum(
        (slot_of.reshape(tok_dev, TOP)[None, :, :] == slot_index[:, None, None]).astype(jnp.int32),
        axis=-1,
    ).astype(jnp.bfloat16)
    outgoing = jnp.dot(placing, normed, preferred_element_type=jnp.float32).astype(jnp.bfloat16)
    outgoing = outgoing.reshape(ep_count, EXP_DEV, capacity, D)
    full_gate, full_up, full_down = (
        lax.all_gather(gate_w, "kv", axis=2, tiled=True),
        lax.all_gather(up_w, "kv", axis=2, tiled=True),
        lax.all_gather(down_w, "kv", axis=1, tiled=True),
    )
    expert_out = expert_full(
        lax.all_to_all(outgoing, "ep", split_axis=0, concat_axis=0, tiled=True),
        full_gate,
        full_up,
        full_down,
    ).astype(jnp.bfloat16)
    returned = lax.all_to_all(expert_out, "ep", split_axis=0, concat_axis=0, tiled=True).reshape(
        expert_count * capacity, D
    )
    picked = jnp.take(returned, slot_of, axis=0).reshape(tok_dev, TOP, D)
    moe_sum = jnp.sum(picked.astype(jnp.float32) * route_weights[0][..., None], axis=1)
    return (hidden_f + moe_sum).astype(jnp.bfloat16)[None]


def solution(mesh):
    placed = (
        P("ep", "kv", None),
        P("ep", "kv", None),
        P("ep", "kv", None),
        P("ep", "kv", None),
        P("ep", "kv", None),
        P("ep", "kv", None),
        P(),
        P("ep"),
        P(),
        P(),
        P("ep", "kv", None),
        P("ep", "kv", None),
        P("ep", None, "kv"),
        P("ep", None, "kv"),
        P("ep", "kv", None),
    )

    def run(*args):
        plan = gather_plan(mesh, [a.shape for a in args])
        body = functools.partial(shards, plan)
        return jax.shard_map(
            body, mesh=mesh, in_specs=placed, out_specs=P("ep", "kv", None), check_vma=False
        )(*args)

    return run
```

```python
import functools
import math

import jax
import jax.numpy as jnp
import numpy as np
from jax import lax
from jax.sharding import PartitionSpec as P

D = 2048
HEAD_DIM = 128
TOP = 8
EXP_DEV = 1


def combined_all(shard, axis, join):
    gathered = jax.tree.map(
        lambda a, kind: lax.all_gather(a.astype(kind), axis),
        shard,
        (jnp.bfloat16, jnp.bfloat16, jnp.bfloat16),
    )

    def take(source):
        return jax.tree.map(
            lambda a, own: lax.dynamic_index_in_dim(a, source, 0, False).astype(own.dtype),
            gathered,
            shard,
        )

    return lax.fori_loop(
        1, lax.axis_size(axis), lambda source, state: join(state, take(source)), take(0)
    )


def expert_full(row_block, gate_part, up_part, down_part):
    gate_val = jnp.einsum(
        "sjkd,jdf->sjkf", row_block, gate_part, preferred_element_type=jnp.float32
    )
    up_val = jnp.einsum("sjkd,jdf->sjkf", row_block, up_part, preferred_element_type=jnp.float32)
    act = (jax.nn.silu(gate_val) * up_val).astype(jnp.bfloat16)
    return jnp.einsum("sjkf,jfd->sjkd", act, down_part, preferred_element_type=jnp.float32)


def full_weights(gate_w, up_w, down_w):
    kv_count = lax.axis_size("kv")
    if kv_count != 2:
        return (
            lax.all_gather(gate_w[0], "kv", axis=1, tiled=True),
            lax.all_gather(up_w[0], "kv", axis=1, tiled=True),
            lax.all_gather(down_w[0], "kv", axis=0, tiled=True),
        )
    hidden = gate_w.shape[2]
    packed = jnp.stack([gate_w[0], up_w[0], down_w[0].reshape(-1, hidden)])
    other = lax.ppermute(packed, "kv", [(0, 1), (1, 0)])
    first = lax.axis_index("kv") == 0
    joined = []
    for slot, axis in zip(range(3), (1, 1, 0)):
        own, far = packed[slot], other[slot]
        if axis == 0:
            own, far = own.reshape(hidden, -1), far.reshape(hidden, -1)
        low = jnp.where(first, own, far)
        high = jnp.where(first, far, own)
        joined.append(jnp.concatenate([low, high], axis=axis))
    return tuple(joined)


def dense_moe(plan, normed, route_ids, route_weights, weight_parts, anchor):
    expert_count = EXP_DEV * lax.axis_size("ep")
    experts = jnp.arange(expert_count, dtype=jnp.int32)
    own_expert = lax.axis_index("ep")
    chosen = route_ids[:, :, None] == experts[None, None, :]
    weight_table = jnp.sum(jnp.where(chosen, route_weights[:, :, None], 0.0), axis=1)
    weight_parts, anchor = lax.optimization_barrier((weight_parts, anchor))
    full = list(full_weights(*weight_parts))

    def expert(rows, table):
        weights = jnp.sum(jnp.where(experts == own_expert, table, 0.0), axis=1)
        gate_val = jnp.dot(rows, full[0], preferred_element_type=jnp.float32)
        up_val = jnp.dot(rows, full[1], preferred_element_type=jnp.float32)
        act = (jax.nn.silu(gate_val) * up_val).astype(jnp.bfloat16)
        out_rows = jnp.dot(act, full[2], preferred_element_type=jnp.float32)
        out_rows = out_rows.astype(jnp.bfloat16).astype(jnp.float32)
        return out_rows * weights[:, None]

    every_table = weight_table[None]
    ep_count = lax.axis_size("ep")
    span = 1
    while span < ep_count:
        swapped = lax.ppermute(every_table, "ep", [(r, r ^ span) for r in range(ep_count)])
        every_table = jnp.concatenate([every_table, swapped], axis=0)
        span *= 2
    origins = {0: np.arange(ep_count)}
    pieces = [((normed, weight_table), None, None)]
    groups = []
    low = 0
    tie_at = next((n + 1 for n, (_, ends) in enumerate(plan) if ends), 0)
    first_wave = [
        [(lax.ppermute(normed, "ep", pairs), None) for pairs in pairs_list] for pairs_list, _ in plan
    ]
    first_wave = lax.optimization_barrier(first_wave)
    for number, (pairs_list, ends) in enumerate(plan):
        grown = []
        for parent, (block, _, _) in enumerate(pieces):
            for slot, pairs in enumerate(pairs_list):
                moved = np.zeros(ep_count, dtype=np.int64)
                for source, target in pairs:
                    moved[target] = origins[parent][source]
                origins[len(pieces) + len(grown)] = moved
                if parent == 0:
                    grown.append((first_wave[number][slot], parent, pairs))
                else:
                    grown.append(((lax.ppermute(block[0], "ep", pairs), None), parent, pairs))
        if number == tie_at:
            tied = lax.optimization_barrier((tuple(full), [piece[0] for piece in grown]))
            full = list(tied[0])
            grown = [(block, parent, pairs) for block, (_, parent, pairs) in zip(tied[1], grown)]
        pieces = pieces + grown
        if ends:
            groups.append((low, len(pieces)))
            low = len(pieces)
    if low < len(pieces) or not groups:
        groups.append((low, len(pieces)))
    partial = [None] * len(pieces)
    size = normed.shape[0]
    ordered = []
    for low, high in reversed(groups):
        members = list(range(low, high))
        if len(members) >= 8:
            half = len(members) // 2
            ordered += [members[:half], members[half:]]
        else:
            ordered.append(members)
    for members in ordered:
        rows = jnp.concatenate([pieces[i][0][0] for i in members], axis=0)
        tables = []
        for i in members:
            if i == 0:
                tables.append(weight_table)
            else:
                place = jnp.bitwise_xor(jnp.asarray(origins[i], jnp.int32)[own_expert], own_expert)
                tables.append(lax.dynamic_index_in_dim(every_table, place, 0, False))
        table = jnp.concatenate(tables, axis=0)
        out = expert(rows, table)
        for offset, i in enumerate(members):
            partial[i] = out[offset * size:(offset + 1) * size]
    for index in reversed(range(1, len(pieces))):
        _, parent, pairs = pieces[index]
        back = [(target, source) for source, target in pairs]
        sent = lax.ppermute(partial[index].astype(jnp.bfloat16), "ep", back)
        partial[parent] = partial[parent] + sent.astype(jnp.float32)
    return partial[0], anchor


def gather_plan(mesh, shapes):
    kv_count, ep_count = mesh.devices.shape
    rows = ep_count * shapes[0][1] // kv_count
    if EXP_DEV != 1 or shapes[12][0] != ep_count or rows > 4096 or ep_count & (ep_count - 1):
        return None
    places = []
    for device in mesh.devices[0]:
        coords = getattr(device, "coords", None)
        core = getattr(device, "core_on_chip", None)
        if coords is None or core is None:
            return None
        places.append(tuple(coords) + (core,))
    width = len(places[0])
    values = [sorted({p[a] for p in places}) for a in range(width)]
    varying = [a for a in range(width) if len(values[a]) > 1]
    total = 1
    for a in varying:
        total *= len(values[a])
    if total != ep_count or len(set(places)) != ep_count:
        return None
    rank_of = {p: r for r, p in enumerate(places)}
    core_axis = width - 1
    order = sorted((a for a in varying if a != core_axis), key=lambda a: -len(values[a]))
    order += [a for a in varying if a == core_axis]
    plan = []
    for a in order:
        size = len(values[a])
        if size & (size - 1) == 0:
            steps = []
            span = size // 2
            while span:
                steps.append(("xor", span))
                span //= 2
        else:
            steps = [("shift", shift) for shift in range(1, size)]
            steps = [steps]
        for number, step in enumerate(steps):
            group = step if isinstance(step, list) else [step]
            stage = []
            for kind, amount in group:
                pairs = []
                for r, p in enumerate(places):
                    index = values[a].index(p[a])
                    moved = list(p)
                    moved[a] = values[a][index ^ amount if kind == "xor" else (index + amount) % size]
                    pairs.append((r, rank_of[tuple(moved)]))
                stage.append(pairs)
            plan.append((stage, number == len(steps) - 1))
    return plan


def joined_attention(queries, new_keys, new_values, cache_keys, cache_values, length):
    kv_rank = lax.axis_index("kv")
    tok_dev = queries.shape[1]
    cl_dev = cache_keys.shape[1]
    feat = queries.shape[2]
    head_count = feat // HEAD_DIM
    score_scale = 1.0 / math.sqrt(HEAD_DIM)
    every_query = lax.all_gather(queries[0], "kv", axis=0, tiled=True)
    new_total = every_query.shape[0]
    query_heads = every_query.reshape(new_total, head_count, HEAD_DIM)
    key_cache = cache_keys[0].reshape(cl_dev, head_count, HEAD_DIM)
    value_cache = cache_values[0].reshape(cl_dev, head_count, HEAD_DIM)
    key_new = new_keys[0].reshape(tok_dev, head_count, HEAD_DIM)
    value_new = new_values[0].reshape(tok_dev, head_count, HEAD_DIM)
    score_cache = (
        jnp.einsum("qhd,khd->qhk", query_heads, key_cache, preferred_element_type=jnp.float32)
        * score_scale
    )
    position = kv_rank * cl_dev + jnp.arange(cl_dev, dtype=jnp.int32)
    score_cache = jnp.where((position < length)[None, None, :], score_cache, -jnp.inf)
    score_new = (
        jnp.einsum("qhd,khd->qhk", query_heads, key_new, preferred_element_type=jnp.float32)
        * score_scale
    )
    local_top = jnp.maximum(jnp.max(score_cache, axis=-1), jnp.max(score_new, axis=-1))
    expo_cache = jnp.exp(score_cache - local_top[..., None])
    expo_new = jnp.exp(score_new - local_top[..., None])
    denom = jnp.sum(expo_cache, axis=-1) + jnp.sum(expo_new, axis=-1)
    summed = jnp.einsum(
        "qhk,khd->qhd",
        expo_cache.astype(jnp.bfloat16),
        value_cache,
        preferred_element_type=jnp.float32,
    )
    summed = summed + jnp.einsum(
        "qhk,khd->qhd", expo_new.astype(jnp.bfloat16), value_new, preferred_element_type=jnp.float32
    )
    summed, denom = (summed.reshape(new_total, feat), denom)

    def join(first, second):
        first_top, first_denom, first_sum = first
        second_top, second_denom, second_sum = second
        joint_top = jnp.maximum(first_top, second_top)
        first_factor = jnp.exp(first_top - joint_top)
        second_factor = jnp.exp(second_top - joint_top)
        rows_here = first_sum.shape[0]
        joint_sum = (
            first_sum.reshape(rows_here, head_count, HEAD_DIM) * first_factor[..., None]
            + second_sum.reshape(rows_here, head_count, HEAD_DIM) * second_factor[..., None]
        )
        return (
            joint_top,
            first_denom * first_factor + second_denom * second_factor,
            joint_sum.reshape(rows_here, feat),
        )

    joint_top, joint_denom, joint_sum = combined_all((local_top, denom, summed), "kv", join)
    row_start = kv_rank * tok_dev
    own_sum = lax.dynamic_slice_in_dim(joint_sum, row_start, tok_dev, 0)
    own_denom = lax.dynamic_slice_in_dim(joint_denom, row_start, tok_dev, 0)
    attended = (
        (own_sum.reshape(tok_dev, head_count, HEAD_DIM) / own_denom[..., None])
        .reshape(tok_dev, feat)
        .astype(jnp.bfloat16)
    )
    return attended


def partial_softmax(query_rows, key_cache, value_cache, key_new, value_new, usable):
    rows, feat = query_rows.shape
    head_count = feat // HEAD_DIM
    score_scale = 1.0 / math.sqrt(HEAD_DIM)
    query_heads = query_rows.reshape(rows, head_count, HEAD_DIM)
    score_cache = (
        jnp.einsum("qhd,khd->qhk", query_heads, key_cache, preferred_element_type=jnp.float32)
        * score_scale
    )
    score_cache = jnp.where(usable[None, None, :], score_cache, -jnp.inf)
    score_new = (
        jnp.einsum("qhd,khd->qhk", query_heads, key_new, preferred_element_type=jnp.float32)
        * score_scale
    )
    top = jnp.maximum(jnp.max(score_cache, axis=-1), jnp.max(score_new, axis=-1))
    expo_cache = jnp.exp(score_cache - top[..., None])
    expo_new = jnp.exp(score_new - top[..., None])
    denom = jnp.sum(expo_cache, axis=-1) + jnp.sum(expo_new, axis=-1)
    summed = jnp.einsum(
        "qhk,khd->qhd", expo_cache.astype(jnp.bfloat16), value_cache,
        preferred_element_type=jnp.float32,
    )
    summed = summed + jnp.einsum(
        "qhk,khd->qhd", expo_new.astype(jnp.bfloat16), value_new, preferred_element_type=jnp.float32
    )
    return top, denom, summed


def paired_attention(own_queries, key_new, value_new, key_cache, value_cache, length):
    kv_rank = lax.axis_index("kv")
    swap = [(0, 1), (1, 0)]
    tok_dev, feat = own_queries.shape
    cl_dev = key_cache.shape[0]
    head_count = feat // HEAD_DIM
    far_queries = lax.ppermute(own_queries, "kv", swap)
    key_cache = key_cache.reshape(cl_dev, head_count, HEAD_DIM)
    value_cache = value_cache.reshape(cl_dev, head_count, HEAD_DIM)
    key_new = key_new.reshape(tok_dev, head_count, HEAD_DIM)
    value_new = value_new.reshape(tok_dev, head_count, HEAD_DIM)
    position = kv_rank * cl_dev + jnp.arange(cl_dev, dtype=jnp.int32)
    usable = position < length
    operands = (key_cache, value_cache, key_new, value_new, usable)
    own_top, own_denom, own_sum = partial_softmax(own_queries, *operands)
    far_top, far_denom, far_sum = partial_softmax(far_queries, *operands)
    back_top, back_denom, back_sum = lax.ppermute(
        (far_top, far_denom, far_sum.astype(jnp.bfloat16)), "kv", swap
    )
    joint_top = jnp.maximum(own_top, back_top)
    own_factor = jnp.exp(own_top - joint_top)
    back_factor = jnp.exp(back_top - joint_top)
    joint_sum = own_sum * own_factor[..., None] + back_sum.astype(jnp.float32) * back_factor[..., None]
    joint_denom = own_denom * own_factor + back_denom * back_factor
    return (joint_sum / joint_denom[..., None]).reshape(tok_dev, feat).astype(jnp.bfloat16)


def shards(
    plan,
    resid,
    queries,
    new_keys,
    new_values,
    cache_keys,
    cache_values,
    cached_len,
    group_request,
    w_out,
    norm_gain,
    route_ids,
    route_weights,
    gate_w,
    up_w,
    down_w,
):
    kv_rank = lax.axis_index("kv")
    ep_count = lax.axis_size("ep")
    tok_dev = resid.shape[1]
    cl_dev = cache_keys.shape[1]
    feat = queries.shape[2]
    head_count = feat // HEAD_DIM
    score_scale = 1.0 / math.sqrt(HEAD_DIM)
    request_index = jnp.arange(cached_len.shape[0], dtype=jnp.int32)
    length = jnp.sum(jnp.where(request_index == group_request[0], cached_len, 0))
    if lax.axis_size("kv") == 2 and plan is not None:
        attended = paired_attention(
            queries[0], new_keys[0], new_values[0], cache_keys[0], cache_values[0], length
        )
    else:
        attended = joined_attention(
            queries, new_keys, new_values, cache_keys, cache_values, length
        )
    proj = jnp.dot(attended, w_out, preferred_element_type=jnp.float32)
    hidden = (resid[0].astype(jnp.float32) + proj).astype(jnp.bfloat16)
    hidden_f = hidden.astype(jnp.float32)
    normed = (
        hidden_f
        * lax.rsqrt(jnp.mean(hidden_f * hidden_f, axis=-1, keepdims=True) + 1e-06)
        * norm_gain.astype(jnp.float32)
    ).astype(jnp.bfloat16)
    if plan is not None:
        moe_sum, _ = dense_moe(
            plan, normed, route_ids[0], route_weights[0], (gate_w, up_w, down_w), attended
        )
        return (hidden_f + moe_sum).astype(jnp.bfloat16)[None]
    expert_count = EXP_DEV * ep_count
    capacity = min(tok_dev, max(2, tok_dev * TOP * 3 // (2 * expert_count)))
    route_flat = route_ids[0].reshape(-1)
    one_hot = (route_flat[:, None] == jnp.arange(expert_count, dtype=jnp.int32)[None, :]).astype(
        jnp.int32
    )
    rank_in = jnp.sum((jnp.cumsum(one_hot, axis=0) - 1) * one_hot, axis=1)
    slot_of = route_flat * capacity + rank_in
    slot_index = jnp.arange(expert_count * capacity, dtype=jnp.int32)
    placing = jnp.sum(
        (slot_of.reshape(tok_dev, TOP)[None, :, :] == slot_index[:, None, None]).astype(jnp.int32),
        axis=-1,
    ).astype(jnp.bfloat16)
    outgoing = jnp.dot(placing, normed, preferred_element_type=jnp.float32).astype(jnp.bfloat16)
    outgoing = outgoing.reshape(ep_count, EXP_DEV, capacity, D)
    full_gate, full_up, full_down = (
        lax.all_gather(gate_w, "kv", axis=2, tiled=True),
        lax.all_gather(up_w, "kv", axis=2, tiled=True),
        lax.all_gather(down_w, "kv", axis=1, tiled=True),
    )
    expert_out = expert_full(
        lax.all_to_all(outgoing, "ep", split_axis=0, concat_axis=0, tiled=True),
        full_gate,
        full_up,
        full_down,
    ).astype(jnp.bfloat16)
    returned = lax.all_to_all(expert_out, "ep", split_axis=0, concat_axis=0, tiled=True).reshape(
        expert_count * capacity, D
    )
    picked = jnp.take(returned, slot_of, axis=0).reshape(tok_dev, TOP, D)
    moe_sum = jnp.sum(picked.astype(jnp.float32) * route_weights[0][..., None], axis=1)
    return (hidden_f + moe_sum).astype(jnp.bfloat16)[None]


def solution(mesh):
    placed = (
        P("ep", "kv", None),
        P("ep", "kv", None),
        P("ep", "kv", None),
        P("ep", "kv", None),
        P("ep", "kv", None),
        P("ep", "kv", None),
        P(),
        P("ep"),
        P(),
        P(),
        P("ep", "kv", None),
        P("ep", "kv", None),
        P("ep", None, "kv"),
        P("ep", None, "kv"),
        P("ep", "kv", None),
    )

    def run(*args):
        plan = gather_plan(mesh, [a.shape for a in args])
        body = functools.partial(shards, plan)
        return jax.shard_map(
            body, mesh=mesh, in_specs=placed, out_specs=P("ep", "kv", None), check_vma=False
        )(*args)

    return run
```

```python
import functools
import math

import jax
import jax.numpy as jnp
import numpy as np
from jax import lax
from jax.sharding import PartitionSpec as P

D = 2048
HEAD_DIM = 128
TOP = 8
EXP_DEV = 1


def combined_all(shard, axis, join):
    gathered = jax.tree.map(
        lambda a, kind: lax.all_gather(a.astype(kind), axis),
        shard,
        (jnp.bfloat16, jnp.bfloat16, jnp.bfloat16),
    )

    def take(source):
        return jax.tree.map(
            lambda a, own: lax.dynamic_index_in_dim(a, source, 0, False).astype(own.dtype),
            gathered,
            shard,
        )

    return lax.fori_loop(
        1, lax.axis_size(axis), lambda source, state: join(state, take(source)), take(0)
    )


def expert_full(row_block, gate_part, up_part, down_part):
    gate_val = jnp.einsum(
        "sjkd,jdf->sjkf", row_block, gate_part, preferred_element_type=jnp.float32
    )
    up_val = jnp.einsum("sjkd,jdf->sjkf", row_block, up_part, preferred_element_type=jnp.float32)
    act = (jax.nn.silu(gate_val) * up_val).astype(jnp.bfloat16)
    return jnp.einsum("sjkf,jfd->sjkd", act, down_part, preferred_element_type=jnp.float32)


def full_weights(gate_w, up_w, down_w):
    kv_count = lax.axis_size("kv")
    if kv_count != 2:
        return (
            lax.all_gather(gate_w[0], "kv", axis=1, tiled=True),
            lax.all_gather(up_w[0], "kv", axis=1, tiled=True),
            lax.all_gather(down_w[0], "kv", axis=0, tiled=True),
        )
    hidden = gate_w.shape[2]
    packed = jnp.stack([gate_w[0], up_w[0], down_w[0].reshape(-1, hidden)])
    other = lax.ppermute(packed, "kv", [(0, 1), (1, 0)])
    first = lax.axis_index("kv") == 0
    joined = []
    for slot, axis in zip(range(3), (1, 1, 0)):
        own, far = packed[slot], other[slot]
        if axis == 0:
            own, far = own.reshape(hidden, -1), far.reshape(hidden, -1)
        low = jnp.where(first, own, far)
        high = jnp.where(first, far, own)
        joined.append(jnp.concatenate([low, high], axis=axis))
    return tuple(joined)


def dense_moe(plan, normed, route_ids, route_weights, weight_parts, anchor):
    expert_count = EXP_DEV * lax.axis_size("ep")
    experts = jnp.arange(expert_count, dtype=jnp.int32)
    own_expert = lax.axis_index("ep")
    chosen = route_ids[:, :, None] == experts[None, None, :]
    weight_table = jnp.sum(jnp.where(chosen, route_weights[:, :, None], 0.0), axis=1)
    weight_parts, anchor = lax.optimization_barrier((weight_parts, anchor))
    full = list(full_weights(*weight_parts))

    def expert(rows, table):
        weights = jnp.sum(jnp.where(experts == own_expert, table, 0.0), axis=1)
        gate_val = jnp.dot(rows, full[0], preferred_element_type=jnp.float32)
        up_val = jnp.dot(rows, full[1], preferred_element_type=jnp.float32)
        act = (jax.nn.silu(gate_val) * up_val).astype(jnp.bfloat16)
        out_rows = jnp.dot(act, full[2], preferred_element_type=jnp.float32)
        out_rows = out_rows.astype(jnp.bfloat16).astype(jnp.float32)
        return out_rows * weights[:, None]

    pieces = [((normed, weight_table), None, None, -1)]
    waves = [[0]]
    axis_of = []
    axis = 0
    for _, ends in plan:
        axis_of.append(axis)
        axis += 1 if ends else 0
    weight_stage = next((n for n, a in enumerate(axis_of) if a == 1), len(plan) - 1)
    weights_tied = False
    while True:
        fresh = []
        for parent in waves[-1]:
            block, _, _, last = pieces[parent]
            for stage in range(last + 1, len(plan)):
                for pairs in plan[stage][0]:
                    fresh.append((lax.ppermute(block, "ep", pairs), parent, pairs, stage))
        if not fresh:
            break
        blocks = [piece[0] for piece in fresh]
        if len(waves) <= 2:
            blocks = lax.optimization_barrier(blocks)
        elif not weights_tied:
            spot = next((k for k, piece in enumerate(fresh) if piece[3] == weight_stage), None)
            if spot is not None:
                tied = lax.optimization_barrier((tuple(full), blocks[spot]))
                full = list(tied[0])
                blocks[spot] = tied[1]
                weights_tied = True
        waves.append(list(range(len(pieces), len(pieces) + len(fresh))))
        pieces += [(b,) + piece[1:] for b, piece in zip(blocks, fresh)]
    groups = {}
    for index, piece in enumerate(pieces):
        groups.setdefault(0 if index == 0 else axis_of[piece[3]], []).append(index)
    member_lists = [members for _, members in sorted(groups.items())]
    partial = [None] * len(pieces)
    size = normed.shape[0]
    ordered = []
    for members in reversed(member_lists):
        if len(members) >= 8:
            half = len(members) // 2
            ordered += [members[:half], members[half:]]
        else:
            ordered.append(members)
    for members in ordered:
        rows = jnp.concatenate([pieces[i][0][0] for i in members], axis=0)
        table = jnp.concatenate([pieces[i][0][1] for i in members], axis=0)
        out = expert(rows, table)
        for offset, i in enumerate(members):
            partial[i] = out[offset * size:(offset + 1) * size]
    for index in reversed(range(1, len(pieces))):
        _, parent, pairs, _ = pieces[index]
        back = [(target, source) for source, target in pairs]
        sent = lax.ppermute(partial[index].astype(jnp.bfloat16), "ep", back)
        partial[parent] = partial[parent] + sent.astype(jnp.float32)
    return partial[0], anchor


def gather_plan(mesh, shapes):
    kv_count, ep_count = mesh.devices.shape
    rows = ep_count * shapes[0][1] // kv_count
    if EXP_DEV != 1 or shapes[12][0] != ep_count or rows > 4096:
        return None
    places = []
    for device in mesh.devices[0]:
        coords = getattr(device, "coords", None)
        core = getattr(device, "core_on_chip", None)
        if coords is None or core is None:
            return None
        places.append(tuple(coords) + (core,))
    width = len(places[0])
    values = [sorted({p[a] for p in places}) for a in range(width)]
    varying = [a for a in range(width) if len(values[a]) > 1]
    total = 1
    for a in varying:
        total *= len(values[a])
    if total != ep_count or len(set(places)) != ep_count:
        return None
    rank_of = {p: r for r, p in enumerate(places)}
    core_axis = width - 1
    order = sorted((a for a in varying if a != core_axis), key=lambda a: -len(values[a]))
    order += [a for a in varying if a == core_axis]
    plan = []
    for a in order:
        size = len(values[a])
        if size & (size - 1) == 0:
            steps = []
            span = size // 2
            while span:
                steps.append(("xor", span))
                span //= 2
        else:
            steps = [("shift", shift) for shift in range(1, size)]
            steps = [steps]
        for number, step in enumerate(steps):
            group = step if isinstance(step, list) else [step]
            stage = []
            for kind, amount in group:
                pairs = []
                for r, p in enumerate(places):
                    index = values[a].index(p[a])
                    moved = list(p)
                    moved[a] = values[a][index ^ amount if kind == "xor" else (index + amount) % size]
                    pairs.append((r, rank_of[tuple(moved)]))
                stage.append(pairs)
            plan.append((stage, number == len(steps) - 1))
    return plan


def joined_attention(queries, new_keys, new_values, cache_keys, cache_values, length):
    kv_rank = lax.axis_index("kv")
    tok_dev = queries.shape[1]
    cl_dev = cache_keys.shape[1]
    feat = queries.shape[2]
    head_count = feat // HEAD_DIM
    score_scale = 1.0 / math.sqrt(HEAD_DIM)
    every_query = lax.all_gather(queries[0], "kv", axis=0, tiled=True)
    new_total = every_query.shape[0]
    query_heads = every_query.reshape(new_total, head_count, HEAD_DIM)
    key_cache = cache_keys[0].reshape(cl_dev, head_count, HEAD_DIM)
    value_cache = cache_values[0].reshape(cl_dev, head_count, HEAD_DIM)
    key_new = new_keys[0].reshape(tok_dev, head_count, HEAD_DIM)
    value_new = new_values[0].reshape(tok_dev, head_count, HEAD_DIM)
    score_cache = (
        jnp.einsum("qhd,khd->qhk", query_heads, key_cache, preferred_element_type=jnp.float32)
        * score_scale
    )
    position = kv_rank * cl_dev + jnp.arange(cl_dev, dtype=jnp.int32)
    score_cache = jnp.where((position < length)[None, None, :], score_cache, -jnp.inf)
    score_new = (
        jnp.einsum("qhd,khd->qhk", query_heads, key_new, preferred_element_type=jnp.float32)
        * score_scale
    )
    local_top = jnp.maximum(jnp.max(score_cache, axis=-1), jnp.max(score_new, axis=-1))
    expo_cache = jnp.exp(score_cache - local_top[..., None])
    expo_new = jnp.exp(score_new - local_top[..., None])
    denom = jnp.sum(expo_cache, axis=-1) + jnp.sum(expo_new, axis=-1)
    summed = jnp.einsum(
        "qhk,khd->qhd",
        expo_cache.astype(jnp.bfloat16),
        value_cache,
        preferred_element_type=jnp.float32,
    )
    summed = summed + jnp.einsum(
        "qhk,khd->qhd", expo_new.astype(jnp.bfloat16), value_new, preferred_element_type=jnp.float32
    )
    summed, denom = (summed.reshape(new_total, feat), denom)

    def join(first, second):
        first_top, first_denom, first_sum = first
        second_top, second_denom, second_sum = second
        joint_top = jnp.maximum(first_top, second_top)
        first_factor = jnp.exp(first_top - joint_top)
        second_factor = jnp.exp(second_top - joint_top)
        rows_here = first_sum.shape[0]
        joint_sum = (
            first_sum.reshape(rows_here, head_count, HEAD_DIM) * first_factor[..., None]
            + second_sum.reshape(rows_here, head_count, HEAD_DIM) * second_factor[..., None]
        )
        return (
            joint_top,
            first_denom * first_factor + second_denom * second_factor,
            joint_sum.reshape(rows_here, feat),
        )

    joint_top, joint_denom, joint_sum = combined_all((local_top, denom, summed), "kv", join)
    row_start = kv_rank * tok_dev
    own_sum = lax.dynamic_slice_in_dim(joint_sum, row_start, tok_dev, 0)
    own_denom = lax.dynamic_slice_in_dim(joint_denom, row_start, tok_dev, 0)
    attended = (
        (own_sum.reshape(tok_dev, head_count, HEAD_DIM) / own_denom[..., None])
        .reshape(tok_dev, feat)
        .astype(jnp.bfloat16)
    )
    return attended


def partial_softmax(query_rows, key_cache, value_cache, key_new, value_new, usable):
    rows, feat = query_rows.shape
    head_count = feat // HEAD_DIM
    score_scale = 1.0 / math.sqrt(HEAD_DIM)
    query_heads = query_rows.reshape(rows, head_count, HEAD_DIM)
    score_cache = (
        jnp.einsum("qhd,khd->qhk", query_heads, key_cache, preferred_element_type=jnp.float32)
        * score_scale
    )
    score_cache = jnp.where(usable[None, None, :], score_cache, -jnp.inf)
    score_new = (
        jnp.einsum("qhd,khd->qhk", query_heads, key_new, preferred_element_type=jnp.float32)
        * score_scale
    )
    top = jnp.maximum(jnp.max(score_cache, axis=-1), jnp.max(score_new, axis=-1))
    expo_cache = jnp.exp(score_cache - top[..., None])
    expo_new = jnp.exp(score_new - top[..., None])
    denom = jnp.sum(expo_cache, axis=-1) + jnp.sum(expo_new, axis=-1)
    summed = jnp.einsum(
        "qhk,khd->qhd", expo_cache.astype(jnp.bfloat16), value_cache,
        preferred_element_type=jnp.float32,
    )
    summed = summed + jnp.einsum(
        "qhk,khd->qhd", expo_new.astype(jnp.bfloat16), value_new, preferred_element_type=jnp.float32
    )
    return top, denom, summed


def paired_attention(own_queries, key_new, value_new, key_cache, value_cache, length):
    kv_rank = lax.axis_index("kv")
    swap = [(0, 1), (1, 0)]
    tok_dev, feat = own_queries.shape
    cl_dev = key_cache.shape[0]
    head_count = feat // HEAD_DIM
    far_queries = lax.ppermute(own_queries, "kv", swap)
    key_cache = key_cache.reshape(cl_dev, head_count, HEAD_DIM)
    value_cache = value_cache.reshape(cl_dev, head_count, HEAD_DIM)
    key_new = key_new.reshape(tok_dev, head_count, HEAD_DIM)
    value_new = value_new.reshape(tok_dev, head_count, HEAD_DIM)
    position = kv_rank * cl_dev + jnp.arange(cl_dev, dtype=jnp.int32)
    usable = position < length
    operands = (key_cache, value_cache, key_new, value_new, usable)
    own_top, own_denom, own_sum = partial_softmax(own_queries, *operands)
    far_top, far_denom, far_sum = partial_softmax(far_queries, *operands)
    back_top, back_denom, back_sum = lax.ppermute(
        (far_top, far_denom, far_sum.astype(jnp.bfloat16)), "kv", swap
    )
    joint_top = jnp.maximum(own_top, back_top)
    own_factor = jnp.exp(own_top - joint_top)
    back_factor = jnp.exp(back_top - joint_top)
    joint_sum = own_sum * own_factor[..., None] + back_sum.astype(jnp.float32) * back_factor[..., None]
    joint_denom = own_denom * own_factor + back_denom * back_factor
    return (joint_sum / joint_denom[..., None]).reshape(tok_dev, feat).astype(jnp.bfloat16)


def shards(
    plan,
    resid,
    queries,
    new_keys,
    new_values,
    cache_keys,
    cache_values,
    cached_len,
    group_request,
    w_out,
    norm_gain,
    route_ids,
    route_weights,
    gate_w,
    up_w,
    down_w,
):
    kv_rank = lax.axis_index("kv")
    ep_count = lax.axis_size("ep")
    tok_dev = resid.shape[1]
    cl_dev = cache_keys.shape[1]
    feat = queries.shape[2]
    head_count = feat // HEAD_DIM
    score_scale = 1.0 / math.sqrt(HEAD_DIM)
    request_index = jnp.arange(cached_len.shape[0], dtype=jnp.int32)
    length = jnp.sum(jnp.where(request_index == group_request[0], cached_len, 0))
    if lax.axis_size("kv") == 2 and plan is not None:
        attended = paired_attention(
            queries[0], new_keys[0], new_values[0], cache_keys[0], cache_values[0], length
        )
    else:
        attended = joined_attention(
            queries, new_keys, new_values, cache_keys, cache_values, length
        )
    proj = jnp.dot(attended, w_out, preferred_element_type=jnp.float32)
    hidden = (resid[0].astype(jnp.float32) + proj).astype(jnp.bfloat16)
    hidden_f = hidden.astype(jnp.float32)
    normed = (
        hidden_f
        * lax.rsqrt(jnp.mean(hidden_f * hidden_f, axis=-1, keepdims=True) + 1e-06)
        * norm_gain.astype(jnp.float32)
    ).astype(jnp.bfloat16)
    if plan is not None:
        moe_sum, _ = dense_moe(
            plan, normed, route_ids[0], route_weights[0], (gate_w, up_w, down_w), attended
        )
        return (hidden_f + moe_sum).astype(jnp.bfloat16)[None]
    expert_count = EXP_DEV * ep_count
    capacity = min(tok_dev, max(2, tok_dev * TOP * 3 // (2 * expert_count)))
    route_flat = route_ids[0].reshape(-1)
    one_hot = (route_flat[:, None] == jnp.arange(expert_count, dtype=jnp.int32)[None, :]).astype(
        jnp.int32
    )
    rank_in = jnp.sum((jnp.cumsum(one_hot, axis=0) - 1) * one_hot, axis=1)
    slot_of = route_flat * capacity + rank_in
    slot_index = jnp.arange(expert_count * capacity, dtype=jnp.int32)
    placing = jnp.sum(
        (slot_of.reshape(tok_dev, TOP)[None, :, :] == slot_index[:, None, None]).astype(jnp.int32),
        axis=-1,
    ).astype(jnp.bfloat16)
    outgoing = jnp.dot(placing, normed, preferred_element_type=jnp.float32).astype(jnp.bfloat16)
    outgoing = outgoing.reshape(ep_count, EXP_DEV, capacity, D)
    full_gate, full_up, full_down = (
        lax.all_gather(gate_w, "kv", axis=2, tiled=True),
        lax.all_gather(up_w, "kv", axis=2, tiled=True),
        lax.all_gather(down_w, "kv", axis=1, tiled=True),
    )
    expert_out = expert_full(
        lax.all_to_all(outgoing, "ep", split_axis=0, concat_axis=0, tiled=True),
        full_gate,
        full_up,
        full_down,
    ).astype(jnp.bfloat16)
    returned = lax.all_to_all(expert_out, "ep", split_axis=0, concat_axis=0, tiled=True).reshape(
        expert_count * capacity, D
    )
    picked = jnp.take(returned, slot_of, axis=0).reshape(tok_dev, TOP, D)
    moe_sum = jnp.sum(picked.astype(jnp.float32) * route_weights[0][..., None], axis=1)
    return (hidden_f + moe_sum).astype(jnp.bfloat16)[None]


def solution(mesh):
    placed = (
        P("ep", "kv", None),
        P("ep", "kv", None),
        P("ep", "kv", None),
        P("ep", "kv", None),
        P("ep", "kv", None),
        P("ep", "kv", None),
        P(),
        P("ep"),
        P(),
        P(),
        P("ep", "kv", None),
        P("ep", "kv", None),
        P("ep", None, "kv"),
        P("ep", None, "kv"),
        P("ep", "kv", None),
    )

    def run(*args):
        plan = gather_plan(mesh, [a.shape for a in args])
        body = functools.partial(shards, plan)
        return jax.shard_map(
            body, mesh=mesh, in_specs=placed, out_specs=P("ep", "kv", None), check_vma=False
        )(*args)

    return run
```

```python
import functools
import math

import jax
import jax.numpy as jnp
import numpy as np
from jax import lax
from jax.sharding import PartitionSpec as P

D = 2048
HEAD_DIM = 128
TOP = 8
EXP_DEV = 1


def combined_all(shard, axis, join):
    gathered = jax.tree.map(
        lambda a, kind: lax.all_gather(a.astype(kind), axis),
        shard,
        (jnp.bfloat16, jnp.bfloat16, jnp.bfloat16),
    )

    def take(source):
        return jax.tree.map(
            lambda a, own: lax.dynamic_index_in_dim(a, source, 0, False).astype(own.dtype),
            gathered,
            shard,
        )

    return lax.fori_loop(
        1, lax.axis_size(axis), lambda source, state: join(state, take(source)), take(0)
    )


def expert_full(row_block, gate_part, up_part, down_part):
    gate_val = jnp.einsum(
        "sjkd,jdf->sjkf", row_block, gate_part, preferred_element_type=jnp.float32
    )
    up_val = jnp.einsum("sjkd,jdf->sjkf", row_block, up_part, preferred_element_type=jnp.float32)
    act = (jax.nn.silu(gate_val) * up_val).astype(jnp.bfloat16)
    return jnp.einsum("sjkf,jfd->sjkd", act, down_part, preferred_element_type=jnp.float32)


def full_weights(gate_w, up_w, down_w):
    kv_count = lax.axis_size("kv")
    if kv_count != 2:
        return (
            lax.all_gather(gate_w[0], "kv", axis=1, tiled=True),
            lax.all_gather(up_w[0], "kv", axis=1, tiled=True),
            lax.all_gather(down_w[0], "kv", axis=0, tiled=True),
        )
    hidden = gate_w.shape[2]
    packed = jnp.stack([gate_w[0], up_w[0], down_w[0].reshape(-1, hidden)])
    other = lax.ppermute(packed, "kv", [(0, 1), (1, 0)])
    first = lax.axis_index("kv") == 0
    joined = []
    for slot, axis in zip(range(3), (1, 1, 0)):
        own, far = packed[slot], other[slot]
        if axis == 0:
            own, far = own.reshape(hidden, -1), far.reshape(hidden, -1)
        low = jnp.where(first, own, far)
        high = jnp.where(first, far, own)
        joined.append(jnp.concatenate([low, high], axis=axis))
    return tuple(joined)


def dense_moe(plan, normed, route_ids, route_weights, weight_parts, anchor):
    expert_count = EXP_DEV * lax.axis_size("ep")
    experts = jnp.arange(expert_count, dtype=jnp.int32)
    own_expert = lax.axis_index("ep")
    chosen = route_ids[:, :, None] == experts[None, None, :]
    weight_table = jnp.sum(jnp.where(chosen, route_weights[:, :, None], 0.0), axis=1)
    weight_parts, anchor = lax.optimization_barrier((weight_parts, anchor))
    full = list(full_weights(*weight_parts))

    def expert(rows, table):
        weights = jnp.sum(jnp.where(experts == own_expert, table, 0.0), axis=1)
        gate_val = jnp.dot(rows, full[0], preferred_element_type=jnp.float32)
        up_val = jnp.dot(rows, full[1], preferred_element_type=jnp.float32)
        act = (jax.nn.silu(gate_val) * up_val).astype(jnp.bfloat16)
        out_rows = jnp.dot(act, full[2], preferred_element_type=jnp.float32)
        out_rows = out_rows.astype(jnp.bfloat16).astype(jnp.float32)
        return out_rows * weights[:, None]

    pieces = [((normed, weight_table), None, None)]
    groups = []
    low = 0
    tie_at = next((n + 1 for n, (_, ends) in enumerate(plan) if ends), 0)
    first_wave = [
        [lax.ppermute(pieces[0][0], "ep", pairs) for pairs in pairs_list] for pairs_list, _ in plan
    ]
    first_wave = lax.optimization_barrier(first_wave)
    for number, (pairs_list, ends) in enumerate(plan):
        grown = []
        for parent, (block, _, _) in enumerate(pieces):
            for slot, pairs in enumerate(pairs_list):
                if parent == 0:
                    grown.append((first_wave[number][slot], parent, pairs))
                else:
                    grown.append((lax.ppermute(block, "ep", pairs), parent, pairs))
        if number == tie_at:
            tied = lax.optimization_barrier((tuple(full), grown[-1][0]))
            full = list(tied[0])
            grown[-1] = (tied[1],) + grown[-1][1:]
        pieces = pieces + grown
        if ends:
            groups.append((low, len(pieces)))
            low = len(pieces)
    if low < len(pieces) or not groups:
        groups.append((low, len(pieces)))
    partial = [None] * len(pieces)
    size = normed.shape[0]
    ordered = []
    for low, high in reversed(groups):
        members = list(range(low, high))
        if len(members) >= 8:
            half = len(members) // 2
            ordered += [members[:half], members[half:]]
        else:
            ordered.append(members)
    for members in ordered:
        rows = jnp.concatenate([pieces[i][0][0] for i in members], axis=0)
        table = jnp.concatenate([pieces[i][0][1] for i in members], axis=0)
        out = expert(rows, table)
        for offset, i in enumerate(members):
            partial[i] = out[offset * size:(offset + 1) * size]
    for index in reversed(range(1, len(pieces))):
        _, parent, pairs = pieces[index]
        back = [(target, source) for source, target in pairs]
        sent = lax.ppermute(partial[index].astype(jnp.bfloat16), "ep", back)
        partial[parent] = partial[parent] + sent.astype(jnp.float32)
    return partial[0], anchor


def gather_plan(mesh, shapes):
    kv_count, ep_count = mesh.devices.shape
    rows = ep_count * shapes[0][1] // kv_count
    if EXP_DEV != 1 or shapes[12][0] != ep_count or rows > 4096:
        return None
    places = []
    for device in mesh.devices[0]:
        coords = getattr(device, "coords", None)
        core = getattr(device, "core_on_chip", None)
        if coords is None or core is None:
            return None
        places.append(tuple(coords) + (core,))
    width = len(places[0])
    values = [sorted({p[a] for p in places}) for a in range(width)]
    varying = [a for a in range(width) if len(values[a]) > 1]
    total = 1
    for a in varying:
        total *= len(values[a])
    if total != ep_count or len(set(places)) != ep_count:
        return None
    rank_of = {p: r for r, p in enumerate(places)}
    core_axis = width - 1
    order = sorted((a for a in varying if a != core_axis), key=lambda a: -len(values[a]))
    order += [a for a in varying if a == core_axis]
    plan = []
    for a in order:
        size = len(values[a])
        if size & (size - 1) == 0:
            steps = []
            span = size // 2
            while span:
                steps.append(("xor", span))
                span //= 2
        else:
            steps = [("shift", shift) for shift in range(1, size)]
            steps = [steps]
        for number, step in enumerate(steps):
            group = step if isinstance(step, list) else [step]
            stage = []
            for kind, amount in group:
                pairs = []
                for r, p in enumerate(places):
                    index = values[a].index(p[a])
                    moved = list(p)
                    moved[a] = values[a][index ^ amount if kind == "xor" else (index + amount) % size]
                    pairs.append((r, rank_of[tuple(moved)]))
                stage.append(pairs)
            plan.append((stage, number == len(steps) - 1))
    return plan


def joined_attention(queries, new_keys, new_values, cache_keys, cache_values, length):
    kv_rank = lax.axis_index("kv")
    tok_dev = queries.shape[1]
    cl_dev = cache_keys.shape[1]
    feat = queries.shape[2]
    head_count = feat // HEAD_DIM
    score_scale = 1.0 / math.sqrt(HEAD_DIM)
    every_query = lax.all_gather(queries[0], "kv", axis=0, tiled=True)
    new_total = every_query.shape[0]
    query_heads = every_query.reshape(new_total, head_count, HEAD_DIM)
    key_cache = cache_keys[0].reshape(cl_dev, head_count, HEAD_DIM)
    value_cache = cache_values[0].reshape(cl_dev, head_count, HEAD_DIM)
    key_new = new_keys[0].reshape(tok_dev, head_count, HEAD_DIM)
    value_new = new_values[0].reshape(tok_dev, head_count, HEAD_DIM)
    score_cache = (
        jnp.einsum("qhd,khd->qhk", query_heads, key_cache, preferred_element_type=jnp.float32)
        * score_scale
    )
    position = kv_rank * cl_dev + jnp.arange(cl_dev, dtype=jnp.int32)
    score_cache = jnp.where((position < length)[None, None, :], score_cache, -jnp.inf)
    score_new = (
        jnp.einsum("qhd,khd->qhk", query_heads, key_new, preferred_element_type=jnp.float32)
        * score_scale
    )
    local_top = jnp.maximum(jnp.max(score_cache, axis=-1), jnp.max(score_new, axis=-1))
    expo_cache = jnp.exp(score_cache - local_top[..., None])
    expo_new = jnp.exp(score_new - local_top[..., None])
    denom = jnp.sum(expo_cache, axis=-1) + jnp.sum(expo_new, axis=-1)
    summed = jnp.einsum(
        "qhk,khd->qhd",
        expo_cache.astype(jnp.bfloat16),
        value_cache,
        preferred_element_type=jnp.float32,
    )
    summed = summed + jnp.einsum(
        "qhk,khd->qhd", expo_new.astype(jnp.bfloat16), value_new, preferred_element_type=jnp.float32
    )
    summed, denom = (summed.reshape(new_total, feat), denom)

    def join(first, second):
        first_top, first_denom, first_sum = first
        second_top, second_denom, second_sum = second
        joint_top = jnp.maximum(first_top, second_top)
        first_factor = jnp.exp(first_top - joint_top)
        second_factor = jnp.exp(second_top - joint_top)
        rows_here = first_sum.shape[0]
        joint_sum = (
            first_sum.reshape(rows_here, head_count, HEAD_DIM) * first_factor[..., None]
            + second_sum.reshape(rows_here, head_count, HEAD_DIM) * second_factor[..., None]
        )
        return (
            joint_top,
            first_denom * first_factor + second_denom * second_factor,
            joint_sum.reshape(rows_here, feat),
        )

    joint_top, joint_denom, joint_sum = combined_all((local_top, denom, summed), "kv", join)
    row_start = kv_rank * tok_dev
    own_sum = lax.dynamic_slice_in_dim(joint_sum, row_start, tok_dev, 0)
    own_denom = lax.dynamic_slice_in_dim(joint_denom, row_start, tok_dev, 0)
    attended = (
        (own_sum.reshape(tok_dev, head_count, HEAD_DIM) / own_denom[..., None])
        .reshape(tok_dev, feat)
        .astype(jnp.bfloat16)
    )
    return attended


def partial_softmax(query_rows, key_cache, value_cache, key_new, value_new, usable):
    rows, feat = query_rows.shape
    head_count = feat // HEAD_DIM
    score_scale = 1.0 / math.sqrt(HEAD_DIM)
    query_heads = query_rows.reshape(rows, head_count, HEAD_DIM)
    score_cache = (
        jnp.einsum("qhd,khd->qhk", query_heads, key_cache, preferred_element_type=jnp.float32)
        * score_scale
    )
    score_cache = jnp.where(usable[None, None, :], score_cache, -jnp.inf)
    score_new = (
        jnp.einsum("qhd,khd->qhk", query_heads, key_new, preferred_element_type=jnp.float32)
        * score_scale
    )
    top = jnp.maximum(jnp.max(score_cache, axis=-1), jnp.max(score_new, axis=-1))
    expo_cache = jnp.exp(score_cache - top[..., None])
    expo_new = jnp.exp(score_new - top[..., None])
    denom = jnp.sum(expo_cache, axis=-1) + jnp.sum(expo_new, axis=-1)
    summed = jnp.einsum(
        "qhk,khd->qhd", expo_cache.astype(jnp.bfloat16), value_cache,
        preferred_element_type=jnp.float32,
    )
    summed = summed + jnp.einsum(
        "qhk,khd->qhd", expo_new.astype(jnp.bfloat16), value_new, preferred_element_type=jnp.float32
    )
    return top, denom, summed


def paired_attention(own_queries, key_new, value_new, key_cache, value_cache, length):
    kv_rank = lax.axis_index("kv")
    swap = [(0, 1), (1, 0)]
    tok_dev, feat = own_queries.shape
    cl_dev = key_cache.shape[0]
    head_count = feat // HEAD_DIM
    far_queries = lax.ppermute(own_queries, "kv", swap)
    key_cache = key_cache.reshape(cl_dev, head_count, HEAD_DIM)
    value_cache = value_cache.reshape(cl_dev, head_count, HEAD_DIM)
    key_new = key_new.reshape(tok_dev, head_count, HEAD_DIM)
    value_new = value_new.reshape(tok_dev, head_count, HEAD_DIM)
    position = kv_rank * cl_dev + jnp.arange(cl_dev, dtype=jnp.int32)
    usable = position < length
    operands = (key_cache, value_cache, key_new, value_new, usable)
    own_top, own_denom, own_sum = partial_softmax(own_queries, *operands)
    far_top, far_denom, far_sum = partial_softmax(far_queries, *operands)
    back_top, back_denom, back_sum = lax.ppermute(
        (far_top, far_denom, far_sum.astype(jnp.bfloat16)), "kv", swap
    )
    joint_top = jnp.maximum(own_top, back_top)
    own_factor = jnp.exp(own_top - joint_top)
    back_factor = jnp.exp(back_top - joint_top)
    joint_sum = own_sum * own_factor[..., None] + back_sum.astype(jnp.float32) * back_factor[..., None]
    joint_denom = own_denom * own_factor + back_denom * back_factor
    return (joint_sum / joint_denom[..., None]).reshape(tok_dev, feat).astype(jnp.bfloat16)


def shards(
    plan,
    resid,
    queries,
    new_keys,
    new_values,
    cache_keys,
    cache_values,
    cached_len,
    group_request,
    w_out,
    norm_gain,
    route_ids,
    route_weights,
    gate_w,
    up_w,
    down_w,
):
    kv_rank = lax.axis_index("kv")
    ep_count = lax.axis_size("ep")
    tok_dev = resid.shape[1]
    cl_dev = cache_keys.shape[1]
    feat = queries.shape[2]
    head_count = feat // HEAD_DIM
    score_scale = 1.0 / math.sqrt(HEAD_DIM)
    request_index = jnp.arange(cached_len.shape[0], dtype=jnp.int32)
    length = jnp.sum(jnp.where(request_index == group_request[0], cached_len, 0))
    if lax.axis_size("kv") == 2 and plan is not None:
        attended = paired_attention(
            queries[0], new_keys[0], new_values[0], cache_keys[0], cache_values[0], length
        )
    else:
        attended = joined_attention(
            queries, new_keys, new_values, cache_keys, cache_values, length
        )
    proj = jnp.dot(attended, w_out, preferred_element_type=jnp.float32)
    hidden = (resid[0].astype(jnp.float32) + proj).astype(jnp.bfloat16)
    hidden_f = hidden.astype(jnp.float32)
    normed = (
        hidden_f
        * lax.rsqrt(jnp.mean(hidden_f * hidden_f, axis=-1, keepdims=True) + 1e-06)
        * norm_gain.astype(jnp.float32)
    ).astype(jnp.bfloat16)
    if plan is not None:
        moe_sum, _ = dense_moe(
            plan, normed, route_ids[0], route_weights[0], (gate_w, up_w, down_w), attended
        )
        return (hidden_f + moe_sum).astype(jnp.bfloat16)[None]
    expert_count = EXP_DEV * ep_count
    capacity = min(tok_dev, max(2, tok_dev * TOP * 3 // (2 * expert_count)))
    route_flat = route_ids[0].reshape(-1)
    one_hot = (route_flat[:, None] == jnp.arange(expert_count, dtype=jnp.int32)[None, :]).astype(
        jnp.int32
    )
    rank_in = jnp.sum((jnp.cumsum(one_hot, axis=0) - 1) * one_hot, axis=1)
    slot_of = route_flat * capacity + rank_in
    slot_index = jnp.arange(expert_count * capacity, dtype=jnp.int32)
    placing = jnp.sum(
        (slot_of.reshape(tok_dev, TOP)[None, :, :] == slot_index[:, None, None]).astype(jnp.int32),
        axis=-1,
    ).astype(jnp.bfloat16)
    outgoing = jnp.dot(placing, normed, preferred_element_type=jnp.float32).astype(jnp.bfloat16)
    outgoing = outgoing.reshape(ep_count, EXP_DEV, capacity, D)
    full_gate, full_up, full_down = (
        lax.all_gather(gate_w, "kv", axis=2, tiled=True),
        lax.all_gather(up_w, "kv", axis=2, tiled=True),
        lax.all_gather(down_w, "kv", axis=1, tiled=True),
    )
    expert_out = expert_full(
        lax.all_to_all(outgoing, "ep", split_axis=0, concat_axis=0, tiled=True),
        full_gate,
        full_up,
        full_down,
    ).astype(jnp.bfloat16)
    returned = lax.all_to_all(expert_out, "ep", split_axis=0, concat_axis=0, tiled=True).reshape(
        expert_count * capacity, D
    )
    picked = jnp.take(returned, slot_of, axis=0).reshape(tok_dev, TOP, D)
    moe_sum = jnp.sum(picked.astype(jnp.float32) * route_weights[0][..., None], axis=1)
    return (hidden_f + moe_sum).astype(jnp.bfloat16)[None]


def solution(mesh):
    placed = (
        P("ep", "kv", None),
        P("ep", "kv", None),
        P("ep", "kv", None),
        P("ep", "kv", None),
        P("ep", "kv", None),
        P("ep", "kv", None),
        P(),
        P("ep"),
        P(),
        P(),
        P("ep", "kv", None),
        P("ep", "kv", None),
        P("ep", None, "kv"),
        P("ep", None, "kv"),
        P("ep", "kv", None),
    )

    def run(*args):
        plan = gather_plan(mesh, [a.shape for a in args])
        body = functools.partial(shards, plan)
        return jax.shard_map(
            body, mesh=mesh, in_specs=placed, out_specs=P("ep", "kv", None), check_vma=False
        )(*args)

    return run
```

```python
import functools
import math

import jax
import jax.numpy as jnp
import numpy as np
from jax import lax
from jax.sharding import PartitionSpec as P

D = 2048
HEAD_DIM = 128
TOP = 8
EXP_DEV = 1


def combined_all(shard, axis, join):
    gathered = jax.tree.map(
        lambda a, kind: lax.all_gather(a.astype(kind), axis),
        shard,
        (jnp.bfloat16, jnp.bfloat16, jnp.bfloat16),
    )

    def take(source):
        return jax.tree.map(
            lambda a, own: lax.dynamic_index_in_dim(a, source, 0, False).astype(own.dtype),
            gathered,
            shard,
        )

    return lax.fori_loop(
        1, lax.axis_size(axis), lambda source, state: join(state, take(source)), take(0)
    )


def expert_full(row_block, gate_part, up_part, down_part):
    gate_val = jnp.einsum(
        "sjkd,jdf->sjkf", row_block, gate_part, preferred_element_type=jnp.float32
    )
    up_val = jnp.einsum("sjkd,jdf->sjkf", row_block, up_part, preferred_element_type=jnp.float32)
    act = (jax.nn.silu(gate_val) * up_val).astype(jnp.bfloat16)
    return jnp.einsum("sjkf,jfd->sjkd", act, down_part, preferred_element_type=jnp.float32)


def full_weights(gate_w, up_w, down_w):
    kv_count = lax.axis_size("kv")
    if kv_count != 2:
        return (
            lax.all_gather(gate_w[0], "kv", axis=1, tiled=True),
            lax.all_gather(up_w[0], "kv", axis=1, tiled=True),
            lax.all_gather(down_w[0], "kv", axis=0, tiled=True),
        )
    hidden = gate_w.shape[2]
    packed = jnp.stack([gate_w[0], up_w[0], down_w[0].reshape(-1, hidden)])
    other = lax.ppermute(packed, "kv", [(0, 1), (1, 0)])
    first = lax.axis_index("kv") == 0
    joined = []
    for slot, axis in zip(range(3), (1, 1, 0)):
        own, far = packed[slot], other[slot]
        if axis == 0:
            own, far = own.reshape(hidden, -1), far.reshape(hidden, -1)
        low = jnp.where(first, own, far)
        high = jnp.where(first, far, own)
        joined.append(jnp.concatenate([low, high], axis=axis))
    return tuple(joined)


def dense_moe(plan, normed, route_ids, route_weights, weight_parts, anchor):
    expert_count = EXP_DEV * lax.axis_size("ep")
    experts = jnp.arange(expert_count, dtype=jnp.int32)
    own_expert = lax.axis_index("ep")
    chosen = route_ids[:, :, None] == experts[None, None, :]
    weight_table = jnp.sum(jnp.where(chosen, route_weights[:, :, None], 0.0), axis=1)
    weight_parts, anchor = lax.optimization_barrier((weight_parts, anchor))
    full = list(full_weights(*weight_parts))

    def expert(rows, table):
        weights = jnp.sum(jnp.where(experts == own_expert, table, 0.0), axis=1)
        gate_val = jnp.dot(rows, full[0], preferred_element_type=jnp.float32)
        up_val = jnp.dot(rows, full[1], preferred_element_type=jnp.float32)
        act = (jax.nn.silu(gate_val) * up_val).astype(jnp.bfloat16)
        out_rows = jnp.dot(act, full[2], preferred_element_type=jnp.float32)
        out_rows = out_rows.astype(jnp.bfloat16).astype(jnp.float32)
        return out_rows * weights[:, None]

    pieces = [((normed, weight_table), None, None)]
    groups = []
    low = 0
    tie_at = next((n + 1 for n, (_, ends) in enumerate(plan) if ends), 0)
    first_wave = [
        [lax.ppermute(pieces[0][0], "ep", pairs) for pairs in pairs_list] for pairs_list, _ in plan
    ]
    first_wave = lax.optimization_barrier(first_wave)
    for number, (pairs_list, ends) in enumerate(plan):
        grown = []
        for parent, (block, _, _) in enumerate(pieces):
            for slot, pairs in enumerate(pairs_list):
                if parent == 0:
                    grown.append((first_wave[number][slot], parent, pairs))
                else:
                    grown.append((lax.ppermute(block, "ep", pairs), parent, pairs))
        if number == tie_at:
            tied = lax.optimization_barrier((tuple(full), grown[-1][0]))
            full = list(tied[0])
            grown[-1] = (tied[1],) + grown[-1][1:]
        pieces = pieces + grown
        if ends:
            groups.append((low, len(pieces)))
            low = len(pieces)
    if low < len(pieces) or not groups:
        groups.append((low, len(pieces)))
    partial = [None] * len(pieces)
    size = normed.shape[0]
    ordered = []
    for low, high in reversed(groups):
        members = list(range(low, high))
        if len(members) >= 4:
            half = len(members) // 2
            ordered += [members[:half], members[half:]]
        else:
            ordered.append(members)
    for members in ordered:
        rows = jnp.concatenate([pieces[i][0][0] for i in members], axis=0)
        table = jnp.concatenate([pieces[i][0][1] for i in members], axis=0)
        out = expert(rows, table)
        for offset, i in enumerate(members):
            partial[i] = out[offset * size:(offset + 1) * size]
    for index in reversed(range(1, len(pieces))):
        _, parent, pairs = pieces[index]
        back = [(target, source) for source, target in pairs]
        sent = lax.ppermute(partial[index].astype(jnp.bfloat16), "ep", back)
        partial[parent] = partial[parent] + sent.astype(jnp.float32)
    return partial[0], anchor


def gather_plan(mesh, shapes):
    kv_count, ep_count = mesh.devices.shape
    rows = ep_count * shapes[0][1] // kv_count
    if EXP_DEV != 1 or shapes[12][0] != ep_count or rows > 4096:
        return None
    places = []
    for device in mesh.devices[0]:
        coords = getattr(device, "coords", None)
        core = getattr(device, "core_on_chip", None)
        if coords is None or core is None:
            return None
        places.append(tuple(coords) + (core,))
    width = len(places[0])
    values = [sorted({p[a] for p in places}) for a in range(width)]
    varying = [a for a in range(width) if len(values[a]) > 1]
    total = 1
    for a in varying:
        total *= len(values[a])
    if total != ep_count or len(set(places)) != ep_count:
        return None
    rank_of = {p: r for r, p in enumerate(places)}
    core_axis = width - 1
    order = sorted((a for a in varying if a != core_axis), key=lambda a: -len(values[a]))
    order += [a for a in varying if a == core_axis]
    plan = []
    for a in order:
        size = len(values[a])
        if size & (size - 1) == 0:
            steps = []
            span = size // 2
            while span:
                steps.append(("xor", span))
                span //= 2
        else:
            steps = [("shift", shift) for shift in range(1, size)]
            steps = [steps]
        for number, step in enumerate(steps):
            group = step if isinstance(step, list) else [step]
            stage = []
            for kind, amount in group:
                pairs = []
                for r, p in enumerate(places):
                    index = values[a].index(p[a])
                    moved = list(p)
                    moved[a] = values[a][index ^ amount if kind == "xor" else (index + amount) % size]
                    pairs.append((r, rank_of[tuple(moved)]))
                stage.append(pairs)
            plan.append((stage, number == len(steps) - 1))
    return plan


def joined_attention(queries, new_keys, new_values, cache_keys, cache_values, length):
    kv_rank = lax.axis_index("kv")
    tok_dev = queries.shape[1]
    cl_dev = cache_keys.shape[1]
    feat = queries.shape[2]
    head_count = feat // HEAD_DIM
    score_scale = 1.0 / math.sqrt(HEAD_DIM)
    every_query = lax.all_gather(queries[0], "kv", axis=0, tiled=True)
    new_total = every_query.shape[0]
    query_heads = every_query.reshape(new_total, head_count, HEAD_DIM)
    key_cache = cache_keys[0].reshape(cl_dev, head_count, HEAD_DIM)
    value_cache = cache_values[0].reshape(cl_dev, head_count, HEAD_DIM)
    key_new = new_keys[0].reshape(tok_dev, head_count, HEAD_DIM)
    value_new = new_values[0].reshape(tok_dev, head_count, HEAD_DIM)
    score_cache = (
        jnp.einsum("qhd,khd->qhk", query_heads, key_cache, preferred_element_type=jnp.float32)
        * score_scale
    )
    position = kv_rank * cl_dev + jnp.arange(cl_dev, dtype=jnp.int32)
    score_cache = jnp.where((position < length)[None, None, :], score_cache, -jnp.inf)
    score_new = (
        jnp.einsum("qhd,khd->qhk", query_heads, key_new, preferred_element_type=jnp.float32)
        * score_scale
    )
    local_top = jnp.maximum(jnp.max(score_cache, axis=-1), jnp.max(score_new, axis=-1))
    expo_cache = jnp.exp(score_cache - local_top[..., None])
    expo_new = jnp.exp(score_new - local_top[..., None])
    denom = jnp.sum(expo_cache, axis=-1) + jnp.sum(expo_new, axis=-1)
    summed = jnp.einsum(
        "qhk,khd->qhd",
        expo_cache.astype(jnp.bfloat16),
        value_cache,
        preferred_element_type=jnp.float32,
    )
    summed = summed + jnp.einsum(
        "qhk,khd->qhd", expo_new.astype(jnp.bfloat16), value_new, preferred_element_type=jnp.float32
    )
    summed, denom = (summed.reshape(new_total, feat), denom)

    def join(first, second):
        first_top, first_denom, first_sum = first
        second_top, second_denom, second_sum = second
        joint_top = jnp.maximum(first_top, second_top)
        first_factor = jnp.exp(first_top - joint_top)
        second_factor = jnp.exp(second_top - joint_top)
        rows_here = first_sum.shape[0]
        joint_sum = (
            first_sum.reshape(rows_here, head_count, HEAD_DIM) * first_factor[..., None]
            + second_sum.reshape(rows_here, head_count, HEAD_DIM) * second_factor[..., None]
        )
        return (
            joint_top,
            first_denom * first_factor + second_denom * second_factor,
            joint_sum.reshape(rows_here, feat),
        )

    joint_top, joint_denom, joint_sum = combined_all((local_top, denom, summed), "kv", join)
    row_start = kv_rank * tok_dev
    own_sum = lax.dynamic_slice_in_dim(joint_sum, row_start, tok_dev, 0)
    own_denom = lax.dynamic_slice_in_dim(joint_denom, row_start, tok_dev, 0)
    attended = (
        (own_sum.reshape(tok_dev, head_count, HEAD_DIM) / own_denom[..., None])
        .reshape(tok_dev, feat)
        .astype(jnp.bfloat16)
    )
    return attended


def partial_softmax(query_rows, key_cache, value_cache, key_new, value_new, usable):
    rows, feat = query_rows.shape
    head_count = feat // HEAD_DIM
    score_scale = 1.0 / math.sqrt(HEAD_DIM)
    query_heads = query_rows.reshape(rows, head_count, HEAD_DIM)
    score_cache = (
        jnp.einsum("qhd,khd->qhk", query_heads, key_cache, preferred_element_type=jnp.float32)
        * score_scale
    )
    score_cache = jnp.where(usable[None, None, :], score_cache, -jnp.inf)
    score_new = (
        jnp.einsum("qhd,khd->qhk", query_heads, key_new, preferred_element_type=jnp.float32)
        * score_scale
    )
    top = jnp.maximum(jnp.max(score_cache, axis=-1), jnp.max(score_new, axis=-1))
    expo_cache = jnp.exp(score_cache - top[..., None])
    expo_new = jnp.exp(score_new - top[..., None])
    denom = jnp.sum(expo_cache, axis=-1) + jnp.sum(expo_new, axis=-1)
    summed = jnp.einsum(
        "qhk,khd->qhd", expo_cache.astype(jnp.bfloat16), value_cache,
        preferred_element_type=jnp.float32,
    )
    summed = summed + jnp.einsum(
        "qhk,khd->qhd", expo_new.astype(jnp.bfloat16), value_new, preferred_element_type=jnp.float32
    )
    return top, denom, summed


def paired_attention(own_queries, key_new, value_new, key_cache, value_cache, length):
    kv_rank = lax.axis_index("kv")
    swap = [(0, 1), (1, 0)]
    tok_dev, feat = own_queries.shape
    cl_dev = key_cache.shape[0]
    head_count = feat // HEAD_DIM
    far_queries = lax.ppermute(own_queries, "kv", swap)
    key_cache = key_cache.reshape(cl_dev, head_count, HEAD_DIM)
    value_cache = value_cache.reshape(cl_dev, head_count, HEAD_DIM)
    key_new = key_new.reshape(tok_dev, head_count, HEAD_DIM)
    value_new = value_new.reshape(tok_dev, head_count, HEAD_DIM)
    position = kv_rank * cl_dev + jnp.arange(cl_dev, dtype=jnp.int32)
    usable = position < length
    operands = (key_cache, value_cache, key_new, value_new, usable)
    own_top, own_denom, own_sum = partial_softmax(own_queries, *operands)
    far_top, far_denom, far_sum = partial_softmax(far_queries, *operands)
    back_top, back_denom, back_sum = lax.ppermute(
        (far_top, far_denom, far_sum.astype(jnp.bfloat16)), "kv", swap
    )
    joint_top = jnp.maximum(own_top, back_top)
    own_factor = jnp.exp(own_top - joint_top)
    back_factor = jnp.exp(back_top - joint_top)
    joint_sum = own_sum * own_factor[..., None] + back_sum.astype(jnp.float32) * back_factor[..., None]
    joint_denom = own_denom * own_factor + back_denom * back_factor
    return (joint_sum / joint_denom[..., None]).reshape(tok_dev, feat).astype(jnp.bfloat16)


def shards(
    plan,
    resid,
    queries,
    new_keys,
    new_values,
    cache_keys,
    cache_values,
    cached_len,
    group_request,
    w_out,
    norm_gain,
    route_ids,
    route_weights,
    gate_w,
    up_w,
    down_w,
):
    kv_rank = lax.axis_index("kv")
    ep_count = lax.axis_size("ep")
    tok_dev = resid.shape[1]
    cl_dev = cache_keys.shape[1]
    feat = queries.shape[2]
    head_count = feat // HEAD_DIM
    score_scale = 1.0 / math.sqrt(HEAD_DIM)
    request_index = jnp.arange(cached_len.shape[0], dtype=jnp.int32)
    length = jnp.sum(jnp.where(request_index == group_request[0], cached_len, 0))
    if lax.axis_size("kv") == 2 and plan is not None:
        attended = paired_attention(
            queries[0], new_keys[0], new_values[0], cache_keys[0], cache_values[0], length
        )
    else:
        attended = joined_attention(
            queries, new_keys, new_values, cache_keys, cache_values, length
        )
    proj = jnp.dot(attended, w_out, preferred_element_type=jnp.float32)
    hidden = (resid[0].astype(jnp.float32) + proj).astype(jnp.bfloat16)
    hidden_f = hidden.astype(jnp.float32)
    normed = (
        hidden_f
        * lax.rsqrt(jnp.mean(hidden_f * hidden_f, axis=-1, keepdims=True) + 1e-06)
        * norm_gain.astype(jnp.float32)
    ).astype(jnp.bfloat16)
    if plan is not None:
        moe_sum, _ = dense_moe(
            plan, normed, route_ids[0], route_weights[0], (gate_w, up_w, down_w), attended
        )
        return (hidden_f + moe_sum).astype(jnp.bfloat16)[None]
    expert_count = EXP_DEV * ep_count
    capacity = min(tok_dev, max(2, tok_dev * TOP * 3 // (2 * expert_count)))
    route_flat = route_ids[0].reshape(-1)
    one_hot = (route_flat[:, None] == jnp.arange(expert_count, dtype=jnp.int32)[None, :]).astype(
        jnp.int32
    )
    rank_in = jnp.sum((jnp.cumsum(one_hot, axis=0) - 1) * one_hot, axis=1)
    slot_of = route_flat * capacity + rank_in
    slot_index = jnp.arange(expert_count * capacity, dtype=jnp.int32)
    placing = jnp.sum(
        (slot_of.reshape(tok_dev, TOP)[None, :, :] == slot_index[:, None, None]).astype(jnp.int32),
        axis=-1,
    ).astype(jnp.bfloat16)
    outgoing = jnp.dot(placing, normed, preferred_element_type=jnp.float32).astype(jnp.bfloat16)
    outgoing = outgoing.reshape(ep_count, EXP_DEV, capacity, D)
    full_gate, full_up, full_down = (
        lax.all_gather(gate_w, "kv", axis=2, tiled=True),
        lax.all_gather(up_w, "kv", axis=2, tiled=True),
        lax.all_gather(down_w, "kv", axis=1, tiled=True),
    )
    expert_out = expert_full(
        lax.all_to_all(outgoing, "ep", split_axis=0, concat_axis=0, tiled=True),
        full_gate,
        full_up,
        full_down,
    ).astype(jnp.bfloat16)
    returned = lax.all_to_all(expert_out, "ep", split_axis=0, concat_axis=0, tiled=True).reshape(
        expert_count * capacity, D
    )
    picked = jnp.take(returned, slot_of, axis=0).reshape(tok_dev, TOP, D)
    moe_sum = jnp.sum(picked.astype(jnp.float32) * route_weights[0][..., None], axis=1)
    return (hidden_f + moe_sum).astype(jnp.bfloat16)[None]


def solution(mesh):
    placed = (
        P("ep", "kv", None),
        P("ep", "kv", None),
        P("ep", "kv", None),
        P("ep", "kv", None),
        P("ep", "kv", None),
        P("ep", "kv", None),
        P(),
        P("ep"),
        P(),
        P(),
        P("ep", "kv", None),
        P("ep", "kv", None),
        P("ep", None, "kv"),
        P("ep", None, "kv"),
        P("ep", "kv", None),
    )

    def run(*args):
        plan = gather_plan(mesh, [a.shape for a in args])
        body = functools.partial(shards, plan)
        return jax.shard_map(
            body, mesh=mesh, in_specs=placed, out_specs=P("ep", "kv", None), check_vma=False
        )(*args)

    return run
```

```python
import functools
import math

import jax
import jax.numpy as jnp
import numpy as np
from jax import lax
from jax.sharding import PartitionSpec as P

D = 2048
HEAD_DIM = 128
TOP = 8
EXP_DEV = 1


def combined_all(shard, axis, join):
    gathered = jax.tree.map(
        lambda a, kind: lax.all_gather(a.astype(kind), axis),
        shard,
        (jnp.bfloat16, jnp.bfloat16, jnp.bfloat16),
    )

    def take(source):
        return jax.tree.map(
            lambda a, own: lax.dynamic_index_in_dim(a, source, 0, False).astype(own.dtype),
            gathered,
            shard,
        )

    return lax.fori_loop(
        1, lax.axis_size(axis), lambda source, state: join(state, take(source)), take(0)
    )


def expert_full(row_block, gate_part, up_part, down_part):
    gate_val = jnp.einsum(
        "sjkd,jdf->sjkf", row_block, gate_part, preferred_element_type=jnp.float32
    )
    up_val = jnp.einsum("sjkd,jdf->sjkf", row_block, up_part, preferred_element_type=jnp.float32)
    act = (jax.nn.silu(gate_val) * up_val).astype(jnp.bfloat16)
    return jnp.einsum("sjkf,jfd->sjkd", act, down_part, preferred_element_type=jnp.float32)


def full_weights(gate_w, up_w, down_w):
    kv_count = lax.axis_size("kv")
    if kv_count != 2:
        return (
            lax.all_gather(gate_w[0], "kv", axis=1, tiled=True),
            lax.all_gather(up_w[0], "kv", axis=1, tiled=True),
            lax.all_gather(down_w[0], "kv", axis=0, tiled=True),
        )
    hidden = gate_w.shape[2]
    packed = jnp.stack([gate_w[0], up_w[0], down_w[0].reshape(-1, hidden)])
    other = lax.ppermute(packed, "kv", [(0, 1), (1, 0)])
    first = lax.axis_index("kv") == 0
    joined = []
    for slot, axis in zip(range(3), (1, 1, 0)):
        own, far = packed[slot], other[slot]
        if axis == 0:
            own, far = own.reshape(hidden, -1), far.reshape(hidden, -1)
        low = jnp.where(first, own, far)
        high = jnp.where(first, far, own)
        joined.append(jnp.concatenate([low, high], axis=axis))
    return tuple(joined)


def dense_moe(plan, normed, route_ids, route_weights, weight_parts, anchor):
    expert_count = EXP_DEV * lax.axis_size("ep")
    experts = jnp.arange(expert_count, dtype=jnp.int32)
    own_expert = lax.axis_index("ep")
    chosen = route_ids[:, :, None] == experts[None, None, :]
    weight_table = jnp.sum(jnp.where(chosen, route_weights[:, :, None], 0.0), axis=1)
    weight_parts, anchor = lax.optimization_barrier((weight_parts, anchor))
    full = list(full_weights(*weight_parts))

    def expert(rows, table):
        weights = jnp.sum(jnp.where(experts == own_expert, table, 0.0), axis=1)
        gate_val = jnp.dot(rows, full[0], preferred_element_type=jnp.float32)
        up_val = jnp.dot(rows, full[1], preferred_element_type=jnp.float32)
        act = (jax.nn.silu(gate_val) * up_val).astype(jnp.bfloat16)
        out_rows = jnp.dot(act, full[2], preferred_element_type=jnp.float32)
        out_rows = out_rows.astype(jnp.bfloat16).astype(jnp.float32)
        return out_rows * weights[:, None]

    pieces = [((normed, weight_table), None, None)]
    groups = []
    low = 0
    tie_at = next((n + 1 for n, (_, ends) in enumerate(plan) if ends), 0)
    first_wave = [
        [lax.ppermute(pieces[0][0], "ep", pairs) for pairs in pairs_list] for pairs_list, _ in plan
    ]
    first_wave = lax.optimization_barrier(first_wave)
    for number, (pairs_list, ends) in enumerate(plan):
        grown = []
        for parent, (block, _, _) in enumerate(pieces):
            for slot, pairs in enumerate(pairs_list):
                if parent == 0:
                    grown.append((first_wave[number][slot], parent, pairs))
                else:
                    grown.append((lax.ppermute(block, "ep", pairs), parent, pairs))
        if number == tie_at:
            tied = lax.optimization_barrier((tuple(full), grown[-1][0]))
            full = list(tied[0])
            grown[-1] = (tied[1],) + grown[-1][1:]
        pieces = pieces + grown
        if ends:
            groups.append((low, len(pieces)))
            low = len(pieces)
    if low < len(pieces) or not groups:
        groups.append((low, len(pieces)))
    partial = [None] * len(pieces)
    size = normed.shape[0]
    ordered = []
    for low, high in reversed(groups):
        members = list(range(low, high))
        if len(members) >= 8:
            part = len(members) // 4
            ordered += [members[k:k + part] for k in range(0, len(members), part)]
        else:
            ordered.append(members)
    for members in ordered:
        rows = jnp.concatenate([pieces[i][0][0] for i in members], axis=0)
        table = jnp.concatenate([pieces[i][0][1] for i in members], axis=0)
        out = expert(rows, table)
        for offset, i in enumerate(members):
            partial[i] = out[offset * size:(offset + 1) * size]
    for index in reversed(range(1, len(pieces))):
        _, parent, pairs = pieces[index]
        back = [(target, source) for source, target in pairs]
        sent = lax.ppermute(partial[index].astype(jnp.bfloat16), "ep", back)
        partial[parent] = partial[parent] + sent.astype(jnp.float32)
    return partial[0], anchor


def gather_plan(mesh, shapes):
    kv_count, ep_count = mesh.devices.shape
    rows = ep_count * shapes[0][1] // kv_count
    if EXP_DEV != 1 or shapes[12][0] != ep_count or rows > 4096:
        return None
    places = []
    for device in mesh.devices[0]:
        coords = getattr(device, "coords", None)
        core = getattr(device, "core_on_chip", None)
        if coords is None or core is None:
            return None
        places.append(tuple(coords) + (core,))
    width = len(places[0])
    values = [sorted({p[a] for p in places}) for a in range(width)]
    varying = [a for a in range(width) if len(values[a]) > 1]
    total = 1
    for a in varying:
        total *= len(values[a])
    if total != ep_count or len(set(places)) != ep_count:
        return None
    rank_of = {p: r for r, p in enumerate(places)}
    core_axis = width - 1
    order = sorted((a for a in varying if a != core_axis), key=lambda a: -len(values[a]))
    order += [a for a in varying if a == core_axis]
    plan = []
    for a in order:
        size = len(values[a])
        if size & (size - 1) == 0:
            steps = []
            span = size // 2
            while span:
                steps.append(("xor", span))
                span //= 2
        else:
            steps = [("shift", shift) for shift in range(1, size)]
            steps = [steps]
        for number, step in enumerate(steps):
            group = step if isinstance(step, list) else [step]
            stage = []
            for kind, amount in group:
                pairs = []
                for r, p in enumerate(places):
                    index = values[a].index(p[a])
                    moved = list(p)
                    moved[a] = values[a][index ^ amount if kind == "xor" else (index + amount) % size]
                    pairs.append((r, rank_of[tuple(moved)]))
                stage.append(pairs)
            plan.append((stage, number == len(steps) - 1))
    return plan


def joined_attention(queries, new_keys, new_values, cache_keys, cache_values, length):
    kv_rank = lax.axis_index("kv")
    tok_dev = queries.shape[1]
    cl_dev = cache_keys.shape[1]
    feat = queries.shape[2]
    head_count = feat // HEAD_DIM
    score_scale = 1.0 / math.sqrt(HEAD_DIM)
    every_query = lax.all_gather(queries[0], "kv", axis=0, tiled=True)
    new_total = every_query.shape[0]
    query_heads = every_query.reshape(new_total, head_count, HEAD_DIM)
    key_cache = cache_keys[0].reshape(cl_dev, head_count, HEAD_DIM)
    value_cache = cache_values[0].reshape(cl_dev, head_count, HEAD_DIM)
    key_new = new_keys[0].reshape(tok_dev, head_count, HEAD_DIM)
    value_new = new_values[0].reshape(tok_dev, head_count, HEAD_DIM)
    score_cache = (
        jnp.einsum("qhd,khd->qhk", query_heads, key_cache, preferred_element_type=jnp.float32)
        * score_scale
    )
    position = kv_rank * cl_dev + jnp.arange(cl_dev, dtype=jnp.int32)
    score_cache = jnp.where((position < length)[None, None, :], score_cache, -jnp.inf)
    score_new = (
        jnp.einsum("qhd,khd->qhk", query_heads, key_new, preferred_element_type=jnp.float32)
        * score_scale
    )
    local_top = jnp.maximum(jnp.max(score_cache, axis=-1), jnp.max(score_new, axis=-1))
    expo_cache = jnp.exp(score_cache - local_top[..., None])
    expo_new = jnp.exp(score_new - local_top[..., None])
    denom = jnp.sum(expo_cache, axis=-1) + jnp.sum(expo_new, axis=-1)
    summed = jnp.einsum(
        "qhk,khd->qhd",
        expo_cache.astype(jnp.bfloat16),
        value_cache,
        preferred_element_type=jnp.float32,
    )
    summed = summed + jnp.einsum(
        "qhk,khd->qhd", expo_new.astype(jnp.bfloat16), value_new, preferred_element_type=jnp.float32
    )
    summed, denom = (summed.reshape(new_total, feat), denom)

    def join(first, second):
        first_top, first_denom, first_sum = first
        second_top, second_denom, second_sum = second
        joint_top = jnp.maximum(first_top, second_top)
        first_factor = jnp.exp(first_top - joint_top)
        second_factor = jnp.exp(second_top - joint_top)
        rows_here = first_sum.shape[0]
        joint_sum = (
            first_sum.reshape(rows_here, head_count, HEAD_DIM) * first_factor[..., None]
            + second_sum.reshape(rows_here, head_count, HEAD_DIM) * second_factor[..., None]
        )
        return (
            joint_top,
            first_denom * first_factor + second_denom * second_factor,
            joint_sum.reshape(rows_here, feat),
        )

    joint_top, joint_denom, joint_sum = combined_all((local_top, denom, summed), "kv", join)
    row_start = kv_rank * tok_dev
    own_sum = lax.dynamic_slice_in_dim(joint_sum, row_start, tok_dev, 0)
    own_denom = lax.dynamic_slice_in_dim(joint_denom, row_start, tok_dev, 0)
    attended = (
        (own_sum.reshape(tok_dev, head_count, HEAD_DIM) / own_denom[..., None])
        .reshape(tok_dev, feat)
        .astype(jnp.bfloat16)
    )
    return attended


def partial_softmax(query_rows, key_cache, value_cache, key_new, value_new, usable):
    rows, feat = query_rows.shape
    head_count = feat // HEAD_DIM
    score_scale = 1.0 / math.sqrt(HEAD_DIM)
    query_heads = query_rows.reshape(rows, head_count, HEAD_DIM)
    score_cache = (
        jnp.einsum("qhd,khd->qhk", query_heads, key_cache, preferred_element_type=jnp.float32)
        * score_scale
    )
    score_cache = jnp.where(usable[None, None, :], score_cache, -jnp.inf)
    score_new = (
        jnp.einsum("qhd,khd->qhk", query_heads, key_new, preferred_element_type=jnp.float32)
        * score_scale
    )
    top = jnp.maximum(jnp.max(score_cache, axis=-1), jnp.max(score_new, axis=-1))
    expo_cache = jnp.exp(score_cache - top[..., None])
    expo_new = jnp.exp(score_new - top[..., None])
    denom = jnp.sum(expo_cache, axis=-1) + jnp.sum(expo_new, axis=-1)
    summed = jnp.einsum(
        "qhk,khd->qhd", expo_cache.astype(jnp.bfloat16), value_cache,
        preferred_element_type=jnp.float32,
    )
    summed = summed + jnp.einsum(
        "qhk,khd->qhd", expo_new.astype(jnp.bfloat16), value_new, preferred_element_type=jnp.float32
    )
    return top, denom, summed


def paired_attention(own_queries, key_new, value_new, key_cache, value_cache, length):
    kv_rank = lax.axis_index("kv")
    swap = [(0, 1), (1, 0)]
    tok_dev, feat = own_queries.shape
    cl_dev = key_cache.shape[0]
    head_count = feat // HEAD_DIM
    far_queries = lax.ppermute(own_queries, "kv", swap)
    key_cache = key_cache.reshape(cl_dev, head_count, HEAD_DIM)
    value_cache = value_cache.reshape(cl_dev, head_count, HEAD_DIM)
    key_new = key_new.reshape(tok_dev, head_count, HEAD_DIM)
    value_new = value_new.reshape(tok_dev, head_count, HEAD_DIM)
    position = kv_rank * cl_dev + jnp.arange(cl_dev, dtype=jnp.int32)
    usable = position < length
    operands = (key_cache, value_cache, key_new, value_new, usable)
    own_top, own_denom, own_sum = partial_softmax(own_queries, *operands)
    far_top, far_denom, far_sum = partial_softmax(far_queries, *operands)
    back_top, back_denom, back_sum = lax.ppermute(
        (far_top, far_denom, far_sum.astype(jnp.bfloat16)), "kv", swap
    )
    joint_top = jnp.maximum(own_top, back_top)
    own_factor = jnp.exp(own_top - joint_top)
    back_factor = jnp.exp(back_top - joint_top)
    joint_sum = own_sum * own_factor[..., None] + back_sum.astype(jnp.float32) * back_factor[..., None]
    joint_denom = own_denom * own_factor + back_denom * back_factor
    return (joint_sum / joint_denom[..., None]).reshape(tok_dev, feat).astype(jnp.bfloat16)


def shards(
    plan,
    resid,
    queries,
    new_keys,
    new_values,
    cache_keys,
    cache_values,
    cached_len,
    group_request,
    w_out,
    norm_gain,
    route_ids,
    route_weights,
    gate_w,
    up_w,
    down_w,
):
    kv_rank = lax.axis_index("kv")
    ep_count = lax.axis_size("ep")
    tok_dev = resid.shape[1]
    cl_dev = cache_keys.shape[1]
    feat = queries.shape[2]
    head_count = feat // HEAD_DIM
    score_scale = 1.0 / math.sqrt(HEAD_DIM)
    request_index = jnp.arange(cached_len.shape[0], dtype=jnp.int32)
    length = jnp.sum(jnp.where(request_index == group_request[0], cached_len, 0))
    if lax.axis_size("kv") == 2 and plan is not None:
        attended = paired_attention(
            queries[0], new_keys[0], new_values[0], cache_keys[0], cache_values[0], length
        )
    else:
        attended = joined_attention(
            queries, new_keys, new_values, cache_keys, cache_values, length
        )
    proj = jnp.dot(attended, w_out, preferred_element_type=jnp.float32)
    hidden = (resid[0].astype(jnp.float32) + proj).astype(jnp.bfloat16)
    hidden_f = hidden.astype(jnp.float32)
    normed = (
        hidden_f
        * lax.rsqrt(jnp.mean(hidden_f * hidden_f, axis=-1, keepdims=True) + 1e-06)
        * norm_gain.astype(jnp.float32)
    ).astype(jnp.bfloat16)
    if plan is not None:
        moe_sum, _ = dense_moe(
            plan, normed, route_ids[0], route_weights[0], (gate_w, up_w, down_w), attended
        )
        return (hidden_f + moe_sum).astype(jnp.bfloat16)[None]
    expert_count = EXP_DEV * ep_count
    capacity = min(tok_dev, max(2, tok_dev * TOP * 3 // (2 * expert_count)))
    route_flat = route_ids[0].reshape(-1)
    one_hot = (route_flat[:, None] == jnp.arange(expert_count, dtype=jnp.int32)[None, :]).astype(
        jnp.int32
    )
    rank_in = jnp.sum((jnp.cumsum(one_hot, axis=0) - 1) * one_hot, axis=1)
    slot_of = route_flat * capacity + rank_in
    slot_index = jnp.arange(expert_count * capacity, dtype=jnp.int32)
    placing = jnp.sum(
        (slot_of.reshape(tok_dev, TOP)[None, :, :] == slot_index[:, None, None]).astype(jnp.int32),
        axis=-1,
    ).astype(jnp.bfloat16)
    outgoing = jnp.dot(placing, normed, preferred_element_type=jnp.float32).astype(jnp.bfloat16)
    outgoing = outgoing.reshape(ep_count, EXP_DEV, capacity, D)
    full_gate, full_up, full_down = (
        lax.all_gather(gate_w, "kv", axis=2, tiled=True),
        lax.all_gather(up_w, "kv", axis=2, tiled=True),
        lax.all_gather(down_w, "kv", axis=1, tiled=True),
    )
    expert_out = expert_full(
        lax.all_to_all(outgoing, "ep", split_axis=0, concat_axis=0, tiled=True),
        full_gate,
        full_up,
        full_down,
    ).astype(jnp.bfloat16)
    returned = lax.all_to_all(expert_out, "ep", split_axis=0, concat_axis=0, tiled=True).reshape(
        expert_count * capacity, D
    )
    picked = jnp.take(returned, slot_of, axis=0).reshape(tok_dev, TOP, D)
    moe_sum = jnp.sum(picked.astype(jnp.float32) * route_weights[0][..., None], axis=1)
    return (hidden_f + moe_sum).astype(jnp.bfloat16)[None]


def solution(mesh):
    placed = (
        P("ep", "kv", None),
        P("ep", "kv", None),
        P("ep", "kv", None),
        P("ep", "kv", None),
        P("ep", "kv", None),
        P("ep", "kv", None),
        P(),
        P("ep"),
        P(),
        P(),
        P("ep", "kv", None),
        P("ep", "kv", None),
        P("ep", None, "kv"),
        P("ep", None, "kv"),
        P("ep", "kv", None),
    )

    def run(*args):
        plan = gather_plan(mesh, [a.shape for a in args])
        body = functools.partial(shards, plan)
        return jax.shard_map(
            body, mesh=mesh, in_specs=placed, out_specs=P("ep", "kv", None), check_vma=False
        )(*args)

    return run
```
